128 devices in a mesh: tm: 16 (over z, x), space: 8 (over y, core).
Axes of the slice: x: 4, y: 4, z: 4, core: 2. Of those that a mesh axis runs over, the one named last changes fastest.
Arguments:
- query_states: bfloat16 [16, 2048, 2560], P('tm', 'space'), may hold values from -45 to 45
- key_states: bfloat16 [16, 2048, 2560], P('tm', 'space'), may hold values from -4 to 4
- value_states: bfloat16 [16, 2048, 2560], P('tm', 'space'), may hold values from -6 to 6
- history: int32 [16], P('tm'), may hold values from 0 to 2, as said below
- neighbours: int32 [16, 8, 2], P('tm', 'space'), may hold values 0 or 1
Outputs:
- attended: bfloat16 [16, 2048, 2560], P('tm', 'space')
The draws below stay inside these ranges and needn't reach their ends.
Inputs may be any that keep to these rules, and one draw needn't show every extreme that they name: Some segment has history exactly 2 in every draw.
All inputs are finite; a program needn't handle non-finite values. No bound on the sum of `neighbours` on one device may be relied on, other than what follows from the above.
Results may differ from the reference program's by a relative error of at most 0.005.
Values may be sent and summed in bfloat16 or wider, within the bound.
No kernel may reach another device: no remote copies, remote signals or barrier semaphores. Data moves between devices by JAX's collectives and lax.ppermute only.
A program may use at most 128 MiB of HBM per device.

```python
import jax
import jax.numpy as jnp
from jax import lax

HEADS = 20
HEAD_DIM = 128
FR = 1
TILE = 256
HIST_MAX = 2
NBLOCKS = 16
NF = 16
NTOK = 2048
N_TM = 16
N_SPACE = 8


def draw_pair(key):
    shape = (NF, NTOK, HEADS * HEAD_DIM)
    key_vals = jnp.clip(jax.random.normal(jax.random.fold_in(key, 11), shape, jnp.float32), -4.0, 4.0)
    query_vals = 3.0 * jnp.clip(jax.random.normal(jax.random.fold_in(key, 12), shape, jnp.float32), -4.0, 4.0)
    return (query_vals, key_vals)


def draw_query_states(key, part):
    return draw_pair(key)[0].astype(jnp.bfloat16)


def draw_key_states(key, part):
    return draw_pair(key)[1].astype(jnp.bfloat16)


def draw_history(key, part):
    lengths = jax.random.randint(jax.random.fold_in(key, 21), (NBLOCKS,), 0, HIST_MAX + 1)
    target = jax.random.randint(jax.random.fold_in(key, 22), (), 0, NBLOCKS)
    return jnp.where(jnp.arange(NBLOCKS) == target, HIST_MAX, lengths).astype(jnp.int32)


def with_ends(values, rng, smallest, top_value):
    shape = values.shape
    spot = [jax.random.randint(jax.random.fold_in(rng, axis), (), 0, shape[axis]) for axis in range(len(shape))]
    values = values.at[tuple(spot)].set(smallest)
    longest = shape.index(max(shape))
    spot[longest] = (spot[longest] + 1) % shape[longest]
    return values.at[tuple(spot)].set(top_value)


def steps_of(own_key, extent, pieces, low, high):
    gain = 1.0
    for position, blocks in pieces:
        heights = jax.random.uniform(jax.random.fold_in(jax.random.fold_in(own_key, 6), position), (blocks,), jnp.float32, low / len(pieces), high / len(pieces))
        gain = gain * jnp.repeat(jnp.exp(heights), extent[position] // blocks).reshape((-1,) + (1,) * (len(extent) - 1 - position))
    return gain


def bell_draw(stream_key, dims, spread, bound, shards=(), kind=jnp.bfloat16):
    array = jax.random.normal(stream_key, dims, jnp.float32) * spread
    if len(shards) > 0:
        array = steps_of(stream_key, dims, shards, -0.22, 0.18) * array
    return jnp.clip(array, min=-bound, max=bound).astype(kind)


def setup_inputs(seed: int = 0) -> dict:
    key_of = jax.random.split(jax.random.key(seed), 6)
    return {
        "query_states": draw_query_states(jax.random.fold_in(key_of[5], 71), 0),
        "key_states": draw_key_states(jax.random.fold_in(key_of[5], 71), 0),
        "value_states": bell_draw(key_of[2], (NF, NTOK, HEADS * HEAD_DIM), 1.0, 6.0, ((0, 16), (1, 8))),
        "history": draw_history(jax.random.fold_in(key_of[5], 71), 0),
        "neighbours": with_ends((jax.random.randint(key_of[4], (NBLOCKS, N_SPACE, 2), 0, 4) < 3).astype(jnp.int32), jax.random.fold_in(key_of[4], 1), 0, 1),
    }


def reference(query_states, key_states, value_states, history, neighbours):
    width_all = query_states.shape[2]
    head_count = width_all // HEAD_DIM
    inv_root = 1.0 / (HEAD_DIM ** 0.5)
    key_pad = jnp.pad(key_states, ((HIST_MAX, 0), (TILE, TILE), (0, 0)))
    value_pad = jnp.pad(value_states, ((HIST_MAX, 0), (TILE, TILE), (0, 0)))
    span = HIST_MAX + FR

    def one_block(index):
        seg = (index // N_SPACE).astype(jnp.int32)
        tile_pos = (index % N_SPACE).astype(jnp.int32)
        zero = jnp.zeros((), jnp.int32)
        queries = lax.dynamic_slice(query_states, (seg * FR, tile_pos * TILE, zero), (FR, TILE, width_all))
        key_block = lax.dynamic_slice(key_pad, (seg * FR, tile_pos * TILE, zero), (span, 3 * TILE, width_all))
        value_block = lax.dynamic_slice(value_pad, (seg * FR, tile_pos * TILE, zero), (span, 3 * TILE, width_all))
        query_rows = queries.reshape(FR * TILE, head_count, HEAD_DIM).astype(jnp.float32)
        key_rows = key_block.reshape(span * 3 * TILE, head_count, HEAD_DIM).astype(jnp.float32)
        value_rows = value_block.reshape(span * 3 * TILE, head_count, HEAD_DIM).astype(jnp.float32)
        key_frame = seg * FR - HIST_MAX + jnp.repeat(jnp.arange(span, dtype=jnp.int32), 3 * TILE)
        third = jnp.tile(jnp.arange(3 * TILE, dtype=jnp.int32) // TILE, span)
        left_open = (neighbours[seg, tile_pos, 0] == 1) & (tile_pos > 0)
        right_open = (neighbours[seg, tile_pos, 1] == 1) & (tile_pos < N_SPACE - 1)
        side_ok = jnp.where(third == 0, left_open, jnp.where(third == 2, right_open, True))
        query_frame = seg * FR + jnp.repeat(jnp.arange(FR, dtype=jnp.int32), TILE)
        allowed = (key_frame[None, :] <= query_frame[:, None]) & (key_frame[None, :] >= seg * FR - history[seg]) & (key_frame >= 0)[None, :] & side_ok[None, :]
        scores = jnp.einsum("rhd,khd->hrk", query_rows, key_rows) * inv_root
        scores = jnp.where(allowed[None], scores, -1e30)
        best = jnp.max(scores, axis=-1)
        weights = jnp.where(allowed[None], jnp.exp(scores - best[..., None]), 0.0)
        denom = jnp.sum(weights, axis=-1)
        weights_low = lax.optimization_barrier(weights.astype(jnp.bfloat16)).astype(jnp.float32)
        numer = jnp.einsum("hrk,khd->hrd", weights_low, value_rows)
        result = numer / denom[..., None]
        return jnp.transpose(result, (1, 0, 2)).reshape(FR, TILE, width_all).astype(jnp.bfloat16)

    blocks = lax.map(one_block, jnp.arange(N_TM * N_SPACE, dtype=jnp.int32))
    blocks = blocks.reshape(N_TM, N_SPACE, FR, TILE, width_all)
    return jnp.transpose(blocks, (0, 2, 1, 3, 4)).reshape(NF, NTOK, width_all)
```

```python
import jax
import jax.numpy as jnp
from jax import lax
from jax.experimental import pallas as pl
from jax.experimental.pallas import tpu as pltpu
from jax.sharding import PartitionSpec as P

HEAD_DIM = 128
HIST_MAX = 2
HG = 5
CHUNKS = 1
NEG = -1e30


def _attn_kernel(flags_ref, q_ref, kl_ref, kc_ref, kr_ref, vl_ref, vc_ref, vr_ref, o_ref, lse_ref, col_ref):
    hg = q_ref.shape[1] // HEAD_DIM
    inv_root = 1.0 / HEAD_DIM**0.5
    seg_ok = flags_ref[1] == 1

    @pl.when(seg_ok)
    def _():
        bias_l = jnp.where(flags_ref[0] == 1, 0.0, NEG).astype(jnp.float32)
        bias_r = jnp.where(flags_ref[2] == 1, 0.0, NEG).astype(jnp.float32)
        col_ref[...] = jnp.zeros_like(col_ref)
        for h in range(hg):
            cols = slice(h * HEAD_DIM, (h + 1) * HEAD_DIM)
            q = q_ref[:, cols]

            def scores(k_ref):
                return (
                    lax.dot_general(
                        q, k_ref[:, cols], (((1,), (1,)), ((), ())), preferred_element_type=jnp.float32
                    )
                    * inv_root
                )

            s_l = scores(kl_ref) + bias_l
            s_c = scores(kc_ref)
            s_r = scores(kr_ref) + bias_r
            m = jnp.maximum(
                jnp.maximum(s_l.max(axis=1, keepdims=True), s_c.max(axis=1, keepdims=True)),
                s_r.max(axis=1, keepdims=True),
            )
            p_l = jnp.exp(s_l - m)
            p_c = jnp.exp(s_c - m)
            p_r = jnp.exp(s_r - m)
            denom = (
                p_l.sum(axis=1, keepdims=True) + p_c.sum(axis=1, keepdims=True) + p_r.sum(axis=1, keepdims=True)
            )
            acc = jnp.dot(p_l.astype(jnp.bfloat16), vl_ref[:, cols], preferred_element_type=jnp.float32)
            acc += jnp.dot(p_c.astype(jnp.bfloat16), vc_ref[:, cols], preferred_element_type=jnp.float32)
            acc += jnp.dot(p_r.astype(jnp.bfloat16), vr_ref[:, cols], preferred_element_type=jnp.float32)
            o_ref[:, cols] = (acc / denom).astype(o_ref.dtype)
            col_ref[:, h : h + 1] = m + jnp.log(denom)
        lse_ref[0] = jnp.transpose(col_ref[...])[:hg, :]

    @pl.when(jnp.logical_not(seg_ok))
    def _():
        o_ref[...] = jnp.zeros_like(o_ref)
        lse_ref[...] = jnp.full(lse_ref.shape, NEG, jnp.float32)


def attend(flags, q, keys, values, width, base, q_offset):
    rows = q.shape[0]
    heads = width // HEAD_DIM
    groups = heads // HG
    lanes = HG * HEAD_DIM
    q_spec = pl.BlockSpec((rows, lanes), lambda g, f: (0, g + q_offset))
    kv_spec = pl.BlockSpec((rows, lanes), lambda g, f: (0, g + base))
    keys_rows = keys[0].shape[0]
    flops = 4 * rows * 3 * keys_rows * HEAD_DIM * heads
    return pl.pallas_call(
        _attn_kernel,
        out_shape=(
            jax.ShapeDtypeStruct((rows, width), jnp.bfloat16),
            jax.ShapeDtypeStruct((groups, HG, rows), jnp.float32),
        ),
        grid_spec=pltpu.PrefetchScalarGridSpec(
            num_scalar_prefetch=1,
            grid=(groups,),
            in_specs=[q_spec] + [kv_spec] * 6,
            out_specs=[
                pl.BlockSpec((rows, lanes), lambda g, f: (0, g)),
                pl.BlockSpec((1, HG, rows), lambda g, f: (g, 0, 0)),
            ],
            scratch_shapes=[pltpu.VMEM((rows, 128), jnp.float32)],
        ),
        cost_estimate=pl.CostEstimate(
            flops=flops,
            transcendentals=rows * 3 * keys_rows * heads,
            bytes_accessed=2 * rows * width * 2 + 6 * keys_rows * width * 2,
        ),
    )(flags, q, *keys, *values)


def merge(o1, lse1, o2, lse2):
    rows, width = o1.shape
    heads = width // HEAD_DIM
    top = jnp.maximum(lse1, lse2)
    e1 = jnp.exp(lse1 - top)
    e2 = jnp.exp(lse2 - top)
    total = e1 + e2
    lse = top + jnp.log(total)
    w1 = jnp.transpose((e1 / total).reshape(heads, rows))[:, :, None]
    w2 = jnp.transpose((e2 / total).reshape(heads, rows))[:, :, None]
    o = o1.reshape(rows, heads, HEAD_DIM).astype(jnp.float32) * w1
    o = o + o2.reshape(rows, heads, HEAD_DIM).astype(jnp.float32) * w2
    return o.reshape(rows, width), lse


def shift_tm(x, by):
    size = lax.axis_size("tm")
    pairs = [(i, i + by) for i in range(size) if 0 <= i + by < size]
    return lax.ppermute(x, "tm", pairs)


def on_device(query_states, key_states, value_states, history, neighbours):
    _, rows, width = query_states.shape
    heads = width // HEAD_DIM
    seg = lax.axis_index("tm")
    tile = lax.axis_index("space")
    tiles = lax.axis_size("space")
    q = query_states[0]
    k = key_states[0]
    v = value_states[0]

    count = tiles
    from_left = [(i, i + 1) for i in range(count - 1)]
    from_right = [(i + 1, i) for i in range(count - 1)]
    k_l, v_l = lax.ppermute((k, v), "space", from_left)
    k_r, v_r = lax.ppermute((k, v), "space", from_right)
    keys = (k_l, k, k_r)
    values = (v_l, v, v_r)

    meta = jnp.concatenate([history.reshape(1), neighbours.reshape(2)]).astype(jnp.int32)
    tile_l = tile > 0
    tile_r = tile < tiles - 1

    def flags_for(m, d):
        seg_ok = m[0] >= d
        return jnp.stack(
            [
                ((m[1] == 1) & tile_l).astype(jnp.int32),
                seg_ok.astype(jnp.int32),
                ((m[2] == 1) & tile_r).astype(jnp.int32),
            ]
        )

    chunk_w = width // CHUNKS
    outs = []
    meta1 = None
    for c in range(CHUNKS):
        qc = q[:, c * chunk_w : (c + 1) * chunk_w]
        if c == 0:
            q1, meta1 = shift_tm((qc, meta), -1)
            q2, meta2 = shift_tm((q1, meta1), -1)
        else:
            q1 = shift_tm(qc, -1)
            q2 = shift_tm(q1, -1)
        f0 = flags_for(meta, 0)
        f1 = flags_for(meta1, 1)
        f2 = flags_for(meta2, 2)
        groups_c = chunk_w // HEAD_DIM // HG
        base = c * groups_c
        o0, l0 = attend(f0, q, keys, values, chunk_w, base, base)
        o1, l1 = attend(f1, q1, keys, values, chunk_w, base, 0)
        o2, l2 = attend(f2, q2, keys, values, chunk_w, base, 0)
        o2_in, l2_in = shift_tm((o2, l2), 1)
        l2_in = jnp.where(seg >= 1, l2_in, NEG)
        oc, lc = merge(o1, l1, o2_in, l2_in)
        oc_in, lc_in = shift_tm((oc.astype(jnp.bfloat16), lc), 1)
        lc_in = jnp.where(seg >= 1, lc_in, NEG)
        out, _ = merge(o0, l0, oc_in, lc_in)
        outs.append(out.astype(jnp.bfloat16))
    result = outs[0] if CHUNKS == 1 else jnp.concatenate(outs, axis=1)
    return result.reshape(1, rows, width)


def solution(mesh):
    placed = (
        P("tm", "space", None),
        P("tm", "space", None),
        P("tm", "space", None),
        P("tm"),
        P("tm", "space", None),
    )
    return jax.shard_map(
        on_device, mesh=mesh, in_specs=placed, out_specs=P("tm", "space", None), check_vma=False
    )
```

```python
import jax
import jax.numpy as jnp
from jax import lax
from jax.experimental import pallas as pl
from jax.experimental.pallas import tpu as pltpu
from jax.sharding import PartitionSpec as P

HEAD_DIM = 128
HG = 5
CHUNKS = 2
NEG = -1e30


def _attn_kernel(flags_ref, q_ref, kl_ref, kc_ref, kr_ref, vl_ref, vc_ref, vr_ref, o_ref, lse_ref, col_ref, m_ref, l_ref, acc_ref):
    hg = q_ref.shape[1] // HEAD_DIM
    inv_root = 1.0 / HEAD_DIM**0.5
    seg_ok = flags_ref[1] == 1

    @pl.when(seg_ok)
    def _():
        for h in range(hg):
            cols = slice(h * HEAD_DIM, (h + 1) * HEAD_DIM)
            q = q_ref[:, cols]

            def scores(k_ref):
                return (
                    lax.dot_general(
                        q, k_ref[:, cols], (((1,), (1,)), ((), ())), preferred_element_type=jnp.float32
                    )
                    * inv_root
                )

            s = scores(kc_ref)
            m = s.max(axis=1, keepdims=True)
            p = jnp.exp(s - m)
            m_ref[...] = m
            l_ref[...] = p.sum(axis=1, keepdims=True)
            acc_ref[...] = jnp.dot(p.astype(jnp.bfloat16), vc_ref[:, cols], preferred_element_type=jnp.float32)
            for flag_i, k_ref, v_ref in ((0, kl_ref, vl_ref), (2, kr_ref, vr_ref)):

                @pl.when(flags_ref[flag_i] == 1)
                def _():
                    s = scores(k_ref)
                    m_old = m_ref[...]
                    m_new = jnp.maximum(m_old, s.max(axis=1, keepdims=True))
                    alpha = jnp.exp(m_old - m_new)
                    p = jnp.exp(s - m_new)
                    l_ref[...] = alpha * l_ref[...] + p.sum(axis=1, keepdims=True)
                    acc_ref[...] = alpha * acc_ref[...] + jnp.dot(
                        p.astype(jnp.bfloat16), v_ref[:, cols], preferred_element_type=jnp.float32
                    )
                    m_ref[...] = m_new

            denom = l_ref[...]
            o_ref[:, cols] = (acc_ref[...] / denom).astype(o_ref.dtype)
            col_ref[:, h : h + 1] = m_ref[...] + jnp.log(denom)
        lse_ref[0] = jnp.transpose(col_ref[...])[:hg, :]

    @pl.when(jnp.logical_not(seg_ok))
    def _():
        o_ref[...] = jnp.zeros_like(o_ref)
        lse_ref[...] = jnp.full(lse_ref.shape, NEG, jnp.float32)


def attend(flags, q, keys, values, width, base, q_base):
    rows = q.shape[0]
    heads = width // HEAD_DIM
    groups = heads // HG
    lanes = HG * HEAD_DIM
    q_spec = pl.BlockSpec((rows, lanes), lambda g, f: (0, g + q_base))
    kv_spec = pl.BlockSpec((rows, lanes), lambda g, f: (0, g + base))
    keys_rows = keys[0].shape[0]
    return pl.pallas_call(
        _attn_kernel,
        out_shape=(
            jax.ShapeDtypeStruct((rows, width), jnp.bfloat16),
            jax.ShapeDtypeStruct((groups, HG, rows), jnp.float32),
        ),
        grid_spec=pltpu.PrefetchScalarGridSpec(
            num_scalar_prefetch=1,
            grid=(groups,),
            in_specs=[q_spec] + [kv_spec] * 6,
            out_specs=[
                pl.BlockSpec((rows, lanes), lambda g, f: (0, g)),
                pl.BlockSpec((1, HG, rows), lambda g, f: (g, 0, 0)),
            ],
            scratch_shapes=[
                pltpu.VMEM((rows, 128), jnp.float32),
                pltpu.VMEM((rows, 1), jnp.float32),
                pltpu.VMEM((rows, 1), jnp.float32),
                pltpu.VMEM((rows, HEAD_DIM), jnp.float32),
            ],
        ),
        cost_estimate=pl.CostEstimate(
            flops=4 * rows * 3 * keys_rows * HEAD_DIM * heads,
            transcendentals=rows * 3 * keys_rows * heads,
            bytes_accessed=2 * rows * width * 2 + 6 * keys_rows * width * 2,
        ),
    )(flags, q, *keys, *values)


def _merge_weights(valid_ref, l1_ref, l2_ref, wt_ref):
    hg = l1_ref.shape[1]
    l1 = l1_ref[0]
    l2 = jnp.where(valid_ref[0] == 1, l2_ref[0], NEG)
    top = jnp.maximum(l1, l2)
    e1 = jnp.exp(l1 - top)
    e2 = jnp.exp(l2 - top)
    total = e1 + e2
    wt_ref[0:hg, :] = e1 / total
    wt_ref[8 : 8 + hg, :] = e2 / total
    return top + jnp.log(total), jnp.transpose(wt_ref[...])


def _merge_body(o1_ref, o2_ref, o_ref, w, hg):
    for h in range(hg):
        cols = slice(h * HEAD_DIM, (h + 1) * HEAD_DIM)
        o = o1_ref[:, cols].astype(jnp.float32) * w[:, h : h + 1]
        o = o + o2_ref[:, cols].astype(jnp.float32) * w[:, 8 + h : 9 + h]
        o_ref[:, cols] = o.astype(o_ref.dtype)


def _merge_kernel(valid_ref, o1_ref, l1_ref, o2_ref, l2_ref, o_ref, l_ref, wt_ref):
    lse, w = _merge_weights(valid_ref, l1_ref, l2_ref, wt_ref)
    l_ref[0] = lse
    _merge_body(o1_ref, o2_ref, o_ref, w, l1_ref.shape[1])


def _final_kernel(valid_ref, o1_ref, l1_ref, o2_ref, l2_ref, o_ref, wt_ref):
    _, w = _merge_weights(valid_ref, l1_ref, l2_ref, wt_ref)
    _merge_body(o1_ref, o2_ref, o_ref, w, l1_ref.shape[1])


def merge(valid, o1, l1, o2, l2, base, final):
    rows, width = o2.shape
    groups = width // HEAD_DIM // HG
    lanes = HG * HEAD_DIM
    o1_spec = pl.BlockSpec((rows, lanes), lambda g, v: (0, g + base))
    l1_spec = pl.BlockSpec((1, HG, rows), lambda g, v: (g + base, 0, 0))
    o2_spec = pl.BlockSpec((rows, lanes), lambda g, v: (0, g))
    l2_spec = pl.BlockSpec((1, HG, rows), lambda g, v: (g, 0, 0))
    if final:
        kernel = _final_kernel
        out_shape = jax.ShapeDtypeStruct(o1.shape, o1.dtype)
        out_specs = o1_spec
        aliases = {1: 0}
    else:
        kernel = _merge_kernel
        out_shape = (
            jax.ShapeDtypeStruct((rows, width), jnp.bfloat16),
            jax.ShapeDtypeStruct((groups, HG, rows), jnp.float32),
        )
        out_specs = [o2_spec, l2_spec]
        aliases = {}
    return pl.pallas_call(
        kernel,
        out_shape=out_shape,
        grid_spec=pltpu.PrefetchScalarGridSpec(
            num_scalar_prefetch=1,
            grid=(groups,),
            in_specs=[o1_spec, l1_spec, o2_spec, l2_spec],
            out_specs=out_specs,
            scratch_shapes=[pltpu.VMEM((128, rows), jnp.float32)],
        ),
        input_output_aliases=aliases,
        cost_estimate=pl.CostEstimate(
            flops=4 * rows * width, transcendentals=0, bytes_accessed=3 * rows * width * 2
        ),
    )(valid, o1, l1, o2, l2)


def shift_tm(x, by):
    size = lax.axis_size("tm")
    pairs = [(i, i + by) for i in range(size) if 0 <= i + by < size]
    return lax.ppermute(x, "tm", pairs)


def on_device(query_states, key_states, value_states, history, neighbours):
    _, rows, width = query_states.shape
    seg = lax.axis_index("tm")
    tile = lax.axis_index("space")
    tiles = lax.axis_size("space")
    q = query_states[0]
    k = key_states[0]
    v = value_states[0]

    meta = jnp.concatenate([history.reshape(1), neighbours.reshape(2)]).astype(jnp.int32)
    meta1 = shift_tm(meta, -1)
    meta2 = shift_tm(meta, -2)

    from_left = [(i, i + 1) for i in range(tiles - 1)]
    from_right = [(i + 1, i) for i in range(tiles - 1)]
    k_l, v_l = lax.ppermute((k, v), "space", from_left)
    k_r, v_r = lax.ppermute((k, v), "space", from_right)
    keys = (k_l, k, k_r)
    values = (v_l, v, v_r)

    tile_l = tile > 0
    tile_r = tile < tiles - 1

    def flags_for(m, d):
        return jnp.stack(
            [
                ((m[1] == 1) & tile_l).astype(jnp.int32),
                (m[0] >= d).astype(jnp.int32),
                ((m[2] == 1) & tile_r).astype(jnp.int32),
            ]
        )

    valid = (seg >= 1).astype(jnp.int32).reshape(1)
    chunk_w = width // CHUNKS
    groups_c = chunk_w // HEAD_DIM // HG
    q1s, q2s = [], []
    for c in range(CHUNKS):
        q1s.append(shift_tm(q[:, c * chunk_w : (c + 1) * chunk_w], -1))
    for c in range(CHUNKS):
        q2s.append(shift_tm(q1s[c], -1))
    o_self, l_self = attend(flags_for(meta, 0), q, keys, values, width, 0, 0)
    f1 = flags_for(meta1, 1)
    f2 = flags_for(meta2, 2)
    result = o_self
    for c in range(CHUNKS):
        base = c * groups_c
        o1, l1 = attend(f1, q1s[c], keys, values, chunk_w, base, 0)
        o2, l2 = attend(f2, q2s[c], keys, values, chunk_w, base, 0)
        o2_in, l2_in = shift_tm((o2, l2), 1)
        oc, lc = merge(valid, o1, l1, o2_in, l2_in, 0, False)
        oc_in, lc_in = shift_tm((oc, lc), 1)
        result = merge(valid, result, l_self, oc_in, lc_in, base, True)
    return result.reshape(1, rows, width)


def solution(mesh):
    placed = (
        P("tm", "space", None),
        P("tm", "space", None),
        P("tm", "space", None),
        P("tm"),
        P("tm", "space", None),
    )
    return jax.shard_map(
        on_device, mesh=mesh, in_specs=placed, out_specs=P("tm", "space", None), check_vma=False
    )
```

```python
import jax
import jax.numpy as jnp
from jax import lax
from jax.experimental import pallas as pl
from jax.experimental.pallas import tpu as pltpu
from jax.sharding import PartitionSpec as P

HEAD_DIM = 128
HG = 5
CHUNKS = 2
NEG = -1e30


def _attn_kernel(flags_ref, q_ref, kl_ref, kc_ref, kr_ref, vl_ref, vc_ref, vr_ref, o_ref, lse_ref, col_ref):
    hg = q_ref.shape[1] // HEAD_DIM
    inv_root = 1.0 / HEAD_DIM**0.5
    seg_ok = flags_ref[1] == 1

    @pl.when(seg_ok)
    def _():
        bias_l = jnp.where(flags_ref[0] == 1, 0.0, NEG).astype(jnp.float32)
        bias_r = jnp.where(flags_ref[2] == 1, 0.0, NEG).astype(jnp.float32)
        for h in range(hg):
            cols = slice(h * HEAD_DIM, (h + 1) * HEAD_DIM)
            q = q_ref[:, cols]

            def scores(k_ref):
                return (
                    lax.dot_general(
                        q, k_ref[:, cols], (((1,), (1,)), ((), ())), preferred_element_type=jnp.float32
                    )
                    * inv_root
                )

            s_l = scores(kl_ref) + bias_l
            s_c = scores(kc_ref)
            s_r = scores(kr_ref) + bias_r
            m = jnp.maximum(
                jnp.maximum(s_l.max(axis=1, keepdims=True), s_c.max(axis=1, keepdims=True)),
                s_r.max(axis=1, keepdims=True),
            )
            p_l = jnp.exp(s_l - m)
            p_c = jnp.exp(s_c - m)
            p_r = jnp.exp(s_r - m)
            denom = (
                p_l.sum(axis=1, keepdims=True) + p_c.sum(axis=1, keepdims=True) + p_r.sum(axis=1, keepdims=True)
            )
            acc = jnp.dot(p_l.astype(jnp.bfloat16), vl_ref[:, cols], preferred_element_type=jnp.float32)
            acc += jnp.dot(p_c.astype(jnp.bfloat16), vc_ref[:, cols], preferred_element_type=jnp.float32)
            acc += jnp.dot(p_r.astype(jnp.bfloat16), vr_ref[:, cols], preferred_element_type=jnp.float32)
            o_ref[:, cols] = (acc / denom).astype(o_ref.dtype)
            col_ref[:, h : h + 1] = m + jnp.log(denom)
        lse_ref[0] = jnp.transpose(col_ref[...])[:hg, :]

    @pl.when(jnp.logical_not(seg_ok))
    def _():
        o_ref[...] = jnp.zeros_like(o_ref)
        lse_ref[...] = jnp.full(lse_ref.shape, NEG, jnp.float32)


def attend(flags, q, keys, values, width, base, q_base):
    rows = keys[0].shape[0]
    heads = width // HEAD_DIM
    groups = heads // HG
    lanes = HG * HEAD_DIM
    q_spec = pl.BlockSpec((rows, lanes), lambda g, f: (0, g + q_base))
    kv_spec = pl.BlockSpec((rows, lanes), lambda g, f: (0, g + base))
    keys_rows = keys[0].shape[0]
    return pl.pallas_call(
        _attn_kernel,
        out_shape=(
            jax.ShapeDtypeStruct((rows, width), jnp.bfloat16),
            jax.ShapeDtypeStruct((groups, HG, rows), jnp.float32),
        ),
        grid_spec=pltpu.PrefetchScalarGridSpec(
            num_scalar_prefetch=1,
            grid=(groups,),
            in_specs=[q_spec] + [kv_spec] * 6,
            out_specs=[
                pl.BlockSpec((rows, lanes), lambda g, f: (0, g)),
                pl.BlockSpec((1, HG, rows), lambda g, f: (g, 0, 0)),
            ],
            scratch_shapes=[pltpu.VMEM((rows, 128), jnp.float32)],
        ),
        cost_estimate=pl.CostEstimate(
            flops=4 * rows * 3 * keys_rows * HEAD_DIM * heads,
            transcendentals=rows * 3 * keys_rows * heads,
            bytes_accessed=2 * rows * width * 2 + 6 * keys_rows * width * 2,
        ),
    )(flags, q, *keys, *values)


def _merge_weights(valid_ref, l1_ref, l2_ref, wt_ref):
    hg = l1_ref.shape[1]
    l1 = l1_ref[0]
    l2 = jnp.where(valid_ref[0] == 1, l2_ref[0], NEG)
    top = jnp.maximum(l1, l2)
    e1 = jnp.exp(l1 - top)
    e2 = jnp.exp(l2 - top)
    total = e1 + e2
    wt_ref[0:hg, :] = e1 / total
    wt_ref[8 : 8 + hg, :] = e2 / total
    return top + jnp.log(total), jnp.transpose(wt_ref[...])


def _merge_body(o1_ref, o2_ref, o_ref, w, hg):
    for h in range(hg):
        cols = slice(h * HEAD_DIM, (h + 1) * HEAD_DIM)
        o = o1_ref[:, cols].astype(jnp.float32) * w[:, h : h + 1]
        o = o + o2_ref[:, cols].astype(jnp.float32) * w[:, 8 + h : 9 + h]
        o_ref[:, cols] = o.astype(o_ref.dtype)


def _merge_kernel(valid_ref, o1_ref, l1_ref, o2_ref, l2_ref, o_ref, l_ref, wt_ref):
    lse, w = _merge_weights(valid_ref, l1_ref, l2_ref, wt_ref)
    l_ref[0] = lse
    _merge_body(o1_ref, o2_ref, o_ref, w, l1_ref.shape[1])


def _final_kernel(valid_ref, o1_ref, l1_ref, o2_ref, l2_ref, o_ref, wt_ref):
    _, w = _merge_weights(valid_ref, l1_ref, l2_ref, wt_ref)
    _merge_body(o1_ref, o2_ref, o_ref, w, l1_ref.shape[1])


def merge(valid, o1, l1, o2, l2, base, final):
    rows, width = o2.shape
    groups = width // HEAD_DIM // HG
    lanes = HG * HEAD_DIM
    o1_spec = pl.BlockSpec((rows, lanes), lambda g, v: (0, g + base))
    l1_spec = pl.BlockSpec((1, HG, rows), lambda g, v: (g + base, 0, 0))
    o2_spec = pl.BlockSpec((rows, lanes), lambda g, v: (0, g))
    l2_spec = pl.BlockSpec((1, HG, rows), lambda g, v: (g, 0, 0))
    if final:
        kernel = _final_kernel
        out_shape = jax.ShapeDtypeStruct(o1.shape, o1.dtype)
        out_specs = o1_spec
        aliases = {1: 0}
    else:
        kernel = _merge_kernel
        out_shape = (
            jax.ShapeDtypeStruct((rows, width), jnp.bfloat16),
            jax.ShapeDtypeStruct((groups, HG, rows), jnp.float32),
        )
        out_specs = [o2_spec, l2_spec]
        aliases = {}
    return pl.pallas_call(
        kernel,
        out_shape=out_shape,
        grid_spec=pltpu.PrefetchScalarGridSpec(
            num_scalar_prefetch=1,
            grid=(groups,),
            in_specs=[o1_spec, l1_spec, o2_spec, l2_spec],
            out_specs=out_specs,
            scratch_shapes=[pltpu.VMEM((128, rows), jnp.float32)],
        ),
        input_output_aliases=aliases,
        cost_estimate=pl.CostEstimate(
            flops=4 * rows * width, transcendentals=0, bytes_accessed=3 * rows * width * 2
        ),
    )(valid, o1, l1, o2, l2)


def shift_tm(x, by):
    size = lax.axis_size("tm")
    pairs = [(i, i + by) for i in range(size) if 0 <= i + by < size]
    return lax.ppermute(x, "tm", pairs)


def on_device(query_states, key_states, value_states, history, neighbours):
    _, rows, width = query_states.shape
    seg = lax.axis_index("tm")
    tile = lax.axis_index("space")
    tiles = lax.axis_size("space")
    q = query_states[0]
    k = key_states[0]
    v = value_states[0]

    meta = jnp.concatenate([history.reshape(1), neighbours.reshape(2)]).astype(jnp.bfloat16)

    from_left = [(i, i + 1) for i in range(tiles - 1)]
    from_right = [(i + 1, i) for i in range(tiles - 1)]
    k_l, v_l = lax.ppermute((k, v), "space", from_left)
    k_r, v_r = lax.ppermute((k, v), "space", from_right)
    keys = (k_l, k, k_r)
    values = (v_l, v, v_r)

    tile_l = tile > 0
    tile_r = tile < tiles - 1

    def flags_for(m, d):
        m = m.astype(jnp.int32)
        return jnp.stack(
            [
                ((m[1] == 1) & tile_l).astype(jnp.int32),
                (m[0] >= d).astype(jnp.int32),
                ((m[2] == 1) & tile_r).astype(jnp.int32),
            ]
        )

    valid = (seg >= 1).astype(jnp.int32).reshape(1)
    chunk_w = width // CHUNKS
    groups_c = chunk_w // HEAD_DIM // HG
    meta_rows = jnp.zeros((16, chunk_w), jnp.bfloat16).at[0, 0:3].set(meta)
    sends = [jnp.concatenate([q[:, :chunk_w], meta_rows], axis=0)]
    sends += [q[:, c * chunk_w : (c + 1) * chunk_w] for c in range(1, CHUNKS)]
    q1s = [shift_tm(x, -1) for x in sends]
    q2s = [shift_tm(x, -1) for x in q1s]
    f1 = flags_for(q1s[0][rows, 0:3], 1)
    f2 = flags_for(q2s[0][rows, 0:3], 2)
    o_self, l_self = attend(flags_for(meta, 0), q, keys, values, width, 0, 0)
    result = o_self
    for c in range(CHUNKS):
        base = c * groups_c
        o1, l1 = attend(f1, q1s[c], keys, values, chunk_w, base, 0)
        if c == 0:
            q2, o_self, l_self, o1, l1 = lax.optimization_barrier((q2s[c], o_self, l_self, o1, l1))
        else:
            q2, o1, l1 = lax.optimization_barrier((q2s[c], o1, l1))
        o2, l2 = attend(f2, q2, keys, values, chunk_w, base, 0)
        o2_in, l2_in = shift_tm((o2, l2), 1)
        oc, lc = merge(valid, o1, l1, o2_in, l2_in, 0, False)
        oc_in, lc_in = shift_tm((oc, lc), 1)
        result = merge(valid, result if c else o_self, l_self, oc_in, lc_in, base, True)
    return result.reshape(1, rows, width)


def solution(mesh):
    placed = (
        P("tm", "space", None),
        P("tm", "space", None),
        P("tm", "space", None),
        P("tm"),
        P("tm", "space", None),
    )
    return jax.shard_map(
        on_device, mesh=mesh, in_specs=placed, out_specs=P("tm", "space", None), check_vma=False
    )
```

```python
import jax
import jax.numpy as jnp
from jax import lax
from jax.experimental import pallas as pl
from jax.experimental.pallas import tpu as pltpu
from jax.sharding import PartitionSpec as P

HEAD_DIM = 128
HG = 5
CHUNKS = 2
NEG = -1e30
EXTRA = 16


def _attn_kernel(flags_ref, q_ref, kl_ref, kc_ref, kr_ref, vl_ref, vc_ref, vr_ref, o_ref, col_ref):
    hg = q_ref.shape[1] // HEAD_DIM
    rows = q_ref.shape[0]
    lanes = o_ref.shape[1]
    inv_root = 1.0 / HEAD_DIM**0.5
    seg_ok = flags_ref[1] == 1

    @pl.when(seg_ok)
    def _():
        bias_l = jnp.where(flags_ref[0] == 1, 0.0, NEG).astype(jnp.float32)
        bias_r = jnp.where(flags_ref[2] == 1, 0.0, NEG).astype(jnp.float32)
        col_ref[...] = jnp.zeros_like(col_ref)
        for h in range(hg):
            cols = slice(h * HEAD_DIM, (h + 1) * HEAD_DIM)
            q = q_ref[:, cols]

            def scores(k_ref):
                return (
                    lax.dot_general(
                        q, k_ref[:, cols], (((1,), (1,)), ((), ())), preferred_element_type=jnp.float32
                    )
                    * inv_root
                )

            s_l = scores(kl_ref) + bias_l
            s_c = scores(kc_ref)
            s_r = scores(kr_ref) + bias_r
            top = jnp.maximum(
                jnp.maximum(s_l.max(axis=1, keepdims=True), s_c.max(axis=1, keepdims=True)),
                s_r.max(axis=1, keepdims=True),
            )
            shift = top.astype(jnp.bfloat16).astype(jnp.float32)
            p_l = jnp.exp(s_l - shift)
            p_c = jnp.exp(s_c - shift)
            p_r = jnp.exp(s_r - shift)
            denom = (
                p_l.sum(axis=1, keepdims=True) + p_c.sum(axis=1, keepdims=True) + p_r.sum(axis=1, keepdims=True)
            )
            acc = jnp.dot(p_l.astype(jnp.bfloat16), vl_ref[:, cols], preferred_element_type=jnp.float32)
            acc += jnp.dot(p_c.astype(jnp.bfloat16), vc_ref[:, cols], preferred_element_type=jnp.float32)
            acc += jnp.dot(p_r.astype(jnp.bfloat16), vr_ref[:, cols], preferred_element_type=jnp.float32)
            o_ref[0:rows, cols] = (acc / denom).astype(o_ref.dtype)
            col_ref[:, h : h + 1] = shift
            col_ref[:, 8 + h : 9 + h] = denom
        stats = jnp.transpose(col_ref[...])[0:EXTRA, :]
        o_ref[rows : rows + EXTRA, 0:rows] = stats.astype(o_ref.dtype)
        o_ref[rows : rows + EXTRA, rows:lanes] = jnp.zeros((EXTRA, lanes - rows), o_ref.dtype)

    @pl.when(jnp.logical_not(seg_ok))
    def _():
        row = lax.broadcasted_iota(jnp.int32, o_ref.shape, 0)
        empty = (row >= rows) & (row < rows + 8)
        o_ref[...] = jnp.where(empty, NEG, 0.0).astype(o_ref.dtype)


def attend(flags, q, k, v, kv_l, kv_r, width, base, q_base):
    rows = k.shape[0]
    heads = width // HEAD_DIM
    groups = heads // HG
    lanes = HG * HEAD_DIM
    q_spec = pl.BlockSpec((rows, lanes), lambda g, f: (0, g + q_base))
    kv_spec = pl.BlockSpec((rows, lanes), lambda g, f: (0, g + base))
    side_k = pl.BlockSpec((None, rows, lanes), lambda g, f: (0, 0, g + base))
    side_v = pl.BlockSpec((None, rows, lanes), lambda g, f: (1, 0, g + base))
    return pl.pallas_call(
        _attn_kernel,
        out_shape=jax.ShapeDtypeStruct((rows + EXTRA, width), jnp.bfloat16),
        grid_spec=pltpu.PrefetchScalarGridSpec(
            num_scalar_prefetch=1,
            grid=(groups,),
            in_specs=[q_spec, side_k, kv_spec, side_k, side_v, kv_spec, side_v],
            out_specs=pl.BlockSpec((rows + EXTRA, lanes), lambda g, f: (0, g)),
            scratch_shapes=[pltpu.VMEM((rows, 128), jnp.float32)],
        ),
        cost_estimate=pl.CostEstimate(
            flops=4 * rows * 3 * rows * HEAD_DIM * heads,
            transcendentals=rows * 3 * rows * heads,
            bytes_accessed=2 * rows * width * 2 + 6 * rows * width * 2,
        ),
    )(flags, q, kv_l, k, kv_r, kv_l, v, kv_r)


def _merge_weights(valid_ref, a_ref, b_ref, wt_ref):
    rows = wt_ref.shape[1]
    hg = a_ref.shape[1] // HEAD_DIM
    a_top = a_ref[rows : rows + hg, 0:rows].astype(jnp.float32)
    a_den = a_ref[rows + 8 : rows + 8 + hg, 0:rows].astype(jnp.float32)
    ok = valid_ref[0] == 1
    b_top = jnp.where(ok, b_ref[rows : rows + hg, 0:rows].astype(jnp.float32), NEG)
    b_den = jnp.where(ok, b_ref[rows + 8 : rows + 8 + hg, 0:rows].astype(jnp.float32), 0.0)
    top = jnp.maximum(a_top, b_top)
    a_w = jnp.exp(a_top - top) * a_den
    b_w = jnp.exp(b_top - top) * b_den
    total = a_w + b_w
    safe = jnp.where(total > 0.0, total, 1.0)
    wt_ref[0:hg, :] = a_w / safe
    wt_ref[8 : 8 + hg, :] = b_w / safe
    return top, total, jnp.transpose(wt_ref[...])


def _merge_body(a_ref, b_ref, o_ref, w, hg, rows):
    for h in range(hg):
        cols = slice(h * HEAD_DIM, (h + 1) * HEAD_DIM)
        o = a_ref[0:rows, cols].astype(jnp.float32) * w[:, h : h + 1]
        o = o + b_ref[0:rows, cols].astype(jnp.float32) * w[:, 8 + h : 9 + h]
        o_ref[0:rows, cols] = o.astype(o_ref.dtype)


def _merge_kernel(valid_ref, a_ref, b_ref, o_ref, wt_ref):
    rows = wt_ref.shape[1]
    lanes = o_ref.shape[1]
    hg = lanes // HEAD_DIM
    top, total, w = _merge_weights(valid_ref, a_ref, b_ref, wt_ref)
    _merge_body(a_ref, b_ref, o_ref, w, hg, rows)
    o_ref[rows : rows + 8, 0:rows] = jnp.zeros((8, rows), o_ref.dtype)
    o_ref[rows + 8 : rows + EXTRA, 0:rows] = jnp.zeros((8, rows), o_ref.dtype)
    o_ref[rows : rows + hg, 0:rows] = top.astype(o_ref.dtype)
    o_ref[rows + 8 : rows + 8 + hg, 0:rows] = total.astype(o_ref.dtype)
    o_ref[rows : rows + EXTRA, rows:lanes] = jnp.zeros((EXTRA, lanes - rows), o_ref.dtype)


def _final_kernel(valid_ref, a_ref, b_ref, *rest):
    o_ref, wt_ref = rest[-2], rest[-1]
    rows = wt_ref.shape[1]
    _, _, w = _merge_weights(valid_ref, a_ref, b_ref, wt_ref)
    _merge_body(a_ref, b_ref, o_ref, w, o_ref.shape[1] // HEAD_DIM, rows)


def merge(valid, a, b, base, final=False, buf=None):
    ext, width = b.shape
    rows = ext - EXTRA
    groups = width // HEAD_DIM // HG
    lanes = HG * HEAD_DIM
    a_spec = pl.BlockSpec((ext, lanes), lambda g, v: (0, g + base))
    b_spec = pl.BlockSpec((ext, lanes), lambda g, v: (0, g))
    in_specs = [a_spec, b_spec]
    operands = [valid, a, b]
    aliases = {}
    if final:
        kernel = _final_kernel
        out_shape = jax.ShapeDtypeStruct((rows, a.shape[1]), jnp.bfloat16)
        out_spec = pl.BlockSpec((rows, lanes), lambda g, v: (0, g + base))
        if buf is not None:
            in_specs.append(pl.BlockSpec(memory_space=pl.ANY))
            operands.append(buf)
            aliases = {3: 0}
    else:
        kernel = _merge_kernel
        out_shape = jax.ShapeDtypeStruct((ext, width), jnp.bfloat16)
        out_spec = b_spec
    return pl.pallas_call(
        kernel,
        out_shape=out_shape,
        grid_spec=pltpu.PrefetchScalarGridSpec(
            num_scalar_prefetch=1,
            grid=(groups,),
            in_specs=in_specs,
            out_specs=out_spec,
            scratch_shapes=[pltpu.VMEM((128, rows), jnp.float32)],
        ),
        input_output_aliases=aliases,
        cost_estimate=pl.CostEstimate(
            flops=4 * rows * width, transcendentals=0, bytes_accessed=3 * rows * width * 2
        ),
    )(*operands)


def shift_tm(x, by):
    size = lax.axis_size("tm")
    pairs = [(i, i + by) for i in range(size) if 0 <= i + by < size]
    return lax.ppermute(x, "tm", pairs)


def on_device(query_states, key_states, value_states, history, neighbours):
    _, rows, width = query_states.shape
    seg = lax.axis_index("tm")
    tile = lax.axis_index("space")
    tiles = lax.axis_size("space")
    q = query_states[0]
    k = key_states[0]
    v = value_states[0]

    meta = jnp.concatenate([history.reshape(1), neighbours.reshape(2)]).astype(jnp.bfloat16)
    chunk_w = width // CHUNKS
    groups_c = chunk_w // HEAD_DIM // HG
    meta_rows = jnp.zeros((EXTRA, chunk_w), jnp.bfloat16).at[0, 0:3].set(meta)
    sends = [jnp.concatenate([q[:, :chunk_w], meta_rows], axis=0)]
    sends += [q[:, c * chunk_w : (c + 1) * chunk_w] for c in range(1, CHUNKS)]
    q1s = [shift_tm(x, -1) for x in sends]

    kv = jnp.stack([k, v])
    kv_l = lax.ppermute(kv, "space", [(i, i + 1) for i in range(tiles - 1)])
    kv_r = lax.ppermute(kv, "space", [(i + 1, i) for i in range(tiles - 1)])

    q2s = [shift_tm(x, -1) for x in q1s]

    tile_l = tile > 0
    tile_r = tile < tiles - 1

    def flags_for(m, d):
        m = m.astype(jnp.int32)
        return jnp.stack(
            [
                ((m[1] == 1) & tile_l).astype(jnp.int32),
                (m[0] >= d).astype(jnp.int32),
                ((m[2] == 1) & tile_r).astype(jnp.int32),
            ]
        )

    valid = (seg >= 1).astype(jnp.int32).reshape(1)
    f1 = flags_for(q1s[0][rows, 0:3], 1)
    f2 = flags_for(q2s[0][rows, 0:3], 2)
    p_self = attend(flags_for(meta, 0), q, k, v, kv_l, kv_r, width, 0, 0)
    result = None
    for c in range(CHUNKS):
        base = c * groups_c
        p1 = attend(f1, q1s[c], k, v, kv_l, kv_r, chunk_w, base, 0)
        if c == 0:
            q2, p_self, p1 = lax.optimization_barrier((q2s[c], p_self, p1))
        else:
            q2, p1 = lax.optimization_barrier((q2s[c], p1))
        p2 = attend(f2, q2, k, v, kv_l, kv_r, chunk_w, base, 0)
        p2_in = shift_tm(p2, 1)
        pc = merge(valid, p1, p2_in, 0)
        pc_in = shift_tm(pc, 1)
        result = merge(valid, p_self, pc_in, base, final=True, buf=result)
    return result.reshape(1, rows, width)


def solution(mesh):
    placed = (
        P("tm", "space", None),
        P("tm", "space", None),
        P("tm", "space", None),
        P("tm"),
        P("tm", "space", None),
    )
    return jax.shard_map(
        on_device, mesh=mesh, in_specs=placed, out_specs=P("tm", "space", None), check_vma=False
    )
```

```python
import jax
import jax.numpy as jnp
from jax import lax
from jax.experimental import pallas as pl
from jax.experimental.pallas import tpu as pltpu
from jax.sharding import PartitionSpec as P

HEAD_DIM = 128
HG = 5
CHUNKS = 2
NEG = -1e30
EXTRA = 16


def _attn_kernel(flags_ref, q_ref, kl_ref, kc_ref, kr_ref, vl_ref, vc_ref, vr_ref, o_ref, col_ref):
    hg = q_ref.shape[1] // HEAD_DIM
    rows = q_ref.shape[0]
    lanes = o_ref.shape[1]
    inv_root = 1.0 / HEAD_DIM**0.5
    seg_ok = flags_ref[1] == 1

    @pl.when(seg_ok)
    def _():
        bias_l = jnp.where(flags_ref[0] == 1, 0.0, NEG).astype(jnp.float32)
        bias_r = jnp.where(flags_ref[2] == 1, 0.0, NEG).astype(jnp.float32)
        col_ref[...] = jnp.zeros_like(col_ref)
        for h in range(hg):
            cols = slice(h * HEAD_DIM, (h + 1) * HEAD_DIM)
            q = q_ref[:, cols]

            def scores(k_ref):
                return (
                    lax.dot_general(
                        q, k_ref[:, cols], (((1,), (1,)), ((), ())), preferred_element_type=jnp.float32
                    )
                    * inv_root
                )

            s_l = scores(kl_ref) + bias_l
            s_c = scores(kc_ref)
            s_r = scores(kr_ref) + bias_r
            top = jnp.maximum(
                jnp.maximum(s_l.max(axis=1, keepdims=True), s_c.max(axis=1, keepdims=True)),
                s_r.max(axis=1, keepdims=True),
            )
            shift = top.astype(jnp.bfloat16).astype(jnp.float32)
            p_l = jnp.exp(s_l - shift)
            p_c = jnp.exp(s_c - shift)
            p_r = jnp.exp(s_r - shift)
            denom = (
                p_l.sum(axis=1, keepdims=True) + p_c.sum(axis=1, keepdims=True) + p_r.sum(axis=1, keepdims=True)
            )
            acc = jnp.dot(p_l.astype(jnp.bfloat16), vl_ref[:, cols], preferred_element_type=jnp.float32)
            acc += jnp.dot(p_c.astype(jnp.bfloat16), vc_ref[:, cols], preferred_element_type=jnp.float32)
            acc += jnp.dot(p_r.astype(jnp.bfloat16), vr_ref[:, cols], preferred_element_type=jnp.float32)
            o_ref[0:rows, cols] = (acc / denom).astype(o_ref.dtype)
            den_hi = denom.astype(jnp.bfloat16).astype(jnp.float32)
            col_ref[:, h : h + 1] = shift
            col_ref[:, hg + h : hg + h + 1] = den_hi
            col_ref[:, 2 * hg + h : 2 * hg + h + 1] = denom - den_hi
        stats = jnp.transpose(col_ref[...])[0:EXTRA, :]
        o_ref[rows : rows + EXTRA, 0:rows] = stats.astype(o_ref.dtype)
        o_ref[rows : rows + EXTRA, rows:lanes] = jnp.zeros((EXTRA, lanes - rows), o_ref.dtype)

    @pl.when(jnp.logical_not(seg_ok))
    def _():
        row = lax.broadcasted_iota(jnp.int32, o_ref.shape, 0)
        empty = (row >= rows) & (row < rows + hg)
        o_ref[...] = jnp.where(empty, NEG, 0.0).astype(o_ref.dtype)


def attend(flags, q, k, v, kv_l, kv_r, width, base, q_base):
    rows = k.shape[0]
    heads = width // HEAD_DIM
    groups = heads // HG
    lanes = HG * HEAD_DIM
    q_spec = pl.BlockSpec((rows, lanes), lambda g, f: (0, g + q_base))
    kv_spec = pl.BlockSpec((rows, lanes), lambda g, f: (0, g + base))
    side_k = pl.BlockSpec((None, rows, lanes), lambda g, f: (0, 0, g + base))
    side_v = pl.BlockSpec((None, rows, lanes), lambda g, f: (1, 0, g + base))
    return pl.pallas_call(
        _attn_kernel,
        out_shape=jax.ShapeDtypeStruct((rows + EXTRA, width), jnp.bfloat16),
        grid_spec=pltpu.PrefetchScalarGridSpec(
            num_scalar_prefetch=1,
            grid=(groups,),
            in_specs=[q_spec, side_k, kv_spec, side_k, side_v, kv_spec, side_v],
            out_specs=pl.BlockSpec((rows + EXTRA, lanes), lambda g, f: (0, g)),
            scratch_shapes=[pltpu.VMEM((rows, 128), jnp.float32)],
        ),
        cost_estimate=pl.CostEstimate(
            flops=4 * rows * 3 * rows * HEAD_DIM * heads,
            transcendentals=rows * 3 * rows * heads,
            bytes_accessed=2 * rows * width * 2 + 6 * rows * width * 2,
        ),
    )(flags, q, kv_l, k, kv_r, kv_l, v, kv_r)


def _merge_weights(valid_ref, a_ref, b_ref, wt_ref):
    rows = wt_ref.shape[1]
    hg = a_ref.shape[1] // HEAD_DIM
    def stats(ref):
        block = ref[rows : rows + EXTRA, 0:rows].astype(jnp.float32)
        return block[0:hg], block[hg : 2 * hg] + block[2 * hg : 3 * hg]

    a_top, a_den = stats(a_ref)
    ok = valid_ref[0] == 1
    b_top, b_den = stats(b_ref)
    b_top = jnp.where(ok, b_top, NEG)
    b_den = jnp.where(ok, b_den, 0.0)
    top = jnp.maximum(a_top, b_top)
    a_w = jnp.exp(a_top - top) * a_den
    b_w = jnp.exp(b_top - top) * b_den
    total = a_w + b_w
    safe = jnp.where(total > 0.0, total, 1.0)
    wt_ref[0:hg, :] = a_w / safe
    wt_ref[8 : 8 + hg, :] = b_w / safe
    return top, total, jnp.transpose(wt_ref[...])


def _merge_body(a_ref, b_ref, o_ref, w, hg, rows):
    for h in range(hg):
        cols = slice(h * HEAD_DIM, (h + 1) * HEAD_DIM)
        o = a_ref[0:rows, cols].astype(jnp.float32) * w[:, h : h + 1]
        o = o + b_ref[0:rows, cols].astype(jnp.float32) * w[:, 8 + h : 9 + h]
        o_ref[0:rows, cols] = o.astype(o_ref.dtype)


def _merge_kernel(valid_ref, a_ref, b_ref, o_ref, wt_ref):
    rows = wt_ref.shape[1]
    lanes = o_ref.shape[1]
    hg = lanes // HEAD_DIM
    top, total, w = _merge_weights(valid_ref, a_ref, b_ref, wt_ref)
    _merge_body(a_ref, b_ref, o_ref, w, hg, rows)
    hi = total.astype(jnp.bfloat16).astype(jnp.float32)
    pad = jnp.zeros((EXTRA - 3 * hg, rows), jnp.float32)
    block = jnp.concatenate([top, hi, total - hi, pad], axis=0)
    o_ref[rows : rows + EXTRA, 0:rows] = block.astype(o_ref.dtype)
    o_ref[rows : rows + EXTRA, rows:lanes] = jnp.zeros((EXTRA, lanes - rows), o_ref.dtype)


def _final_kernel(valid_ref, a_ref, b_ref, *rest):
    o_ref, wt_ref = rest[-2], rest[-1]
    rows = wt_ref.shape[1]
    _, _, w = _merge_weights(valid_ref, a_ref, b_ref, wt_ref)
    _merge_body(a_ref, b_ref, o_ref, w, o_ref.shape[1] // HEAD_DIM, rows)


def merge(valid, a, b, base, final=False, buf=None):
    ext, width = b.shape
    rows = ext - EXTRA
    groups = width // HEAD_DIM // HG
    lanes = HG * HEAD_DIM
    a_spec = pl.BlockSpec((ext, lanes), lambda g, v: (0, g + base))
    b_spec = pl.BlockSpec((ext, lanes), lambda g, v: (0, g))
    in_specs = [a_spec, b_spec]
    operands = [valid, a, b]
    aliases = {}
    if final:
        kernel = _final_kernel
        out_shape = jax.ShapeDtypeStruct((rows, a.shape[1]), jnp.bfloat16)
        out_spec = pl.BlockSpec((rows, lanes), lambda g, v: (0, g + base))
        if buf is not None:
            in_specs.append(pl.BlockSpec(memory_space=pl.ANY))
            operands.append(buf)
            aliases = {3: 0}
    else:
        kernel = _merge_kernel
        out_shape = jax.ShapeDtypeStruct((ext, width), jnp.bfloat16)
        out_spec = b_spec
    return pl.pallas_call(
        kernel,
        out_shape=out_shape,
        grid_spec=pltpu.PrefetchScalarGridSpec(
            num_scalar_prefetch=1,
            grid=(groups,),
            in_specs=in_specs,
            out_specs=out_spec,
            scratch_shapes=[pltpu.VMEM((128, rows), jnp.float32)],
        ),
        input_output_aliases=aliases,
        cost_estimate=pl.CostEstimate(
            flops=4 * rows * width, transcendentals=0, bytes_accessed=3 * rows * width * 2
        ),
    )(*operands)


def shift_tm(x, by):
    size = lax.axis_size("tm")
    pairs = [(i, i + by) for i in range(size) if 0 <= i + by < size]
    return lax.ppermute(x, "tm", pairs)


def on_device(query_states, key_states, value_states, history, neighbours):
    _, rows, width = query_states.shape
    seg = lax.axis_index("tm")
    tile = lax.axis_index("space")
    tiles = lax.axis_size("space")
    q = query_states[0]
    k = key_states[0]
    v = value_states[0]
    tile_l = tile > 0
    tile_r = tile < tiles - 1

    def flags_for(m, d):
        m = m.astype(jnp.int32)
        return jnp.stack(
            [
                ((m[1] == 1) & tile_l).astype(jnp.int32),
                (m[0] >= d).astype(jnp.int32),
                ((m[2] == 1) & tile_r).astype(jnp.int32),
            ]
        )

    meta = jnp.concatenate([history.reshape(1), neighbours.reshape(2)]).astype(jnp.bfloat16)
    chunk_w = width // CHUNKS
    groups_c = chunk_w // HEAD_DIM // HG
    meta_rows = jnp.zeros((EXTRA, chunk_w), jnp.bfloat16).at[0, 0:3].set(meta)
    sends = [jnp.concatenate([q[:, :chunk_w], meta_rows], axis=0)]
    sends += [q[:, c * chunk_w : (c + 1) * chunk_w] for c in range(1, CHUNKS)]
    q1s = [shift_tm(x, -1) for x in sends]

    kv = jnp.stack([k, v])
    kv_l = lax.ppermute(kv, "space", [(i, i + 1) for i in range(tiles - 1)])
    kv_r = lax.ppermute(kv, "space", [(i + 1, i) for i in range(tiles - 1)])

    f1 = flags_for(q1s[0][rows, 0:3], 1)
    p_self = attend(flags_for(meta, 0), q, k, v, kv_l, kv_r, width, 0, 0)
    p1s, q2s = [], []
    for c in range(CHUNKS):
        p1 = attend(f1, q1s[c], k, v, kv_l, kv_r, chunk_w, c * groups_c, 0)
        if c == 0:
            relay, p1 = lax.optimization_barrier((q1s[c], p1))
        else:
            relay, p1, p_self = lax.optimization_barrier((q1s[c], p1, p_self))
        p1s.append(p1)
        q2s.append(shift_tm(relay, -1))

    valid = (seg >= 1).astype(jnp.int32).reshape(1)
    f2 = flags_for(q2s[0][rows, 0:3], 2)
    result = None
    for c in range(CHUNKS):
        base = c * groups_c
        p2 = attend(f2, q2s[c], k, v, kv_l, kv_r, chunk_w, base, 0)
        p2_in = shift_tm(p2, 1)
        pc = merge(valid, p1s[c], p2_in, 0)
        pc_in = shift_tm(pc, 1)
        result = merge(valid, p_self, pc_in, base, final=True, buf=result)
    return result.reshape(1, rows, width)


def solution(mesh):
    placed = (
        P("tm", "space", None),
        P("tm", "space", None),
        P("tm", "space", None),
        P("tm"),
        P("tm", "space", None),
    )
    return jax.shard_map(
        on_device, mesh=mesh, in_specs=placed, out_specs=P("tm", "space", None), check_vma=False
    )
```

```python
import jax
import jax.numpy as jnp
from jax import lax
from jax.experimental import pallas as pl
from jax.experimental.pallas import tpu as pltpu
from jax.sharding import PartitionSpec as P

HEAD_DIM = 128
HG = 5
CHUNKS = 2
NEG = -1e30
EXTRA = 16


def _store_stats(o_ref, st_ref, t, hg, rows):
    hi = t[0 : 2 * hg].astype(jnp.bfloat16).astype(jnp.float32)
    st_ref[...] = jnp.zeros_like(st_ref)
    st_ref[0 : 2 * hg, 0:rows] = hi
    st_ref[0 : 2 * hg, rows : 2 * rows] = t[0 : 2 * hg] - hi
    o_ref[rows : rows + EXTRA, :] = st_ref[...].astype(o_ref.dtype)


def _load_stats(ref, hg, rows):
    block = ref[rows : rows + EXTRA, :].astype(jnp.float32)
    full = block[0 : 2 * hg, 0:rows] + block[0 : 2 * hg, rows : 2 * rows]
    return full[0:hg], full[hg : 2 * hg]


def _attn_kernel(flags_ref, q_ref, kl_ref, kc_ref, kr_ref, vl_ref, vc_ref, vr_ref, o_ref, col_ref, st_ref):
    hg = q_ref.shape[1] // HEAD_DIM
    rows = q_ref.shape[0]
    lanes = o_ref.shape[1]
    inv_root = 1.0 / HEAD_DIM**0.5
    seg_ok = flags_ref[1] == 1

    @pl.when(seg_ok)
    def _():
        bias_l = jnp.where(flags_ref[0] == 1, 0.0, NEG).astype(jnp.float32)
        bias_r = jnp.where(flags_ref[2] == 1, 0.0, NEG).astype(jnp.float32)
        col_ref[...] = jnp.zeros_like(col_ref)
        for h in range(hg):
            cols = slice(h * HEAD_DIM, (h + 1) * HEAD_DIM)
            q = q_ref[:, cols]

            def scores(k_ref):
                return (
                    lax.dot_general(
                        q, k_ref[:, cols], (((1,), (1,)), ((), ())), preferred_element_type=jnp.float32
                    )
                    * inv_root
                )

            s_l = scores(kl_ref) + bias_l
            s_c = scores(kc_ref)
            s_r = scores(kr_ref) + bias_r
            top = jnp.maximum(
                jnp.maximum(s_l.max(axis=1, keepdims=True), s_c.max(axis=1, keepdims=True)),
                s_r.max(axis=1, keepdims=True),
            )
            shift = top
            p_l = jnp.exp(s_l - shift)
            p_c = jnp.exp(s_c - shift)
            p_r = jnp.exp(s_r - shift)
            denom = (
                p_l.sum(axis=1, keepdims=True) + p_c.sum(axis=1, keepdims=True) + p_r.sum(axis=1, keepdims=True)
            )
            acc = jnp.dot(p_l.astype(jnp.bfloat16), vl_ref[:, cols], preferred_element_type=jnp.float32)
            acc += jnp.dot(p_c.astype(jnp.bfloat16), vc_ref[:, cols], preferred_element_type=jnp.float32)
            acc += jnp.dot(p_r.astype(jnp.bfloat16), vr_ref[:, cols], preferred_element_type=jnp.float32)
            o_ref[0:rows, cols] = (acc / denom).astype(o_ref.dtype)
            col_ref[:, h : h + 1] = shift
            col_ref[:, hg + h : hg + h + 1] = denom
        _store_stats(o_ref, st_ref, jnp.transpose(col_ref[...]), hg, rows)

    @pl.when(jnp.logical_not(seg_ok))
    def _():
        row = lax.broadcasted_iota(jnp.int32, o_ref.shape, 0)
        lane = lax.broadcasted_iota(jnp.int32, o_ref.shape, 1)
        empty = (row >= rows) & (row < rows + hg) & (lane < rows)
        o_ref[...] = jnp.where(empty, NEG, 0.0).astype(o_ref.dtype)


def attend(flags, q, k, v, kv_l, kv_r, width, base, q_base):
    rows = k.shape[0]
    heads = width // HEAD_DIM
    groups = heads // HG
    lanes = HG * HEAD_DIM
    q_spec = pl.BlockSpec((rows, lanes), lambda g, f: (0, g + q_base))
    kv_spec = pl.BlockSpec((rows, lanes), lambda g, f: (0, g + base))
    side_k = pl.BlockSpec((None, rows, lanes), lambda g, f: (0, 0, g + base))
    side_v = pl.BlockSpec((None, rows, lanes), lambda g, f: (1, 0, g + base))
    return pl.pallas_call(
        _attn_kernel,
        out_shape=jax.ShapeDtypeStruct((rows + EXTRA, width), jnp.bfloat16),
        grid_spec=pltpu.PrefetchScalarGridSpec(
            num_scalar_prefetch=1,
            grid=(groups,),
            in_specs=[q_spec, side_k, kv_spec, side_k, side_v, kv_spec, side_v],
            out_specs=pl.BlockSpec((rows + EXTRA, lanes), lambda g, f: (0, g)),
            scratch_shapes=[pltpu.VMEM((rows, 128), jnp.float32), pltpu.VMEM((EXTRA, lanes), jnp.float32)],
        ),
        cost_estimate=pl.CostEstimate(
            flops=4 * rows * 3 * rows * HEAD_DIM * heads,
            transcendentals=rows * 3 * rows * heads,
            bytes_accessed=2 * rows * width * 2 + 6 * rows * width * 2,
        ),
    )(flags, q, kv_l, k, kv_r, kv_l, v, kv_r)


def _merge_weights(valid_ref, a_ref, b_ref, wt_ref):
    rows = wt_ref.shape[1]
    hg = a_ref.shape[1] // HEAD_DIM
    a_top, a_den = _load_stats(a_ref, hg, rows)
    ok = valid_ref[0] == 1
    b_top, b_den = _load_stats(b_ref, hg, rows)
    b_top = jnp.where(ok, b_top, NEG)
    b_den = jnp.where(ok, b_den, 0.0)
    top = jnp.maximum(a_top, b_top)
    a_w = jnp.exp(a_top - top) * a_den
    b_w = jnp.exp(b_top - top) * b_den
    total = a_w + b_w
    safe = jnp.where(total > 0.0, total, 1.0)
    wt_ref[0:hg, :] = a_w / safe
    wt_ref[8 : 8 + hg, :] = b_w / safe
    return top, total, jnp.transpose(wt_ref[...])


def _merge_body(a_ref, b_ref, o_ref, w, hg, rows):
    for h in range(hg):
        cols = slice(h * HEAD_DIM, (h + 1) * HEAD_DIM)
        o = a_ref[0:rows, cols].astype(jnp.float32) * w[:, h : h + 1]
        o = o + b_ref[0:rows, cols].astype(jnp.float32) * w[:, 8 + h : 9 + h]
        o_ref[0:rows, cols] = o.astype(o_ref.dtype)


def _merge_kernel(valid_ref, a_ref, b_ref, o_ref, wt_ref, st_ref):
    rows = wt_ref.shape[1]
    hg = o_ref.shape[1] // HEAD_DIM
    top, total, w = _merge_weights(valid_ref, a_ref, b_ref, wt_ref)
    _merge_body(a_ref, b_ref, o_ref, w, hg, rows)
    wt_ref[0:hg, :] = top
    wt_ref[hg : 2 * hg, :] = total
    _store_stats(o_ref, st_ref, wt_ref[...], hg, rows)


def _final_kernel(valid_ref, a_ref, b_ref, *rest):
    o_ref, wt_ref = rest[-2], rest[-1]
    rows = wt_ref.shape[1]
    _, _, w = _merge_weights(valid_ref, a_ref, b_ref, wt_ref)
    _merge_body(a_ref, b_ref, o_ref, w, o_ref.shape[1] // HEAD_DIM, rows)


def merge(valid, a, b, base, final=False, buf=None):
    ext, width = b.shape
    rows = ext - EXTRA
    groups = width // HEAD_DIM // HG
    lanes = HG * HEAD_DIM
    a_spec = pl.BlockSpec((ext, lanes), lambda g, v: (0, g + base))
    b_spec = pl.BlockSpec((ext, lanes), lambda g, v: (0, g))
    in_specs = [a_spec, b_spec]
    operands = [valid, a, b]
    aliases = {}
    if final:
        kernel = _final_kernel
        out_shape = jax.ShapeDtypeStruct((rows, a.shape[1]), jnp.bfloat16)
        out_spec = pl.BlockSpec((rows, lanes), lambda g, v: (0, g + base))
        if buf is not None:
            in_specs.append(pl.BlockSpec(memory_space=pl.ANY))
            operands.append(buf)
            aliases = {3: 0}
    else:
        kernel = _merge_kernel
        out_shape = jax.ShapeDtypeStruct((ext, width), jnp.bfloat16)
        out_spec = b_spec
    return pl.pallas_call(
        kernel,
        out_shape=out_shape,
        grid_spec=pltpu.PrefetchScalarGridSpec(
            num_scalar_prefetch=1,
            grid=(groups,),
            in_specs=in_specs,
            out_specs=out_spec,
            scratch_shapes=[pltpu.VMEM((128, rows), jnp.float32)]
            + ([] if final else [pltpu.VMEM((EXTRA, lanes), jnp.float32)]),
        ),
        input_output_aliases=aliases,
        cost_estimate=pl.CostEstimate(
            flops=4 * rows * width, transcendentals=0, bytes_accessed=3 * rows * width * 2
        ),
    )(*operands)


def shift_tm(x, by):
    size = lax.axis_size("tm")
    pairs = [(i, i + by) for i in range(size) if 0 <= i + by < size]
    return lax.ppermute(x, "tm", pairs)


def on_device(query_states, key_states, value_states, history, neighbours):
    _, rows, width = query_states.shape
    seg = lax.axis_index("tm")
    tile = lax.axis_index("space")
    tiles = lax.axis_size("space")
    q = query_states[0]
    k = key_states[0]
    v = value_states[0]
    tile_l = tile > 0
    tile_r = tile < tiles - 1

    def flags_for(m, d):
        m = m.astype(jnp.int32)
        return jnp.stack(
            [
                ((m[1] == 1) & tile_l).astype(jnp.int32),
                (m[0] >= d).astype(jnp.int32),
                ((m[2] == 1) & tile_r).astype(jnp.int32),
            ]
        )

    meta = jnp.concatenate([history.reshape(1), neighbours.reshape(2)]).astype(jnp.bfloat16)
    chunk_w = width // CHUNKS
    groups_c = chunk_w // HEAD_DIM // HG
    meta_rows = jnp.zeros((EXTRA, chunk_w), jnp.bfloat16).at[0, 0:3].set(meta)
    sends = [jnp.concatenate([q[:, :chunk_w], meta_rows], axis=0)]
    sends += [q[:, c * chunk_w : (c + 1) * chunk_w] for c in range(1, CHUNKS)]
    q1s = [shift_tm(x, -1) for x in sends]

    kv = jnp.stack([k, v])
    kv_l = lax.ppermute(kv, "space", [(i, i + 1) for i in range(tiles - 1)])
    kv_r = lax.ppermute(kv, "space", [(i + 1, i) for i in range(tiles - 1)])

    f1 = flags_for(q1s[0][rows, 0:3], 1)
    p_self = attend(flags_for(meta, 0), q, k, v, kv_l, kv_r, width, 0, 0)
    p1s, q2s = [], []
    for c in range(CHUNKS):
        p1 = attend(f1, q1s[c], k, v, kv_l, kv_r, chunk_w, c * groups_c, 0)
        relay, p1 = lax.optimization_barrier((q1s[c], p1))
        p1s.append(p1)
        q2s.append(shift_tm(relay, -1))

    valid = (seg >= 1).astype(jnp.int32).reshape(1)
    f2 = flags_for(q2s[0][rows, 0:3], 2)
    result = None
    for c in range(CHUNKS):
        base = c * groups_c
        q2 = q2s[c]
        if c == 0:
            q2, p_self = lax.optimization_barrier((q2, p_self))
        p2 = attend(f2, q2, k, v, kv_l, kv_r, chunk_w, base, 0)
        p2_in = shift_tm(p2, 1)
        pc = merge(valid, p1s[c], p2_in, 0)
        pc_in = shift_tm(pc, 1)
        result = merge(valid, p_self, pc_in, base, final=True, buf=result)
    return result.reshape(1, rows, width)


def solution(mesh):
    placed = (
        P("tm", "space", None),
        P("tm", "space", None),
        P("tm", "space", None),
        P("tm"),
        P("tm", "space", None),
    )
    return jax.shard_map(
        on_device, mesh=mesh, in_specs=placed, out_specs=P("tm", "space", None), check_vma=False
    )
```

```python
import jax
import jax.numpy as jnp
from jax import lax
from jax.experimental import pallas as pl
from jax.experimental.pallas import tpu as pltpu
from jax.sharding import PartitionSpec as P

HEAD_DIM = 128
HG = 5
CHUNKS = 4
NEG = -1e30
EXTRA = 16


def _store_stats(o_ref, st_ref, t, hg, rows):
    hi = t[0 : 2 * hg].astype(jnp.bfloat16).astype(jnp.float32)
    st_ref[...] = jnp.zeros_like(st_ref)
    st_ref[0 : 2 * hg, 0:rows] = hi
    st_ref[0 : 2 * hg, rows : 2 * rows] = t[0 : 2 * hg] - hi
    o_ref[rows : rows + EXTRA, :] = st_ref[...].astype(o_ref.dtype)


def _load_stats(ref, hg, rows):
    block = ref[rows : rows + EXTRA, :].astype(jnp.float32)
    full = block[0 : 2 * hg, 0:rows] + block[0 : 2 * hg, rows : 2 * rows]
    return full[0:hg], full[hg : 2 * hg]


def _attn_kernel(flags_ref, q_ref, kl_ref, kc_ref, kr_ref, vl_ref, vc_ref, vr_ref, o_ref, col_ref, st_ref):
    hg = q_ref.shape[1] // HEAD_DIM
    rows = q_ref.shape[0]
    lanes = o_ref.shape[1]
    inv_root = 1.0 / HEAD_DIM**0.5
    seg_ok = flags_ref[1] == 1

    @pl.when(seg_ok)
    def _():
        bias_l = jnp.where(flags_ref[0] == 1, 0.0, NEG).astype(jnp.float32)
        bias_r = jnp.where(flags_ref[2] == 1, 0.0, NEG).astype(jnp.float32)
        col_ref[...] = jnp.zeros_like(col_ref)
        for h in range(hg):
            cols = slice(h * HEAD_DIM, (h + 1) * HEAD_DIM)
            q = q_ref[:, cols]

            def scores(k_ref):
                return (
                    lax.dot_general(
                        q, k_ref[:, cols], (((1,), (1,)), ((), ())), preferred_element_type=jnp.float32
                    )
                    * inv_root
                )

            s_l = scores(kl_ref) + bias_l
            s_c = scores(kc_ref)
            s_r = scores(kr_ref) + bias_r
            top = jnp.maximum(
                jnp.maximum(s_l.max(axis=1, keepdims=True), s_c.max(axis=1, keepdims=True)),
                s_r.max(axis=1, keepdims=True),
            )
            shift = top
            p_l = jnp.exp(s_l - shift)
            p_c = jnp.exp(s_c - shift)
            p_r = jnp.exp(s_r - shift)
            denom = (
                p_l.sum(axis=1, keepdims=True) + p_c.sum(axis=1, keepdims=True) + p_r.sum(axis=1, keepdims=True)
            )
            acc = jnp.dot(p_l.astype(jnp.bfloat16), vl_ref[:, cols], preferred_element_type=jnp.float32)
            acc += jnp.dot(p_c.astype(jnp.bfloat16), vc_ref[:, cols], preferred_element_type=jnp.float32)
            acc += jnp.dot(p_r.astype(jnp.bfloat16), vr_ref[:, cols], preferred_element_type=jnp.float32)
            o_ref[0:rows, cols] = (acc / denom).astype(o_ref.dtype)
            col_ref[:, h : h + 1] = shift
            col_ref[:, hg + h : hg + h + 1] = denom
        _store_stats(o_ref, st_ref, jnp.transpose(col_ref[...]), hg, rows)

    @pl.when(jnp.logical_not(seg_ok))
    def _():
        row = lax.broadcasted_iota(jnp.int32, o_ref.shape, 0)
        lane = lax.broadcasted_iota(jnp.int32, o_ref.shape, 1)
        empty = (row >= rows) & (row < rows + hg) & (lane < rows)
        o_ref[...] = jnp.where(empty, NEG, 0.0).astype(o_ref.dtype)


def attend(flags, q, k, v, kv_l, kv_r, width, base, q_base):
    rows = k.shape[0]
    heads = width // HEAD_DIM
    groups = heads // HG
    lanes = HG * HEAD_DIM
    q_spec = pl.BlockSpec((rows, lanes), lambda g, f: (0, g + q_base))
    kv_spec = pl.BlockSpec((rows, lanes), lambda g, f: (0, g + base))
    side_k = pl.BlockSpec((None, rows, lanes), lambda g, f: (0, 0, g + base))
    side_v = pl.BlockSpec((None, rows, lanes), lambda g, f: (1, 0, g + base))
    return pl.pallas_call(
        _attn_kernel,
        out_shape=jax.ShapeDtypeStruct((rows + EXTRA, width), jnp.bfloat16),
        grid_spec=pltpu.PrefetchScalarGridSpec(
            num_scalar_prefetch=1,
            grid=(groups,),
            in_specs=[q_spec, side_k, kv_spec, side_k, side_v, kv_spec, side_v],
            out_specs=pl.BlockSpec((rows + EXTRA, lanes), lambda g, f: (0, g)),
            scratch_shapes=[pltpu.VMEM((rows, 128), jnp.float32), pltpu.VMEM((EXTRA, lanes), jnp.float32)],
        ),
        cost_estimate=pl.CostEstimate(
            flops=4 * rows * 3 * rows * HEAD_DIM * heads,
            transcendentals=rows * 3 * rows * heads,
            bytes_accessed=2 * rows * width * 2 + 6 * rows * width * 2,
        ),
    )(flags, q, kv_l, k, kv_r, kv_l, v, kv_r)


def _merge_weights(valid_ref, a_ref, b_ref, wt_ref):
    rows = wt_ref.shape[1]
    hg = a_ref.shape[1] // HEAD_DIM
    a_top, a_den = _load_stats(a_ref, hg, rows)
    ok = valid_ref[0] == 1
    b_top, b_den = _load_stats(b_ref, hg, rows)
    b_top = jnp.where(ok, b_top, NEG)
    b_den = jnp.where(ok, b_den, 0.0)
    top = jnp.maximum(a_top, b_top)
    a_w = jnp.exp(a_top - top) * a_den
    b_w = jnp.exp(b_top - top) * b_den
    total = a_w + b_w
    safe = jnp.where(total > 0.0, total, 1.0)
    wt_ref[0:hg, :] = a_w / safe
    wt_ref[8 : 8 + hg, :] = b_w / safe
    return top, total, jnp.transpose(wt_ref[...])


def _merge_body(a_ref, b_ref, o_ref, w, hg, rows):
    for h in range(hg):
        cols = slice(h * HEAD_DIM, (h + 1) * HEAD_DIM)
        o = a_ref[0:rows, cols].astype(jnp.float32) * w[:, h : h + 1]
        o = o + b_ref[0:rows, cols].astype(jnp.float32) * w[:, 8 + h : 9 + h]
        o_ref[0:rows, cols] = o.astype(o_ref.dtype)


def _merge_kernel(valid_ref, a_ref, b_ref, o_ref, wt_ref, st_ref):
    rows = wt_ref.shape[1]
    hg = o_ref.shape[1] // HEAD_DIM
    top, total, w = _merge_weights(valid_ref, a_ref, b_ref, wt_ref)
    _merge_body(a_ref, b_ref, o_ref, w, hg, rows)
    wt_ref[0:hg, :] = top
    wt_ref[hg : 2 * hg, :] = total
    _store_stats(o_ref, st_ref, wt_ref[...], hg, rows)


def _final_kernel(valid_ref, a_ref, b_ref, *rest):
    o_ref, wt_ref = rest[-2], rest[-1]
    rows = wt_ref.shape[1]
    _, _, w = _merge_weights(valid_ref, a_ref, b_ref, wt_ref)
    _merge_body(a_ref, b_ref, o_ref, w, o_ref.shape[1] // HEAD_DIM, rows)


def merge(valid, a, b, base, final=False, buf=None):
    ext, width = b.shape
    rows = ext - EXTRA
    groups = width // HEAD_DIM // HG
    lanes = HG * HEAD_DIM
    a_spec = pl.BlockSpec((ext, lanes), lambda g, v: (0, g + base))
    b_spec = pl.BlockSpec((ext, lanes), lambda g, v: (0, g))
    in_specs = [a_spec, b_spec]
    operands = [valid, a, b]
    aliases = {}
    if final:
        kernel = _final_kernel
        out_shape = jax.ShapeDtypeStruct((rows, a.shape[1]), jnp.bfloat16)
        out_spec = pl.BlockSpec((rows, lanes), lambda g, v: (0, g + base))
        if buf is not None:
            in_specs.append(pl.BlockSpec(memory_space=pl.ANY))
            operands.append(buf)
            aliases = {3: 0}
    else:
        kernel = _merge_kernel
        out_shape = jax.ShapeDtypeStruct((ext, width), jnp.bfloat16)
        out_spec = b_spec
    return pl.pallas_call(
        kernel,
        out_shape=out_shape,
        grid_spec=pltpu.PrefetchScalarGridSpec(
            num_scalar_prefetch=1,
            grid=(groups,),
            in_specs=in_specs,
            out_specs=out_spec,
            scratch_shapes=[pltpu.VMEM((128, rows), jnp.float32)]
            + ([] if final else [pltpu.VMEM((EXTRA, lanes), jnp.float32)]),
        ),
        input_output_aliases=aliases,
        cost_estimate=pl.CostEstimate(
            flops=4 * rows * width, transcendentals=0, bytes_accessed=3 * rows * width * 2
        ),
    )(*operands)


def shift_tm(x, by):
    size = lax.axis_size("tm")
    pairs = [(i, i + by) for i in range(size) if 0 <= i + by < size]
    return lax.ppermute(x, "tm", pairs)


def on_device(query_states, key_states, value_states, history, neighbours):
    _, rows, width = query_states.shape
    seg = lax.axis_index("tm")
    tile = lax.axis_index("space")
    tiles = lax.axis_size("space")
    q = query_states[0]
    k = key_states[0]
    v = value_states[0]
    tile_l = tile > 0
    tile_r = tile < tiles - 1

    def flags_for(m, d):
        m = m.astype(jnp.int32)
        return jnp.stack(
            [
                ((m[1] == 1) & tile_l).astype(jnp.int32),
                (m[0] >= d).astype(jnp.int32),
                ((m[2] == 1) & tile_r).astype(jnp.int32),
            ]
        )

    meta = jnp.concatenate([history.reshape(1), neighbours.reshape(2)]).astype(jnp.bfloat16)
    chunk_w = width // CHUNKS
    groups_c = chunk_w // HEAD_DIM // HG
    meta_rows = jnp.zeros((EXTRA, chunk_w), jnp.bfloat16).at[0, 0:3].set(meta)
    sends = [jnp.concatenate([q[:, :chunk_w], meta_rows], axis=0)]
    sends += [q[:, c * chunk_w : (c + 1) * chunk_w] for c in range(1, CHUNKS)]
    q1s = [shift_tm(x, -1) for x in sends]

    kv = jnp.stack([k, v])
    kv_l = lax.ppermute(kv, "space", [(i, i + 1) for i in range(tiles - 1)])
    kv_r = lax.ppermute(kv, "space", [(i + 1, i) for i in range(tiles - 1)])

    f1 = flags_for(q1s[0][rows, 0:3], 1)
    p_self = attend(flags_for(meta, 0), q, k, v, kv_l, kv_r, width, 0, 0)
    p1s, q2s = [], []
    for c in range(CHUNKS):
        p1 = attend(f1, q1s[c], k, v, kv_l, kv_r, chunk_w, c * groups_c, 0)
        relay, p1 = lax.optimization_barrier((q1s[c], p1))
        p1s.append(p1)
        q2s.append(shift_tm(relay, -1))

    valid = (seg >= 1).astype(jnp.int32).reshape(1)
    f2 = flags_for(q2s[0][rows, 0:3], 2)
    result = None
    for c in range(CHUNKS):
        base = c * groups_c
        q2 = q2s[c]
        if c == 0:
            q2, p_self = lax.optimization_barrier((q2, p_self))
        p2 = attend(f2, q2, k, v, kv_l, kv_r, chunk_w, base, 0)
        p2_in = shift_tm(p2, 1)
        pc = merge(valid, p1s[c], p2_in, 0)
        pc_in = shift_tm(pc, 1)
        result = merge(valid, p_self, pc_in, base, final=True, buf=result)
    return result.reshape(1, rows, width)


def solution(mesh):
    placed = (
        P("tm", "space", None),
        P("tm", "space", None),
        P("tm", "space", None),
        P("tm"),
        P("tm", "space", None),
    )
    return jax.shard_map(
        on_device, mesh=mesh, in_specs=placed, out_specs=P("tm", "space", None), check_vma=False
    )
```

```python
import jax
import jax.numpy as jnp
from jax import lax
from jax.experimental import pallas as pl
from jax.experimental.pallas import tpu as pltpu
from jax.sharding import PartitionSpec as P

HEAD_DIM = 128
HG = 5
CHUNKS = 2
NEG = -1e30
EXTRA = 16


def _store_stats(o_ref, st_ref, t, hg, rows):
    hi = t[0 : 2 * hg].astype(jnp.bfloat16).astype(jnp.float32)
    st_ref[...] = jnp.zeros_like(st_ref)
    st_ref[0 : 2 * hg, 0:rows] = hi
    st_ref[0 : 2 * hg, rows : 2 * rows] = t[0 : 2 * hg] - hi
    o_ref[rows : rows + EXTRA, :] = st_ref[...].astype(o_ref.dtype)


def _load_stats(ref, hg, rows):
    block = ref[rows : rows + EXTRA, :].astype(jnp.float32)
    full = block[0 : 2 * hg, 0:rows] + block[0 : 2 * hg, rows : 2 * rows]
    return full[0:hg], full[hg : 2 * hg]


def _attn_kernel(flags_ref, q_ref, kl_ref, kc_ref, kr_ref, vl_ref, vc_ref, vr_ref, o_ref, col_ref, st_ref):
    hg = q_ref.shape[1] // HEAD_DIM
    rows = q_ref.shape[0]
    lanes = o_ref.shape[1]
    inv_root = 1.0 / HEAD_DIM**0.5
    seg_ok = flags_ref[1] == 1

    @pl.when(seg_ok)
    def _():
        bias_l = jnp.where(flags_ref[0] == 1, 0.0, NEG).astype(jnp.float32)
        bias_r = jnp.where(flags_ref[2] == 1, 0.0, NEG).astype(jnp.float32)
        col_ref[...] = jnp.zeros_like(col_ref)
        for h in range(hg):
            cols = slice(h * HEAD_DIM, (h + 1) * HEAD_DIM)
            q = q_ref[:, cols]

            def scores(k_ref):
                return (
                    lax.dot_general(
                        q, k_ref[:, cols], (((1,), (1,)), ((), ())), preferred_element_type=jnp.float32
                    )
                    * inv_root
                )

            s_l = scores(kl_ref) + bias_l
            s_c = scores(kc_ref)
            s_r = scores(kr_ref) + bias_r
            top = jnp.maximum(
                jnp.maximum(s_l.max(axis=1, keepdims=True), s_c.max(axis=1, keepdims=True)),
                s_r.max(axis=1, keepdims=True),
            )
            shift = top
            p_l = jnp.exp(s_l - shift)
            p_c = jnp.exp(s_c - shift)
            p_r = jnp.exp(s_r - shift)
            denom = (
                p_l.sum(axis=1, keepdims=True) + p_c.sum(axis=1, keepdims=True) + p_r.sum(axis=1, keepdims=True)
            )
            acc = jnp.dot(p_l.astype(jnp.bfloat16), vl_ref[:, cols], preferred_element_type=jnp.float32)
            acc += jnp.dot(p_c.astype(jnp.bfloat16), vc_ref[:, cols], preferred_element_type=jnp.float32)
            acc += jnp.dot(p_r.astype(jnp.bfloat16), vr_ref[:, cols], preferred_element_type=jnp.float32)
            o_ref[0:rows, cols] = (acc / denom).astype(o_ref.dtype)
            col_ref[:, h : h + 1] = shift
            col_ref[:, hg + h : hg + h + 1] = denom
        _store_stats(o_ref, st_ref, jnp.transpose(col_ref[...]), hg, rows)

    @pl.when(jnp.logical_not(seg_ok))
    def _():
        row = lax.broadcasted_iota(jnp.int32, o_ref.shape, 0)
        lane = lax.broadcasted_iota(jnp.int32, o_ref.shape, 1)
        empty = (row >= rows) & (row < rows + hg) & (lane < rows)
        o_ref[...] = jnp.where(empty, NEG, 0.0).astype(o_ref.dtype)


def attend(flags, q, k, v, kv_l, kv_r, width, base, q_base):
    rows = k.shape[0]
    heads = width // HEAD_DIM
    groups = heads // HG
    lanes = HG * HEAD_DIM
    q_spec = pl.BlockSpec((rows, lanes), lambda g, f: (0, g + q_base))
    kv_spec = pl.BlockSpec((rows, lanes), lambda g, f: (0, g + base))
    side_k = pl.BlockSpec((None, rows, lanes), lambda g, f: (0, 0, g + base))
    side_v = pl.BlockSpec((None, rows, lanes), lambda g, f: (1, 0, g + base))
    return pl.pallas_call(
        _attn_kernel,
        out_shape=jax.ShapeDtypeStruct((rows + EXTRA, width), jnp.bfloat16),
        grid_spec=pltpu.PrefetchScalarGridSpec(
            num_scalar_prefetch=1,
            grid=(groups,),
            in_specs=[q_spec, side_k, kv_spec, side_k, side_v, kv_spec, side_v],
            out_specs=pl.BlockSpec((rows + EXTRA, lanes), lambda g, f: (0, g)),
            scratch_shapes=[pltpu.VMEM((rows, 128), jnp.float32), pltpu.VMEM((EXTRA, lanes), jnp.float32)],
        ),
        cost_estimate=pl.CostEstimate(
            flops=4 * rows * 3 * rows * HEAD_DIM * heads,
            transcendentals=rows * 3 * rows * heads,
            bytes_accessed=2 * rows * width * 2 + 6 * rows * width * 2,
        ),
    )(flags, q, kv_l, k, kv_r, kv_l, v, kv_r)


def _merge_weights(valid_ref, a_ref, b_ref, wt_ref):
    rows = wt_ref.shape[1]
    hg = a_ref.shape[1] // HEAD_DIM
    a_top, a_den = _load_stats(a_ref, hg, rows)
    ok = valid_ref[0] == 1
    b_top, b_den = _load_stats(b_ref, hg, rows)
    b_top = jnp.where(ok, b_top, NEG)
    b_den = jnp.where(ok, b_den, 0.0)
    top = jnp.maximum(a_top, b_top)
    a_w = jnp.exp(a_top - top) * a_den
    b_w = jnp.exp(b_top - top) * b_den
    total = a_w + b_w
    safe = jnp.where(total > 0.0, total, 1.0)
    wt_ref[0:hg, :] = a_w / safe
    wt_ref[8 : 8 + hg, :] = b_w / safe
    return top, total, jnp.transpose(wt_ref[...])


def _merge_body(a_ref, b_ref, o_ref, w, hg, rows):
    for h in range(hg):
        cols = slice(h * HEAD_DIM, (h + 1) * HEAD_DIM)
        o = a_ref[0:rows, cols].astype(jnp.float32) * w[:, h : h + 1]
        o = o + b_ref[0:rows, cols].astype(jnp.float32) * w[:, 8 + h : 9 + h]
        o_ref[0:rows, cols] = o.astype(o_ref.dtype)


def _merge_kernel(valid_ref, a_ref, b_ref, o_ref, wt_ref, st_ref):
    rows = wt_ref.shape[1]
    hg = o_ref.shape[1] // HEAD_DIM
    top, total, w = _merge_weights(valid_ref, a_ref, b_ref, wt_ref)
    _merge_body(a_ref, b_ref, o_ref, w, hg, rows)
    wt_ref[0:hg, :] = top
    wt_ref[hg : 2 * hg, :] = total
    _store_stats(o_ref, st_ref, wt_ref[...], hg, rows)


def _final_kernel(valid_ref, a_ref, b_ref, *rest):
    o_ref, wt_ref = rest[-2], rest[-1]
    rows = wt_ref.shape[1]
    _, _, w = _merge_weights(valid_ref, a_ref, b_ref, wt_ref)
    _merge_body(a_ref, b_ref, o_ref, w, o_ref.shape[1] // HEAD_DIM, rows)


def merge(valid, a, b, base, final=False, buf=None, out_width=None):
    ext, width = b.shape
    rows = ext - EXTRA
    groups = width // HEAD_DIM // HG
    lanes = HG * HEAD_DIM
    a_base = 0 if out_width is not None else base
    a_spec = pl.BlockSpec((ext, lanes), lambda g, v: (0, g + a_base))
    b_spec = pl.BlockSpec((ext, lanes), lambda g, v: (0, g))
    in_specs = [a_spec, b_spec]
    operands = [valid, a, b]
    aliases = {}
    if final:
        kernel = _final_kernel
        out_shape = jax.ShapeDtypeStruct((rows, out_width or a.shape[1]), jnp.bfloat16)
        out_spec = pl.BlockSpec((rows, lanes), lambda g, v: (0, g + base))
        if buf is not None:
            in_specs.append(pl.BlockSpec(memory_space=pl.ANY))
            operands.append(buf)
            aliases = {3: 0}
    else:
        kernel = _merge_kernel
        out_shape = jax.ShapeDtypeStruct((ext, width), jnp.bfloat16)
        out_spec = b_spec
    return pl.pallas_call(
        kernel,
        out_shape=out_shape,
        grid_spec=pltpu.PrefetchScalarGridSpec(
            num_scalar_prefetch=1,
            grid=(groups,),
            in_specs=in_specs,
            out_specs=out_spec,
            scratch_shapes=[pltpu.VMEM((128, rows), jnp.float32)]
            + ([] if final else [pltpu.VMEM((EXTRA, lanes), jnp.float32)]),
        ),
        input_output_aliases=aliases,
        cost_estimate=pl.CostEstimate(
            flops=4 * rows * width, transcendentals=0, bytes_accessed=3 * rows * width * 2
        ),
    )(*operands)


def shift_tm(x, by):
    size = lax.axis_size("tm")
    pairs = [(i, i + by) for i in range(size) if 0 <= i + by < size]
    return lax.ppermute(x, "tm", pairs)


def on_device(query_states, key_states, value_states, history, neighbours):
    _, rows, width = query_states.shape
    seg = lax.axis_index("tm")
    tile = lax.axis_index("space")
    tiles = lax.axis_size("space")
    q = query_states[0]
    k = key_states[0]
    v = value_states[0]
    tile_l = tile > 0
    tile_r = tile < tiles - 1

    def flags_for(m, d):
        m = m.astype(jnp.int32)
        return jnp.stack(
            [
                ((m[1] == 1) & tile_l).astype(jnp.int32),
                (m[0] >= d).astype(jnp.int32),
                ((m[2] == 1) & tile_r).astype(jnp.int32),
            ]
        )

    meta = jnp.concatenate([history.reshape(1), neighbours.reshape(2)]).astype(jnp.bfloat16)
    chunk_w = width // CHUNKS
    groups_c = chunk_w // HEAD_DIM // HG
    meta_rows = jnp.zeros((EXTRA, chunk_w), jnp.bfloat16).at[0, 0:3].set(meta)
    sends = [jnp.concatenate([q[:, :chunk_w], meta_rows], axis=0)]
    sends += [q[:, c * chunk_w : (c + 1) * chunk_w] for c in range(1, CHUNKS)]
    q1s = [shift_tm(x, -1) for x in sends]

    kv = jnp.stack([k, v])
    kv_l = lax.ppermute(kv, "space", [(i, i + 1) for i in range(tiles - 1)])
    kv_r = lax.ppermute(kv, "space", [(i + 1, i) for i in range(tiles - 1)])

    f1 = flags_for(q1s[0][rows, 0:3], 1)
    p1s, q2s = [], []
    for c in range(CHUNKS):
        p1 = attend(f1, q1s[c], k, v, kv_l, kv_r, chunk_w, c * groups_c, 0)
        relay, p1 = lax.optimization_barrier((q1s[c], p1))
        p1s.append(p1)
        q2s.append(shift_tm(relay, -1))

    valid = (seg >= 1).astype(jnp.int32).reshape(1)
    f0 = flags_for(meta, 0)
    f2 = flags_for(q2s[0][rows, 0:3], 2)
    result = None
    q_self = q
    for c in range(CHUNKS):
        base = c * groups_c
        p_self = attend(f0, q_self, k, v, kv_l, kv_r, chunk_w, base, base)
        q2, p_self = lax.optimization_barrier((q2s[c], p_self))
        p2 = attend(f2, q2, k, v, kv_l, kv_r, chunk_w, base, 0)
        q_self, p2 = lax.optimization_barrier((q, p2))
        p2_in = shift_tm(p2, 1)
        pc = merge(valid, p1s[c], p2_in, 0)
        pc_in = shift_tm(pc, 1)
        result = merge(valid, p_self, pc_in, base, final=True, buf=result, out_width=width)
    return result.reshape(1, rows, width)


def solution(mesh):
    placed = (
        P("tm", "space", None),
        P("tm", "space", None),
        P("tm", "space", None),
        P("tm"),
        P("tm", "space", None),
    )
    return jax.shard_map(
        on_device, mesh=mesh, in_specs=placed, out_specs=P("tm", "space", None), check_vma=False
    )
```

```python
import jax
import jax.numpy as jnp
from jax import lax
from jax.experimental import pallas as pl
from jax.experimental.pallas import tpu as pltpu
from jax.sharding import PartitionSpec as P

HEAD_DIM = 128
HG = 5
CHUNKS = 2
NEG = -1e30
EXTRA = 16


def _store_stats(o_ref, st_ref, t, hg, rows):
    hi = t[0 : 2 * hg].astype(jnp.bfloat16).astype(jnp.float32)
    st_ref[...] = jnp.zeros_like(st_ref)
    st_ref[0 : 2 * hg, 0:rows] = hi
    st_ref[0 : 2 * hg, rows : 2 * rows] = t[0 : 2 * hg] - hi
    o_ref[rows : rows + EXTRA, :] = st_ref[...].astype(o_ref.dtype)


def _load_stats(ref, hg, rows):
    block = ref[rows : rows + EXTRA, :].astype(jnp.float32)
    full = block[0 : 2 * hg, 0:rows] + block[0 : 2 * hg, rows : 2 * rows]
    return full[0:hg], full[hg : 2 * hg]


def _attn_kernel(flags_ref, q_ref, kl_ref, kc_ref, kr_ref, vl_ref, vc_ref, vr_ref, o_ref, col_ref, st_ref):
    hg = q_ref.shape[1] // HEAD_DIM
    rows = q_ref.shape[0]
    lanes = o_ref.shape[1]
    inv_root = 1.0 / HEAD_DIM**0.5
    seg_ok = flags_ref[1] == 1

    @pl.when(seg_ok)
    def _():
        bias_l = jnp.where(flags_ref[0] == 1, 0.0, NEG).astype(jnp.float32)
        bias_r = jnp.where(flags_ref[2] == 1, 0.0, NEG).astype(jnp.float32)
        col_ref[...] = jnp.zeros_like(col_ref)
        for h in range(hg):
            cols = slice(h * HEAD_DIM, (h + 1) * HEAD_DIM)
            q = q_ref[:, cols]

            def scores(k_ref):
                return (
                    lax.dot_general(
                        q, k_ref[:, cols], (((1,), (1,)), ((), ())), preferred_element_type=jnp.float32
                    )
                    * inv_root
                )

            s_l = scores(kl_ref) + bias_l
            s_c = scores(kc_ref)
            s_r = scores(kr_ref) + bias_r
            top = jnp.maximum(
                jnp.maximum(s_l.max(axis=1, keepdims=True), s_c.max(axis=1, keepdims=True)),
                s_r.max(axis=1, keepdims=True),
            )
            shift = top
            p_l = jnp.exp(s_l - shift)
            p_c = jnp.exp(s_c - shift)
            p_r = jnp.exp(s_r - shift)
            denom = (
                p_l.sum(axis=1, keepdims=True) + p_c.sum(axis=1, keepdims=True) + p_r.sum(axis=1, keepdims=True)
            )
            acc = jnp.dot(p_l.astype(jnp.bfloat16), vl_ref[:, cols], preferred_element_type=jnp.float32)
            acc += jnp.dot(p_c.astype(jnp.bfloat16), vc_ref[:, cols], preferred_element_type=jnp.float32)
            acc += jnp.dot(p_r.astype(jnp.bfloat16), vr_ref[:, cols], preferred_element_type=jnp.float32)
            o_ref[0:rows, cols] = (acc / denom).astype(o_ref.dtype)
            col_ref[:, h : h + 1] = shift
            col_ref[:, hg + h : hg + h + 1] = denom
        _store_stats(o_ref, st_ref, jnp.transpose(col_ref[...]), hg, rows)

    @pl.when(jnp.logical_not(seg_ok))
    def _():
        row = lax.broadcasted_iota(jnp.int32, o_ref.shape, 0)
        lane = lax.broadcasted_iota(jnp.int32, o_ref.shape, 1)
        empty = (row >= rows) & (row < rows + hg) & (lane < rows)
        o_ref[...] = jnp.where(empty, NEG, 0.0).astype(o_ref.dtype)


def attend(flags, q, k, v, kv_l, kv_r, width, base, q_base):
    rows = k.shape[0]
    heads = width // HEAD_DIM
    groups = heads // HG
    lanes = HG * HEAD_DIM
    q_spec = pl.BlockSpec((rows, lanes), lambda g, f: (0, g + q_base))
    kv_spec = pl.BlockSpec((rows, lanes), lambda g, f: (0, g + base))
    side_k = pl.BlockSpec((None, rows, lanes), lambda g, f: (0, 0, g + base))
    side_v = pl.BlockSpec((None, rows, lanes), lambda g, f: (1, 0, g + base))
    return pl.pallas_call(
        _attn_kernel,
        out_shape=jax.ShapeDtypeStruct((rows + EXTRA, width), jnp.bfloat16),
        grid_spec=pltpu.PrefetchScalarGridSpec(
            num_scalar_prefetch=1,
            grid=(groups,),
            in_specs=[q_spec, side_k, kv_spec, side_k, side_v, kv_spec, side_v],
            out_specs=pl.BlockSpec((rows + EXTRA, lanes), lambda g, f: (0, g)),
            scratch_shapes=[pltpu.VMEM((rows, 128), jnp.float32), pltpu.VMEM((EXTRA, lanes), jnp.float32)],
        ),
        cost_estimate=pl.CostEstimate(
            flops=4 * rows * 3 * rows * HEAD_DIM * heads,
            transcendentals=rows * 3 * rows * heads,
            bytes_accessed=2 * rows * width * 2 + 6 * rows * width * 2,
        ),
    )(flags, q, kv_l, k, kv_r, kv_l, v, kv_r)


def _merge_weights(valid_ref, a_ref, b_ref, wt_ref):
    rows = wt_ref.shape[1]
    hg = a_ref.shape[1] // HEAD_DIM
    a_top, a_den = _load_stats(a_ref, hg, rows)
    ok = valid_ref[0] == 1
    b_top, b_den = _load_stats(b_ref, hg, rows)
    b_top = jnp.where(ok, b_top, NEG)
    b_den = jnp.where(ok, b_den, 0.0)
    top = jnp.maximum(a_top, b_top)
    a_w = jnp.exp(a_top - top) * a_den
    b_w = jnp.exp(b_top - top) * b_den
    total = a_w + b_w
    safe = jnp.where(total > 0.0, total, 1.0)
    wt_ref[0:hg, :] = a_w / safe
    wt_ref[8 : 8 + hg, :] = b_w / safe
    return top, total, jnp.transpose(wt_ref[...])


def _merge_body(a_ref, b_ref, o_ref, w, hg, rows):
    for h in range(hg):
        cols = slice(h * HEAD_DIM, (h + 1) * HEAD_DIM)
        o = a_ref[0:rows, cols].astype(jnp.float32) * w[:, h : h + 1]
        o = o + b_ref[0:rows, cols].astype(jnp.float32) * w[:, 8 + h : 9 + h]
        o_ref[0:rows, cols] = o.astype(o_ref.dtype)


def _merge_kernel(valid_ref, a_ref, b_ref, o_ref, wt_ref, st_ref):
    rows = wt_ref.shape[1]
    hg = o_ref.shape[1] // HEAD_DIM
    top, total, w = _merge_weights(valid_ref, a_ref, b_ref, wt_ref)
    _merge_body(a_ref, b_ref, o_ref, w, hg, rows)
    wt_ref[0:hg, :] = top
    wt_ref[hg : 2 * hg, :] = total
    _store_stats(o_ref, st_ref, wt_ref[...], hg, rows)


def _final_kernel(valid_ref, a_ref, b_ref, *rest):
    o_ref, wt_ref = rest[-2], rest[-1]
    rows = wt_ref.shape[1]
    _, _, w = _merge_weights(valid_ref, a_ref, b_ref, wt_ref)
    _merge_body(a_ref, b_ref, o_ref, w, o_ref.shape[1] // HEAD_DIM, rows)


def merge(valid, a, b, base, final=False, buf=None, out_width=None):
    ext, width = b.shape
    rows = ext - EXTRA
    groups = width // HEAD_DIM // HG
    lanes = HG * HEAD_DIM
    a_base = 0 if out_width is not None else base
    a_spec = pl.BlockSpec((ext, lanes), lambda g, v: (0, g + a_base))
    b_spec = pl.BlockSpec((ext, lanes), lambda g, v: (0, g))
    in_specs = [a_spec, b_spec]
    operands = [valid, a, b]
    aliases = {}
    if final:
        kernel = _final_kernel
        out_shape = jax.ShapeDtypeStruct((rows, out_width or a.shape[1]), jnp.bfloat16)
        out_spec = pl.BlockSpec((rows, lanes), lambda g, v: (0, g + base))
        if buf is not None:
            in_specs.append(pl.BlockSpec(memory_space=pl.ANY))
            operands.append(buf)
            aliases = {3: 0}
    else:
        kernel = _merge_kernel
        out_shape = jax.ShapeDtypeStruct((ext, width), jnp.bfloat16)
        out_spec = b_spec
    return pl.pallas_call(
        kernel,
        out_shape=out_shape,
        grid_spec=pltpu.PrefetchScalarGridSpec(
            num_scalar_prefetch=1,
            grid=(groups,),
            in_specs=in_specs,
            out_specs=out_spec,
            scratch_shapes=[pltpu.VMEM((128, rows), jnp.float32)]
            + ([] if final else [pltpu.VMEM((EXTRA, lanes), jnp.float32)]),
        ),
        input_output_aliases=aliases,
        cost_estimate=pl.CostEstimate(
            flops=4 * rows * width, transcendentals=0, bytes_accessed=3 * rows * width * 2
        ),
    )(*operands)


def _split_kernel(meta_ref, q_ref, *out_refs):
    rows = q_ref.shape[0]
    chunk_w = out_refs[0].shape[1]
    for c, o_ref in enumerate(out_refs):
        o_ref[0:rows, :] = q_ref[:, c * chunk_w : (c + 1) * chunk_w]
    row = lax.broadcasted_iota(jnp.int32, (EXTRA, chunk_w), 0)
    lane = lax.broadcasted_iota(jnp.int32, (EXTRA, chunk_w), 1)
    extra = jnp.zeros((EXTRA, chunk_w), jnp.float32)
    for i in range(3):
        extra = jnp.where((row == 0) & (lane == i), meta_ref[i].astype(jnp.float32), extra)
    out_refs[0][rows : rows + EXTRA, :] = extra.astype(out_refs[0].dtype)


def split_queries(meta, q, chunks):
    rows, width = q.shape
    chunk_w = width // chunks
    shapes = [jax.ShapeDtypeStruct((rows + EXTRA, chunk_w), q.dtype)]
    shapes += [jax.ShapeDtypeStruct((rows, chunk_w), q.dtype)] * (chunks - 1)
    vmem = pltpu.MemorySpace.VMEM
    return pl.pallas_call(
        _split_kernel,
        out_shape=shapes,
        in_specs=[pl.BlockSpec(memory_space=pltpu.SMEM), pl.BlockSpec(memory_space=vmem)],
        out_specs=[pl.BlockSpec(memory_space=vmem)] * chunks,
    )(meta, q)


def shift_tm(x, by):
    size = lax.axis_size("tm")
    pairs = [(i, i + by) for i in range(size) if 0 <= i + by < size]
    return lax.ppermute(x, "tm", pairs)


def on_device(query_states, key_states, value_states, history, neighbours):
    _, rows, width = query_states.shape
    seg = lax.axis_index("tm")
    tile = lax.axis_index("space")
    tiles = lax.axis_size("space")
    q = query_states[0]
    k = key_states[0]
    v = value_states[0]
    tile_l = tile > 0
    tile_r = tile < tiles - 1

    def flags_for(m, d):
        m = m.astype(jnp.int32)
        return jnp.stack(
            [
                ((m[1] == 1) & tile_l).astype(jnp.int32),
                (m[0] >= d).astype(jnp.int32),
                ((m[2] == 1) & tile_r).astype(jnp.int32),
            ]
        )

    meta = jnp.concatenate([history.reshape(1), neighbours.reshape(2)]).astype(jnp.int32)
    chunk_w = width // CHUNKS
    groups_c = chunk_w // HEAD_DIM // HG
    sends = split_queries(meta, q, CHUNKS)
    q1s = [shift_tm(x, -1) for x in sends]

    kv = jnp.stack([k, v])
    kv_l = lax.ppermute(kv, "space", [(i, i + 1) for i in range(tiles - 1)])
    kv_r = lax.ppermute(kv, "space", [(i + 1, i) for i in range(tiles - 1)])

    f1 = flags_for(q1s[0][rows, 0:3], 1)
    p1s, q2s = [], []
    for c in range(CHUNKS):
        p1 = attend(f1, q1s[c], k, v, kv_l, kv_r, chunk_w, c * groups_c, 0)
        relay, p1 = lax.optimization_barrier((q1s[c], p1))
        p1s.append(p1)
        q2s.append(shift_tm(relay, -1))

    valid = (seg >= 1).astype(jnp.int32).reshape(1)
    f0 = flags_for(meta, 0)
    f2 = flags_for(q2s[0][rows, 0:3], 2)
    result = None
    q_self = q
    for c in range(CHUNKS):
        base = c * groups_c
        p_self = attend(f0, q_self, k, v, kv_l, kv_r, chunk_w, base, base)
        q2, p_self = lax.optimization_barrier((q2s[c], p_self))
        p2 = attend(f2, q2, k, v, kv_l, kv_r, chunk_w, base, 0)
        q_self, p2 = lax.optimization_barrier((q, p2))
        p2_in = shift_tm(p2, 1)
        pc = merge(valid, p1s[c], p2_in, 0)
        pc_in = shift_tm(pc, 1)
        result = merge(valid, p_self, pc_in, base, final=True, buf=result, out_width=width)
    return result.reshape(1, rows, width)


def solution(mesh):
    placed = (
        P("tm", "space", None),
        P("tm", "space", None),
        P("tm", "space", None),
        P("tm"),
        P("tm", "space", None),
    )
    return jax.shard_map(
        on_device, mesh=mesh, in_specs=placed, out_specs=P("tm", "space", None), check_vma=False
    )
```

```python
import jax
import jax.numpy as jnp
from jax import lax
from jax.experimental import pallas as pl
from jax.experimental.pallas import tpu as pltpu
from jax.sharding import PartitionSpec as P

HEAD_DIM = 128
HG = 5
CHUNKS = 2
NEG = -1e30
EXTRA = 16


def _store_stats(o_ref, st_ref, t, hg, rows):
    hi = t[0 : 2 * hg].astype(jnp.bfloat16).astype(jnp.float32)
    st_ref[...] = jnp.zeros_like(st_ref)
    st_ref[0 : 2 * hg, 0:rows] = hi
    st_ref[0 : 2 * hg, rows : 2 * rows] = t[0 : 2 * hg] - hi
    o_ref[rows : rows + EXTRA, :] = st_ref[...].astype(o_ref.dtype)


def _load_stats(ref, hg, rows):
    block = ref[rows : rows + EXTRA, :].astype(jnp.float32)
    full = block[0 : 2 * hg, 0:rows] + block[0 : 2 * hg, rows : 2 * rows]
    return full[0:hg], full[hg : 2 * hg]


def _attn_kernel(flags_ref, q_ref, kl_ref, kc_ref, kr_ref, vl_ref, vc_ref, vr_ref, o_ref, col_ref, st_ref):
    hg = q_ref.shape[1] // HEAD_DIM
    rows = q_ref.shape[0]
    lanes = o_ref.shape[1]
    inv_root = 1.0 / HEAD_DIM**0.5
    seg_ok = flags_ref[1] == 1

    @pl.when(seg_ok)
    def _():
        bias_l = jnp.where(flags_ref[0] == 1, 0.0, NEG).astype(jnp.float32)
        bias_r = jnp.where(flags_ref[2] == 1, 0.0, NEG).astype(jnp.float32)
        col_ref[...] = jnp.zeros_like(col_ref)
        for h in range(hg):
            cols = slice(h * HEAD_DIM, (h + 1) * HEAD_DIM)
            q = q_ref[:, cols]

            def scores(k_ref):
                return (
                    lax.dot_general(
                        q, k_ref[:, cols], (((1,), (1,)), ((), ())), preferred_element_type=jnp.float32
                    )
                    * inv_root
                )

            s_l = scores(kl_ref) + bias_l
            s_c = scores(kc_ref)
            s_r = scores(kr_ref) + bias_r
            top = jnp.maximum(
                jnp.maximum(s_l.max(axis=1, keepdims=True), s_c.max(axis=1, keepdims=True)),
                s_r.max(axis=1, keepdims=True),
            )
            shift = top
            p_l = jnp.exp(s_l - shift)
            p_c = jnp.exp(s_c - shift)
            p_r = jnp.exp(s_r - shift)
            denom = (
                p_l.sum(axis=1, keepdims=True) + p_c.sum(axis=1, keepdims=True) + p_r.sum(axis=1, keepdims=True)
            )
            acc = jnp.dot(p_l.astype(jnp.bfloat16), vl_ref[:, cols], preferred_element_type=jnp.float32)
            acc += jnp.dot(p_c.astype(jnp.bfloat16), vc_ref[:, cols], preferred_element_type=jnp.float32)
            acc += jnp.dot(p_r.astype(jnp.bfloat16), vr_ref[:, cols], preferred_element_type=jnp.float32)
            o_ref[0:rows, cols] = (acc / denom).astype(o_ref.dtype)
            col_ref[:, h : h + 1] = shift
            col_ref[:, hg + h : hg + h + 1] = denom
        _store_stats(o_ref, st_ref, jnp.transpose(col_ref[...]), hg, rows)

    @pl.when(jnp.logical_not(seg_ok))
    def _():
        row = lax.broadcasted_iota(jnp.int32, o_ref.shape, 0)
        lane = lax.broadcasted_iota(jnp.int32, o_ref.shape, 1)
        empty = (row >= rows) & (row < rows + hg) & (lane < rows)
        o_ref[...] = jnp.where(empty, NEG, 0.0).astype(o_ref.dtype)


def attend(flags, q, k, v, kv_l, kv_r, width, base, q_base):
    rows = k.shape[0]
    heads = width // HEAD_DIM
    groups = heads // HG
    lanes = HG * HEAD_DIM
    q_spec = pl.BlockSpec((rows, lanes), lambda g, f: (0, g + q_base))
    kv_spec = pl.BlockSpec((rows, lanes), lambda g, f: (0, g + base))
    side_k = pl.BlockSpec((None, rows, lanes), lambda g, f: (0, 0, g + base))
    side_v = pl.BlockSpec((None, rows, lanes), lambda g, f: (1, 0, g + base))
    return pl.pallas_call(
        _attn_kernel,
        out_shape=jax.ShapeDtypeStruct((rows + EXTRA, width), jnp.bfloat16),
        grid_spec=pltpu.PrefetchScalarGridSpec(
            num_scalar_prefetch=1,
            grid=(groups,),
            in_specs=[q_spec, side_k, kv_spec, side_k, side_v, kv_spec, side_v],
            out_specs=pl.BlockSpec((rows + EXTRA, lanes), lambda g, f: (0, g)),
            scratch_shapes=[pltpu.VMEM((rows, 128), jnp.float32), pltpu.VMEM((EXTRA, lanes), jnp.float32)],
        ),
        cost_estimate=pl.CostEstimate(
            flops=4 * rows * 3 * rows * HEAD_DIM * heads,
            transcendentals=rows * 3 * rows * heads,
            bytes_accessed=2 * rows * width * 2 + 6 * rows * width * 2,
        ),
    )(flags, q, kv_l, k, kv_r, kv_l, v, kv_r)


def _merge_weights(valid_ref, a_ref, b_ref, wt_ref):
    rows = wt_ref.shape[1]
    hg = a_ref.shape[1] // HEAD_DIM
    a_top, a_den = _load_stats(a_ref, hg, rows)
    ok = valid_ref[0] == 1
    b_top, b_den = _load_stats(b_ref, hg, rows)
    b_top = jnp.where(ok, b_top, NEG)
    b_den = jnp.where(ok, b_den, 0.0)
    top = jnp.maximum(a_top, b_top)
    a_w = jnp.exp(a_top - top) * a_den
    b_w = jnp.exp(b_top - top) * b_den
    total = a_w + b_w
    safe = jnp.where(total > 0.0, total, 1.0)
    wt_ref[0:hg, :] = a_w / safe
    wt_ref[8 : 8 + hg, :] = b_w / safe
    return top, total, jnp.transpose(wt_ref[...])


def _merge_body(a_ref, b_ref, o_ref, w, hg, rows):
    for h in range(hg):
        cols = slice(h * HEAD_DIM, (h + 1) * HEAD_DIM)
        o = a_ref[0:rows, cols].astype(jnp.float32) * w[:, h : h + 1]
        o = o + b_ref[0:rows, cols].astype(jnp.float32) * w[:, 8 + h : 9 + h]
        o_ref[0:rows, cols] = o.astype(o_ref.dtype)


def _merge_kernel(valid_ref, a_ref, b_ref, o_ref, wt_ref, st_ref):
    rows = wt_ref.shape[1]
    hg = o_ref.shape[1] // HEAD_DIM
    top, total, w = _merge_weights(valid_ref, a_ref, b_ref, wt_ref)
    _merge_body(a_ref, b_ref, o_ref, w, hg, rows)
    wt_ref[0:hg, :] = top
    wt_ref[hg : 2 * hg, :] = total
    _store_stats(o_ref, st_ref, wt_ref[...], hg, rows)


def _final_kernel(valid_ref, a_ref, b_ref, *rest):
    o_ref, wt_ref = rest[-2], rest[-1]
    rows = wt_ref.shape[1]
    _, _, w = _merge_weights(valid_ref, a_ref, b_ref, wt_ref)
    _merge_body(a_ref, b_ref, o_ref, w, o_ref.shape[1] // HEAD_DIM, rows)


def merge(valid, a, b, base, final=False, buf=None, out_width=None):
    ext, width = b.shape
    rows = ext - EXTRA
    groups = width // HEAD_DIM // HG
    lanes = HG * HEAD_DIM
    a_base = 0 if out_width is not None else base
    a_spec = pl.BlockSpec((ext, lanes), lambda g, v: (0, g + a_base))
    b_spec = pl.BlockSpec((ext, lanes), lambda g, v: (0, g))
    in_specs = [a_spec, b_spec]
    operands = [valid, a, b]
    aliases = {}
    if final:
        kernel = _final_kernel
        out_shape = jax.ShapeDtypeStruct((rows, out_width or a.shape[1]), jnp.bfloat16)
        out_spec = pl.BlockSpec((rows, lanes), lambda g, v: (0, g + base))
        if buf is not None:
            in_specs.append(pl.BlockSpec(memory_space=pl.ANY))
            operands.append(buf)
            aliases = {3: 0}
    else:
        kernel = _merge_kernel
        out_shape = jax.ShapeDtypeStruct((ext, width), jnp.bfloat16)
        out_spec = b_spec
    return pl.pallas_call(
        kernel,
        out_shape=out_shape,
        grid_spec=pltpu.PrefetchScalarGridSpec(
            num_scalar_prefetch=1,
            grid=(groups,),
            in_specs=in_specs,
            out_specs=out_spec,
            scratch_shapes=[pltpu.VMEM((128, rows), jnp.float32)]
            + ([] if final else [pltpu.VMEM((EXTRA, lanes), jnp.float32)]),
        ),
        input_output_aliases=aliases,
        cost_estimate=pl.CostEstimate(
            flops=4 * rows * width, transcendentals=0, bytes_accessed=3 * rows * width * 2
        ),
    )(*operands)


def shift_tm(x, by):
    size = lax.axis_size("tm")
    pairs = [(i, i + by) for i in range(size) if 0 <= i + by < size]
    return lax.ppermute(x, "tm", pairs)


def on_device(query_states, key_states, value_states, history, neighbours):
    _, rows, width = query_states.shape
    seg = lax.axis_index("tm")
    tile = lax.axis_index("space")
    tiles = lax.axis_size("space")
    q = query_states[0]
    k = key_states[0]
    v = value_states[0]
    tile_l = tile > 0
    tile_r = tile < tiles - 1

    def flags_for(m, d):
        m = m.astype(jnp.int32)
        return jnp.stack(
            [
                ((m[1] == 1) & tile_l).astype(jnp.int32),
                (m[0] >= d).astype(jnp.int32),
                ((m[2] == 1) & tile_r).astype(jnp.int32),
            ]
        )

    meta = jnp.concatenate([history.reshape(1), neighbours.reshape(2)]).astype(jnp.bfloat16)
    chunk_w = width // CHUNKS
    groups_c = chunk_w // HEAD_DIM // HG
    meta_rows = jnp.zeros((EXTRA, chunk_w), jnp.bfloat16).at[0, 0:3].set(meta)
    sends = [jnp.concatenate([q[:, :chunk_w], meta_rows], axis=0)]
    sends += [q[:, c * chunk_w : (c + 1) * chunk_w] for c in range(1, CHUNKS)]
    q1s = [shift_tm(x, -1) for x in sends]

    kv = jnp.stack([k, v])
    kv_l = lax.ppermute(kv, "space", [(i, i + 1) for i in range(tiles - 1)])
    kv_r = lax.ppermute(kv, "space", [(i + 1, i) for i in range(tiles - 1)])

    f1 = flags_for(q1s[0][rows, 0:3], 1)
    p1s, q2s = [], []
    for c in range(CHUNKS):
        p1s.append(attend(f1, q1s[c], k, v, kv_l, kv_r, chunk_w, c * groups_c, 0))
        relay = q1s[c]
        if c > 0:
            relay, p1s[0], p1s[c] = lax.optimization_barrier((relay, p1s[0], p1s[c]))
        q2s.append(shift_tm(relay, -1))

    valid = (seg >= 1).astype(jnp.int32).reshape(1)
    f0 = flags_for(meta, 0)
    f2 = flags_for(q2s[0][rows, 0:3], 2)
    result = None
    q_self = q
    for c in range(CHUNKS):
        base = c * groups_c
        p_self = attend(f0, q_self, k, v, kv_l, kv_r, chunk_w, base, base)
        q2, p_self = lax.optimization_barrier((q2s[c], p_self))
        p2 = attend(f2, q2, k, v, kv_l, kv_r, chunk_w, base, 0)
        q_self, p2 = lax.optimization_barrier((q, p2))
        p2_in = shift_tm(p2, 1)
        pc = merge(valid, p1s[c], p2_in, 0)
        pc_in = shift_tm(pc, 1)
        result = merge(valid, p_self, pc_in, base, final=True, buf=result, out_width=width)
    return result.reshape(1, rows, width)


def solution(mesh):
    placed = (
        P("tm", "space", None),
        P("tm", "space", None),
        P("tm", "space", None),
        P("tm"),
        P("tm", "space", None),
    )
    return jax.shard_map(
        on_device, mesh=mesh, in_specs=placed, out_specs=P("tm", "space", None), check_vma=False
    )
```

```python
import jax
import jax.numpy as jnp
from jax import lax
from jax.experimental import pallas as pl
from jax.experimental.pallas import tpu as pltpu
from jax.sharding import PartitionSpec as P

HEAD_DIM = 128
HG = 5
CHUNKS = 2
NEG = -1e30
EXTRA = 16


def _store_stats(o_ref, st_ref, t, hg, rows):
    hi = t[0 : 2 * hg].astype(jnp.bfloat16).astype(jnp.float32)
    st_ref[...] = jnp.zeros_like(st_ref)
    st_ref[0 : 2 * hg, 0:rows] = hi
    st_ref[0 : 2 * hg, rows : 2 * rows] = t[0 : 2 * hg] - hi
    o_ref[rows : rows + EXTRA, :] = st_ref[...].astype(o_ref.dtype)


def _load_stats(ref, hg, rows):
    block = ref[rows : rows + EXTRA, :].astype(jnp.float32)
    full = block[0 : 2 * hg, 0:rows] + block[0 : 2 * hg, rows : 2 * rows]
    return full[0:hg], full[hg : 2 * hg]


def _attn_kernel(flags_ref, q_ref, kl_ref, kc_ref, kr_ref, vl_ref, vc_ref, vr_ref, o_ref, col_ref, st_ref):
    hg = q_ref.shape[1] // HEAD_DIM
    rows = q_ref.shape[0]
    lanes = o_ref.shape[1]
    inv_root = 1.0 / HEAD_DIM**0.5
    seg_ok = flags_ref[1] == 1

    @pl.when(seg_ok)
    def _():
        bias_l = jnp.where(flags_ref[0] == 1, 0.0, NEG).astype(jnp.float32)
        bias_r = jnp.where(flags_ref[2] == 1, 0.0, NEG).astype(jnp.float32)
        col_ref[...] = jnp.zeros_like(col_ref)
        for h in range(hg):
            cols = slice(h * HEAD_DIM, (h + 1) * HEAD_DIM)
            q = q_ref[:, cols]

            def scores(k_ref):
                return (
                    lax.dot_general(
                        q, k_ref[:, cols], (((1,), (1,)), ((), ())), preferred_element_type=jnp.float32
                    )
                    * inv_root
                )

            s_l = scores(kl_ref) + bias_l
            s_c = scores(kc_ref)
            s_r = scores(kr_ref) + bias_r
            top = jnp.maximum(
                jnp.maximum(s_l.max(axis=1, keepdims=True), s_c.max(axis=1, keepdims=True)),
                s_r.max(axis=1, keepdims=True),
            )
            shift = top
            p_l = jnp.exp(s_l - shift)
            p_c = jnp.exp(s_c - shift)
            p_r = jnp.exp(s_r - shift)
            denom = (
                p_l.sum(axis=1, keepdims=True) + p_c.sum(axis=1, keepdims=True) + p_r.sum(axis=1, keepdims=True)
            )
            acc = jnp.dot(p_l.astype(jnp.bfloat16), vl_ref[:, cols], preferred_element_type=jnp.float32)
            acc += jnp.dot(p_c.astype(jnp.bfloat16), vc_ref[:, cols], preferred_element_type=jnp.float32)
            acc += jnp.dot(p_r.astype(jnp.bfloat16), vr_ref[:, cols], preferred_element_type=jnp.float32)
            o_ref[0:rows, cols] = (acc / denom).astype(o_ref.dtype)
            col_ref[:, h : h + 1] = shift
            col_ref[:, hg + h : hg + h + 1] = denom
        _store_stats(o_ref, st_ref, jnp.transpose(col_ref[...]), hg, rows)

    @pl.when(jnp.logical_not(seg_ok))
    def _():
        row = lax.broadcasted_iota(jnp.int32, o_ref.shape, 0)
        lane = lax.broadcasted_iota(jnp.int32, o_ref.shape, 1)
        empty = (row >= rows) & (row < rows + hg) & (lane < rows)
        o_ref[...] = jnp.where(empty, NEG, 0.0).astype(o_ref.dtype)


def attend(flags, q, k, v, kv_l, kv_r, width, base, q_base):
    rows = k.shape[0]
    heads = width // HEAD_DIM
    groups = heads // HG
    lanes = HG * HEAD_DIM
    q_spec = pl.BlockSpec((rows, lanes), lambda g, f: (0, g + q_base))
    kv_spec = pl.BlockSpec((rows, lanes), lambda g, f: (0, g + base))
    side_k = pl.BlockSpec((None, rows, lanes), lambda g, f: (0, 0, g + base))
    side_v = pl.BlockSpec((None, rows, lanes), lambda g, f: (1, 0, g + base))
    return pl.pallas_call(
        _attn_kernel,
        out_shape=jax.ShapeDtypeStruct((rows + EXTRA, width), jnp.bfloat16),
        grid_spec=pltpu.PrefetchScalarGridSpec(
            num_scalar_prefetch=1,
            grid=(groups,),
            in_specs=[q_spec, side_k, kv_spec, side_k, side_v, kv_spec, side_v],
            out_specs=pl.BlockSpec((rows + EXTRA, lanes), lambda g, f: (0, g)),
            scratch_shapes=[pltpu.VMEM((rows, 128), jnp.float32), pltpu.VMEM((EXTRA, lanes), jnp.float32)],
        ),
        cost_estimate=pl.CostEstimate(
            flops=4 * rows * 3 * rows * HEAD_DIM * heads,
            transcendentals=rows * 3 * rows * heads,
            bytes_accessed=2 * rows * width * 2 + 6 * rows * width * 2,
        ),
    )(flags, q, kv_l, k, kv_r, kv_l, v, kv_r)


def _merge_weights(valid_ref, a_ref, b_ref, wt_ref):
    rows = wt_ref.shape[1]
    hg = a_ref.shape[1] // HEAD_DIM
    a_top, a_den = _load_stats(a_ref, hg, rows)
    ok = valid_ref[0] == 1
    b_top, b_den = _load_stats(b_ref, hg, rows)
    b_top = jnp.where(ok, b_top, NEG)
    b_den = jnp.where(ok, b_den, 0.0)
    top = jnp.maximum(a_top, b_top)
    a_w = jnp.exp(a_top - top) * a_den
    b_w = jnp.exp(b_top - top) * b_den
    total = a_w + b_w
    safe = jnp.where(total > 0.0, total, 1.0)
    wt_ref[0:hg, :] = a_w / safe
    wt_ref[8 : 8 + hg, :] = b_w / safe
    return top, total, jnp.transpose(wt_ref[...])


def _merge_body(a_ref, b_ref, o_ref, w, hg, rows):
    for h in range(hg):
        cols = slice(h * HEAD_DIM, (h + 1) * HEAD_DIM)
        o = a_ref[0:rows, cols].astype(jnp.float32) * w[:, h : h + 1]
        o = o + b_ref[0:rows, cols].astype(jnp.float32) * w[:, 8 + h : 9 + h]
        o_ref[0:rows, cols] = o.astype(o_ref.dtype)


def _merge_kernel(valid_ref, a_ref, b_ref, o_ref, wt_ref, st_ref):
    rows = wt_ref.shape[1]
    hg = o_ref.shape[1] // HEAD_DIM
    top, total, w = _merge_weights(valid_ref, a_ref, b_ref, wt_ref)
    _merge_body(a_ref, b_ref, o_ref, w, hg, rows)
    wt_ref[0:hg, :] = top
    wt_ref[hg : 2 * hg, :] = total
    _store_stats(o_ref, st_ref, wt_ref[...], hg, rows)


def _final_kernel(valid_ref, a_ref, b_ref, *rest):
    o_ref, wt_ref = rest[-2], rest[-1]
    rows = wt_ref.shape[1]
    _, _, w = _merge_weights(valid_ref, a_ref, b_ref, wt_ref)
    _merge_body(a_ref, b_ref, o_ref, w, o_ref.shape[1] // HEAD_DIM, rows)


def merge(valid, a, b, base, final=False, buf=None, out_width=None):
    ext, width = b.shape
    rows = ext - EXTRA
    groups = width // HEAD_DIM // HG
    lanes = HG * HEAD_DIM
    a_base = 0 if out_width is not None else base
    a_spec = pl.BlockSpec((ext, lanes), lambda g, v: (0, g + a_base))
    b_spec = pl.BlockSpec((ext, lanes), lambda g, v: (0, g))
    in_specs = [a_spec, b_spec]
    operands = [valid, a, b]
    aliases = {}
    if final:
        kernel = _final_kernel
        out_shape = jax.ShapeDtypeStruct((rows, out_width or a.shape[1]), jnp.bfloat16)
        out_spec = pl.BlockSpec((rows, lanes), lambda g, v: (0, g + base))
        if buf is not None:
            in_specs.append(pl.BlockSpec(memory_space=pl.ANY))
            operands.append(buf)
            aliases = {3: 0}
    else:
        kernel = _merge_kernel
        out_shape = jax.ShapeDtypeStruct((ext, width), jnp.bfloat16)
        out_spec = b_spec
    return pl.pallas_call(
        kernel,
        out_shape=out_shape,
        grid_spec=pltpu.PrefetchScalarGridSpec(
            num_scalar_prefetch=1,
            grid=(groups,),
            in_specs=in_specs,
            out_specs=out_spec,
            scratch_shapes=[pltpu.VMEM((128, rows), jnp.float32)]
            + ([] if final else [pltpu.VMEM((EXTRA, lanes), jnp.float32)]),
        ),
        input_output_aliases=aliases,
        cost_estimate=pl.CostEstimate(
            flops=4 * rows * width, transcendentals=0, bytes_accessed=3 * rows * width * 2
        ),
    )(*operands)


def shift_tm(x, by):
    size = lax.axis_size("tm")
    pairs = [(i, i + by) for i in range(size) if 0 <= i + by < size]
    return lax.ppermute(x, "tm", pairs)


def on_device(query_states, key_states, value_states, history, neighbours):
    _, rows, width = query_states.shape
    seg = lax.axis_index("tm")
    tile = lax.axis_index("space")
    tiles = lax.axis_size("space")
    q = query_states[0]
    k = key_states[0]
    v = value_states[0]
    tile_l = tile > 0
    tile_r = tile < tiles - 1

    def flags_for(m, d):
        m = m.astype(jnp.int32)
        return jnp.stack(
            [
                ((m[1] == 1) & tile_l).astype(jnp.int32),
                (m[0] >= d).astype(jnp.int32),
                ((m[2] == 1) & tile_r).astype(jnp.int32),
            ]
        )

    meta = jnp.concatenate([history.reshape(1), neighbours.reshape(2)]).astype(jnp.bfloat16)
    chunk_w = width // CHUNKS
    groups_c = chunk_w // HEAD_DIM // HG
    meta_rows = jnp.zeros((EXTRA, chunk_w), jnp.bfloat16).at[0, 0:3].set(meta)
    sends = [jnp.concatenate([q[:, :chunk_w], meta_rows], axis=0)]
    sends += [q[:, c * chunk_w : (c + 1) * chunk_w] for c in range(1, CHUNKS)]
    q1s = [shift_tm(sends[0], -1)]

    kv = jnp.stack([k, v])
    kv_l = lax.ppermute(kv, "space", [(i, i + 1) for i in range(tiles - 1)])
    kv_r = lax.ppermute(kv, "space", [(i + 1, i) for i in range(tiles - 1)])

    f1 = flags_for(q1s[0][rows, 0:3], 1)
    f0 = flags_for(meta, 0)
    valid = (seg >= 1).astype(jnp.int32).reshape(1)
    result = None
    q_pa, q_self = q1s[0], q
    q2_prev = shift_tm(q1s[0], -1)
    f2 = flags_for(q2_prev[rows, 0:3], 2)
    for c in range(CHUNKS):
        base = c * groups_c
        if c == 0:
            q2 = q2_prev
        else:
            held, _ = lax.optimization_barrier((sends[c], q2_prev))
            q1 = shift_tm(held, -1)
            q_pa, _ = lax.optimization_barrier((q1, p2))
            q_relay = q1
        p1 = attend(f1, q_pa, k, v, kv_l, kv_r, chunk_w, base, 0)
        if c > 0:
            q_relay, p1 = lax.optimization_barrier((q_relay, p1))
            q2 = shift_tm(q_relay, -1)
        p_self = attend(f0, q_self, k, v, kv_l, kv_r, chunk_w, base, base)
        q2, p_self, p1 = lax.optimization_barrier((q2, p_self, p1))
        p2 = attend(f2, q2, k, v, kv_l, kv_r, chunk_w, base, 0)
        q_self, p2 = lax.optimization_barrier((q, p2))
        q2_prev = q2
        p2_in = shift_tm(p2, 1)
        pc = merge(valid, p1, p2_in, 0)
        pc_in = shift_tm(pc, 1)
        result = merge(valid, p_self, pc_in, base, final=True, buf=result, out_width=width)
    return result.reshape(1, rows, width)


def solution(mesh):
    placed = (
        P("tm", "space", None),
        P("tm", "space", None),
        P("tm", "space", None),
        P("tm"),
        P("tm", "space", None),
    )
    return jax.shard_map(
        on_device, mesh=mesh, in_specs=placed, out_specs=P("tm", "space", None), check_vma=False
    )
```

```python
import jax
import jax.numpy as jnp
from jax import lax
from jax.experimental import pallas as pl
from jax.experimental.pallas import tpu as pltpu
from jax.sharding import PartitionSpec as P

HEAD_DIM = 128
HG = 5
CHUNKS = 2
NEG = -1e30
EXTRA = 16


def _store_stats(o_ref, st_ref, t, hg, rows):
    top, den = t[0:hg], t[hg : 2 * hg]
    top_hi = top.astype(jnp.bfloat16).astype(jnp.float32)
    rest = top - top_hi
    top_mid = rest.astype(jnp.bfloat16).astype(jnp.float32)
    den_hi = den.astype(jnp.bfloat16).astype(jnp.float32)
    st_ref[...] = jnp.zeros_like(st_ref)
    st_ref[0:hg, 0:rows] = top_hi
    st_ref[0:hg, rows : 2 * rows] = top_mid
    st_ref[2 * hg : 3 * hg, 0:rows] = rest - top_mid
    st_ref[hg : 2 * hg, 0:rows] = den_hi
    st_ref[hg : 2 * hg, rows : 2 * rows] = den - den_hi
    o_ref[rows : rows + EXTRA, :] = st_ref[...].astype(o_ref.dtype)


def _load_stats(ref, hg, rows):
    block = ref[rows : rows + EXTRA, :].astype(jnp.float32)
    top = block[0:hg, 0:rows] + block[0:hg, rows : 2 * rows] + block[2 * hg : 3 * hg, 0:rows]
    den = block[hg : 2 * hg, 0:rows] + block[hg : 2 * hg, rows : 2 * rows]
    return top, den


def _attn_kernel(flags_ref, q_ref, kl_ref, kc_ref, kr_ref, vl_ref, vc_ref, vr_ref, o_ref, col_ref, st_ref):
    hg = q_ref.shape[1] // HEAD_DIM
    rows = q_ref.shape[0]
    lanes = o_ref.shape[1]
    inv_root = 1.0 / HEAD_DIM**0.5
    seg_ok = flags_ref[1] == 1

    @pl.when(seg_ok)
    def _():
        bias_l = jnp.where(flags_ref[0] == 1, 0.0, NEG).astype(jnp.float32)
        bias_r = jnp.where(flags_ref[2] == 1, 0.0, NEG).astype(jnp.float32)
        col_ref[...] = jnp.zeros_like(col_ref)
        for h in range(hg):
            cols = slice(h * HEAD_DIM, (h + 1) * HEAD_DIM)
            q = q_ref[:, cols]

            def scores(k_ref):
                return (
                    lax.dot_general(
                        q, k_ref[:, cols], (((1,), (1,)), ((), ())), preferred_element_type=jnp.float32
                    )
                    * inv_root
                )

            s_l = scores(kl_ref) + bias_l
            s_c = scores(kc_ref)
            s_r = scores(kr_ref) + bias_r
            top = jnp.maximum(
                jnp.maximum(s_l.max(axis=1, keepdims=True), s_c.max(axis=1, keepdims=True)),
                s_r.max(axis=1, keepdims=True),
            )
            shift = top
            p_l = jnp.exp(s_l - shift)
            p_c = jnp.exp(s_c - shift)
            p_r = jnp.exp(s_r - shift)
            denom = (
                p_l.sum(axis=1, keepdims=True) + p_c.sum(axis=1, keepdims=True) + p_r.sum(axis=1, keepdims=True)
            )
            acc = jnp.dot(p_l.astype(jnp.bfloat16), vl_ref[:, cols], preferred_element_type=jnp.float32)
            acc += jnp.dot(p_c.astype(jnp.bfloat16), vc_ref[:, cols], preferred_element_type=jnp.float32)
            acc += jnp.dot(p_r.astype(jnp.bfloat16), vr_ref[:, cols], preferred_element_type=jnp.float32)
            o_ref[0:rows, cols] = (acc / denom).astype(o_ref.dtype)
            col_ref[:, h : h + 1] = shift
            col_ref[:, hg + h : hg + h + 1] = denom
        _store_stats(o_ref, st_ref, jnp.transpose(col_ref[...]), hg, rows)

    @pl.when(jnp.logical_not(seg_ok))
    def _():
        row = lax.broadcasted_iota(jnp.int32, o_ref.shape, 0)
        lane = lax.broadcasted_iota(jnp.int32, o_ref.shape, 1)
        empty = (row >= rows) & (row < rows + hg) & (lane < rows)
        o_ref[...] = jnp.where(empty, NEG, 0.0).astype(o_ref.dtype)


def attend(flags, q, k, v, kv_l, kv_r, width, base, q_base):
    rows = k.shape[0]
    heads = width // HEAD_DIM
    groups = heads // HG
    lanes = HG * HEAD_DIM
    q_spec = pl.BlockSpec((rows, lanes), lambda g, f: (0, g + q_base))
    kv_spec = pl.BlockSpec((rows, lanes), lambda g, f: (0, g + base))
    side_k = pl.BlockSpec((None, rows, lanes), lambda g, f: (0, 0, g + base))
    side_v = pl.BlockSpec((None, rows, lanes), lambda g, f: (1, 0, g + base))
    return pl.pallas_call(
        _attn_kernel,
        out_shape=jax.ShapeDtypeStruct((rows + EXTRA, width), jnp.bfloat16),
        grid_spec=pltpu.PrefetchScalarGridSpec(
            num_scalar_prefetch=1,
            grid=(groups,),
            in_specs=[q_spec, side_k, kv_spec, side_k, side_v, kv_spec, side_v],
            out_specs=pl.BlockSpec((rows + EXTRA, lanes), lambda g, f: (0, g)),
            scratch_shapes=[pltpu.VMEM((rows, 128), jnp.float32), pltpu.VMEM((EXTRA, lanes), jnp.float32)],
        ),
        cost_estimate=pl.CostEstimate(
            flops=4 * rows * 3 * rows * HEAD_DIM * heads,
            transcendentals=rows * 3 * rows * heads,
            bytes_accessed=2 * rows * width * 2 + 6 * rows * width * 2,
        ),
    )(flags, q, kv_l, k, kv_r, kv_l, v, kv_r)


def _merge_weights(valid_ref, a_ref, b_ref, wt_ref):
    rows = wt_ref.shape[1]
    hg = a_ref.shape[1] // HEAD_DIM
    a_top, a_den = _load_stats(a_ref, hg, rows)
    ok = valid_ref[0] == 1
    b_top, b_den = _load_stats(b_ref, hg, rows)
    b_top = jnp.where(ok, b_top, NEG)
    b_den = jnp.where(ok, b_den, 0.0)
    top = jnp.maximum(a_top, b_top)
    a_w = jnp.exp(a_top - top) * a_den
    b_w = jnp.exp(b_top - top) * b_den
    total = a_w + b_w
    safe = jnp.where(total > 0.0, total, 1.0)
    wt_ref[0:hg, :] = a_w / safe
    wt_ref[8 : 8 + hg, :] = b_w / safe
    return top, total, jnp.transpose(wt_ref[...])


def _merge_body(a_ref, b_ref, o_ref, w, hg, rows):
    for h in range(hg):
        cols = slice(h * HEAD_DIM, (h + 1) * HEAD_DIM)
        o = a_ref[0:rows, cols].astype(jnp.float32) * w[:, h : h + 1]
        o = o + b_ref[0:rows, cols].astype(jnp.float32) * w[:, 8 + h : 9 + h]
        o_ref[0:rows, cols] = o.astype(o_ref.dtype)


def _merge_kernel(valid_ref, a_ref, b_ref, o_ref, wt_ref, st_ref):
    rows = wt_ref.shape[1]
    hg = o_ref.shape[1] // HEAD_DIM
    top, total, w = _merge_weights(valid_ref, a_ref, b_ref, wt_ref)
    _merge_body(a_ref, b_ref, o_ref, w, hg, rows)
    wt_ref[0:hg, :] = top
    wt_ref[hg : 2 * hg, :] = total
    _store_stats(o_ref, st_ref, wt_ref[...], hg, rows)


def _final_kernel(valid_ref, a_ref, b_ref, *rest):
    o_ref, wt_ref = rest[-2], rest[-1]
    rows = wt_ref.shape[1]
    _, _, w = _merge_weights(valid_ref, a_ref, b_ref, wt_ref)
    _merge_body(a_ref, b_ref, o_ref, w, o_ref.shape[1] // HEAD_DIM, rows)


def merge(valid, a, b, base, final=False, buf=None, out_width=None):
    ext, width = b.shape
    rows = ext - EXTRA
    groups = width // HEAD_DIM // HG
    lanes = HG * HEAD_DIM
    a_base = 0 if out_width is not None else base
    a_spec = pl.BlockSpec((ext, lanes), lambda g, v: (0, g + a_base))
    b_spec = pl.BlockSpec((ext, lanes), lambda g, v: (0, g))
    in_specs = [a_spec, b_spec]
    operands = [valid, a, b]
    aliases = {}
    if final:
        kernel = _final_kernel
        out_shape = jax.ShapeDtypeStruct((rows, out_width or a.shape[1]), jnp.bfloat16)
        out_spec = pl.BlockSpec((rows, lanes), lambda g, v: (0, g + base))
        if buf is not None:
            in_specs.append(pl.BlockSpec(memory_space=pl.ANY))
            operands.append(buf)
            aliases = {3: 0}
    else:
        kernel = _merge_kernel
        out_shape = jax.ShapeDtypeStruct((ext, width), jnp.bfloat16)
        out_spec = b_spec
    return pl.pallas_call(
        kernel,
        out_shape=out_shape,
        grid_spec=pltpu.PrefetchScalarGridSpec(
            num_scalar_prefetch=1,
            grid=(groups,),
            in_specs=in_specs,
            out_specs=out_spec,
            scratch_shapes=[pltpu.VMEM((128, rows), jnp.float32)]
            + ([] if final else [pltpu.VMEM((EXTRA, lanes), jnp.float32)]),
        ),
        input_output_aliases=aliases,
        cost_estimate=pl.CostEstimate(
            flops=4 * rows * width, transcendentals=0, bytes_accessed=3 * rows * width * 2
        ),
    )(*operands)


def shift_tm(x, by):
    size = lax.axis_size("tm")
    pairs = [(i, i + by) for i in range(size) if 0 <= i + by < size]
    return lax.ppermute(x, "tm", pairs)


def on_device(query_states, key_states, value_states, history, neighbours):
    _, rows, width = query_states.shape
    seg = lax.axis_index("tm")
    tile = lax.axis_index("space")
    tiles = lax.axis_size("space")
    q = query_states[0]
    k = key_states[0]
    v = value_states[0]
    tile_l = tile > 0
    tile_r = tile < tiles - 1

    def flags_for(m, d):
        m = m.astype(jnp.int32)
        return jnp.stack(
            [
                ((m[1] == 1) & tile_l).astype(jnp.int32),
                (m[0] >= d).astype(jnp.int32),
                ((m[2] == 1) & tile_r).astype(jnp.int32),
            ]
        )

    meta = jnp.concatenate([history.reshape(1), neighbours.reshape(2)]).astype(jnp.bfloat16)
    chunk_w = width // CHUNKS
    groups_c = chunk_w // HEAD_DIM // HG
    meta_rows = jnp.zeros((EXTRA, chunk_w), jnp.bfloat16).at[0, 0:3].set(meta)
    sends = [jnp.concatenate([q[:, :chunk_w], meta_rows], axis=0)]
    sends += [q[:, c * chunk_w : (c + 1) * chunk_w] for c in range(1, CHUNKS)]
    q1s = [shift_tm(x, -1) for x in sends]

    kv = jnp.stack([k, v])
    kv_l = lax.ppermute(kv, "space", [(i, i + 1) for i in range(tiles - 1)])
    kv_r = lax.ppermute(kv, "space", [(i + 1, i) for i in range(tiles - 1)])

    f1 = flags_for(q1s[0][rows, 0:3], 1)
    p1s, q2s = [], []
    for c in range(CHUNKS):
        p1s.append(attend(f1, q1s[c], k, v, kv_l, kv_r, chunk_w, c * groups_c, 0))
        relay = q1s[c]
        if c > 0:
            relay, p1s[0], p1s[c] = lax.optimization_barrier((relay, p1s[0], p1s[c]))
        q2s.append(shift_tm(relay, -1))

    valid = (seg >= 1).astype(jnp.int32).reshape(1)
    f0 = flags_for(meta, 0)
    f2 = flags_for(q2s[0][rows, 0:3], 2)
    result = None
    q_self = q
    for c in range(CHUNKS):
        base = c * groups_c
        p_self = attend(f0, q_self, k, v, kv_l, kv_r, chunk_w, base, base)
        q2, p_self = lax.optimization_barrier((q2s[c], p_self))
        p2 = attend(f2, q2, k, v, kv_l, kv_r, chunk_w, base, 0)
        q_self, p2 = lax.optimization_barrier((q, p2))
        p2_in = shift_tm(p2, 1)
        pc = merge(valid, p1s[c], p2_in, 0)
        pc_in = shift_tm(pc, 1)
        result = merge(valid, p_self, pc_in, base, final=True, buf=result, out_width=width)
    return result.reshape(1, rows, width)


def solution(mesh):
    placed = (
        P("tm", "space", None),
        P("tm", "space", None),
        P("tm", "space", None),
        P("tm"),
        P("tm", "space", None),
    )
    return jax.shard_map(
        on_device, mesh=mesh, in_specs=placed, out_specs=P("tm", "space", None), check_vma=False
    )
```

```python
import jax
import jax.numpy as jnp
from jax import lax
from jax.experimental import pallas as pl
from jax.experimental.pallas import tpu as pltpu
from jax.sharding import PartitionSpec as P

HEAD_DIM = 128
HG = 5
CHUNKS = 2
NEG = -1e30
EXTRA = 16


def _store_stats(o_ref, st_ref, t, hg, rows):
    top, den = t[0:hg], t[hg : 2 * hg]
    top_hi = top.astype(jnp.bfloat16).astype(jnp.float32)
    rest = top - top_hi
    top_mid = rest.astype(jnp.bfloat16).astype(jnp.float32)
    den_hi = den.astype(jnp.bfloat16).astype(jnp.float32)
    st_ref[...] = jnp.zeros_like(st_ref)
    st_ref[0:hg, 0:rows] = top_hi
    st_ref[0:hg, rows : 2 * rows] = top_mid
    st_ref[2 * hg : 3 * hg, 0:rows] = rest - top_mid
    st_ref[hg : 2 * hg, 0:rows] = den_hi
    st_ref[hg : 2 * hg, rows : 2 * rows] = den - den_hi
    o_ref[rows : rows + EXTRA, :] = st_ref[...].astype(o_ref.dtype)


def _load_stats(ref, hg, rows):
    block = ref[rows : rows + EXTRA, :].astype(jnp.float32)
    top = block[0:hg, 0:rows] + block[0:hg, rows : 2 * rows] + block[2 * hg : 3 * hg, 0:rows]
    den = block[hg : 2 * hg, 0:rows] + block[hg : 2 * hg, rows : 2 * rows]
    return top, den


def _attn_kernel(flags_ref, q_ref, kl_ref, kc_ref, kr_ref, vl_ref, vc_ref, vr_ref, o_ref, col_ref, st_ref):
    hg = q_ref.shape[1] // HEAD_DIM
    rows = q_ref.shape[0]
    lanes = o_ref.shape[1]
    inv_root = 1.0 / HEAD_DIM**0.5
    seg_ok = flags_ref[1] == 1

    @pl.when(seg_ok)
    def _():
        bias_l = jnp.where(flags_ref[0] == 1, 0.0, NEG).astype(jnp.float32)
        bias_r = jnp.where(flags_ref[2] == 1, 0.0, NEG).astype(jnp.float32)
        col_ref[...] = jnp.zeros_like(col_ref)
        for h in range(hg):
            cols = slice(h * HEAD_DIM, (h + 1) * HEAD_DIM)
            q = q_ref[:, cols]

            def scores(k_ref):
                return (
                    lax.dot_general(
                        q, k_ref[:, cols], (((1,), (1,)), ((), ())), preferred_element_type=jnp.float32
                    )
                    * inv_root
                )

            s_l = scores(kl_ref) + bias_l
            s_c = scores(kc_ref)
            s_r = scores(kr_ref) + bias_r
            top = jnp.maximum(
                jnp.maximum(s_l.max(axis=1, keepdims=True), s_c.max(axis=1, keepdims=True)),
                s_r.max(axis=1, keepdims=True),
            )
            shift = top
            p_l = jnp.exp(s_l - shift)
            p_c = jnp.exp(s_c - shift)
            p_r = jnp.exp(s_r - shift)
            denom = (
                p_l.sum(axis=1, keepdims=True) + p_c.sum(axis=1, keepdims=True) + p_r.sum(axis=1, keepdims=True)
            )
            acc = jnp.dot(p_l.astype(jnp.bfloat16), vl_ref[:, cols], preferred_element_type=jnp.float32)
            acc += jnp.dot(p_c.astype(jnp.bfloat16), vc_ref[:, cols], preferred_element_type=jnp.float32)
            acc += jnp.dot(p_r.astype(jnp.bfloat16), vr_ref[:, cols], preferred_element_type=jnp.float32)
            o_ref[0:rows, cols] = (acc / denom).astype(o_ref.dtype)
            col_ref[:, h : h + 1] = shift
            col_ref[:, hg + h : hg + h + 1] = denom
        _store_stats(o_ref, st_ref, jnp.transpose(col_ref[...]), hg, rows)

    @pl.when(jnp.logical_not(seg_ok))
    def _():
        row = lax.broadcasted_iota(jnp.int32, o_ref.shape, 0)
        lane = lax.broadcasted_iota(jnp.int32, o_ref.shape, 1)
        empty = (row >= rows) & (row < rows + hg) & (lane < rows)
        o_ref[...] = jnp.where(empty, NEG, 0.0).astype(o_ref.dtype)


def attend(flags, q, k, v, kv_l, kv_r, width, base, q_base):
    rows = k.shape[0]
    heads = width // HEAD_DIM
    groups = heads // HG
    lanes = HG * HEAD_DIM
    q_spec = pl.BlockSpec((rows, lanes), lambda g, f: (0, g + q_base))
    kv_spec = pl.BlockSpec((rows, lanes), lambda g, f: (0, g + base))
    side_k = pl.BlockSpec((None, rows, lanes), lambda g, f: (0, 0, g + base))
    side_v = pl.BlockSpec((None, rows, lanes), lambda g, f: (1, 0, g + base))
    return pl.pallas_call(
        _attn_kernel,
        out_shape=jax.ShapeDtypeStruct((rows + EXTRA, width), jnp.bfloat16),
        grid_spec=pltpu.PrefetchScalarGridSpec(
            num_scalar_prefetch=1,
            grid=(groups,),
            in_specs=[q_spec, side_k, kv_spec, side_k, side_v, kv_spec, side_v],
            out_specs=pl.BlockSpec((rows + EXTRA, lanes), lambda g, f: (0, g)),
            scratch_shapes=[pltpu.VMEM((rows, 128), jnp.float32), pltpu.VMEM((EXTRA, lanes), jnp.float32)],
        ),
        cost_estimate=pl.CostEstimate(
            flops=4 * rows * 3 * rows * HEAD_DIM * heads,
            transcendentals=rows * 3 * rows * heads,
            bytes_accessed=2 * rows * width * 2 + 6 * rows * width * 2,
        ),
    )(flags, q, kv_l, k, kv_r, kv_l, v, kv_r)


def _merge_weights(valid_ref, a_ref, b_ref, wt_ref):
    rows = wt_ref.shape[1]
    hg = a_ref.shape[1] // HEAD_DIM
    a_top, a_den = _load_stats(a_ref, hg, rows)
    ok = valid_ref[0] == 1
    b_top, b_den = _load_stats(b_ref, hg, rows)
    b_top = jnp.where(ok, b_top, NEG)
    b_den = jnp.where(ok, b_den, 0.0)
    top = jnp.maximum(a_top, b_top)
    a_w = jnp.exp(a_top - top) * a_den
    b_w = jnp.exp(b_top - top) * b_den
    total = a_w + b_w
    safe = jnp.where(total > 0.0, total, 1.0)
    wt_ref[0:hg, :] = a_w / safe
    wt_ref[8 : 8 + hg, :] = b_w / safe
    return top, total, jnp.transpose(wt_ref[...])


def _merge_body(a_ref, b_ref, o_ref, w, hg, rows):
    for h in range(hg):
        cols = slice(h * HEAD_DIM, (h + 1) * HEAD_DIM)
        o = a_ref[0:rows, cols].astype(jnp.float32) * w[:, h : h + 1]
        o = o + b_ref[0:rows, cols].astype(jnp.float32) * w[:, 8 + h : 9 + h]
        o_ref[0:rows, cols] = o.astype(o_ref.dtype)


def _merge_kernel(valid_ref, a_ref, b_ref, o_ref, wt_ref, st_ref):
    rows = wt_ref.shape[1]
    hg = o_ref.shape[1] // HEAD_DIM
    top, total, w = _merge_weights(valid_ref, a_ref, b_ref, wt_ref)
    _merge_body(a_ref, b_ref, o_ref, w, hg, rows)
    wt_ref[0:hg, :] = top
    wt_ref[hg : 2 * hg, :] = total
    _store_stats(o_ref, st_ref, wt_ref[...], hg, rows)


def _final_kernel(valid_ref, a_ref, b_ref, *rest):
    o_ref, wt_ref = rest[-2], rest[-1]
    rows = wt_ref.shape[1]
    _, _, w = _merge_weights(valid_ref, a_ref, b_ref, wt_ref)
    _merge_body(a_ref, b_ref, o_ref, w, o_ref.shape[1] // HEAD_DIM, rows)


def merge(valid, a, b, base, final=False, buf=None, out_width=None):
    ext, width = b.shape
    rows = ext - EXTRA
    groups = width // HEAD_DIM // HG
    lanes = HG * HEAD_DIM
    a_base = 0 if out_width is not None else base
    a_spec = pl.BlockSpec((ext, lanes), lambda g, v: (0, g + a_base))
    b_spec = pl.BlockSpec((ext, lanes), lambda g, v: (0, g))
    in_specs = [a_spec, b_spec]
    operands = [valid, a, b]
    aliases = {}
    if final:
        kernel = _final_kernel
        out_shape = jax.ShapeDtypeStruct((rows, out_width or a.shape[1]), jnp.bfloat16)
        out_spec = pl.BlockSpec((rows, lanes), lambda g, v: (0, g + base))
        if buf is not None:
            in_specs.append(pl.BlockSpec(memory_space=pl.ANY))
            operands.append(buf)
            aliases = {3: 0}
    else:
        kernel = _merge_kernel
        out_shape = jax.ShapeDtypeStruct((ext, width), jnp.bfloat16)
        out_spec = b_spec
    return pl.pallas_call(
        kernel,
        out_shape=out_shape,
        grid_spec=pltpu.PrefetchScalarGridSpec(
            num_scalar_prefetch=1,
            grid=(groups,),
            in_specs=in_specs,
            out_specs=out_spec,
            scratch_shapes=[pltpu.VMEM((128, rows), jnp.float32)]
            + ([] if final else [pltpu.VMEM((EXTRA, lanes), jnp.float32)]),
        ),
        input_output_aliases=aliases,
        cost_estimate=pl.CostEstimate(
            flops=4 * rows * width, transcendentals=0, bytes_accessed=3 * rows * width * 2
        ),
    )(*operands)


def _stack_kernel(k_ref, v_ref, o_ref):
    o_ref[0] = k_ref[...]
    o_ref[1] = v_ref[...]


def stack_kv(k, v):
    rows, width = k.shape
    lanes = width // 2
    spec = pl.BlockSpec((rows, lanes), lambda g: (0, g))
    return pl.pallas_call(
        _stack_kernel,
        out_shape=jax.ShapeDtypeStruct((2, rows, width), k.dtype),
        grid=(2,),
        in_specs=[spec, spec],
        out_specs=pl.BlockSpec((2, rows, lanes), lambda g: (0, 0, g)),
        cost_estimate=pl.CostEstimate(flops=0, transcendentals=0, bytes_accessed=4 * rows * width * 2),
    )(k, v)


def shift_tm(x, by):
    size = lax.axis_size("tm")
    pairs = [(i, i + by) for i in range(size) if 0 <= i + by < size]
    return lax.ppermute(x, "tm", pairs)


def on_device(query_states, key_states, value_states, history, neighbours):
    _, rows, width = query_states.shape
    seg = lax.axis_index("tm")
    tile = lax.axis_index("space")
    tiles = lax.axis_size("space")
    q = query_states[0]
    k = key_states[0]
    v = value_states[0]
    tile_l = tile > 0
    tile_r = tile < tiles - 1

    def flags_for(m, d):
        m = m.astype(jnp.int32)
        return jnp.stack(
            [
                ((m[1] == 1) & tile_l).astype(jnp.int32),
                (m[0] >= d).astype(jnp.int32),
                ((m[2] == 1) & tile_r).astype(jnp.int32),
            ]
        )

    meta = jnp.concatenate([history.reshape(1), neighbours.reshape(2)]).astype(jnp.bfloat16)
    chunk_w = width // CHUNKS
    groups_c = chunk_w // HEAD_DIM // HG
    meta_rows = jnp.zeros((EXTRA, chunk_w), jnp.bfloat16).at[0, 0:3].set(meta)
    sends = [jnp.concatenate([q[:, :chunk_w], meta_rows], axis=0)]
    sends += [q[:, c * chunk_w : (c + 1) * chunk_w] for c in range(1, CHUNKS)]
    q1s = [shift_tm(x, -1) for x in sends]

    kv = stack_kv(k, v)
    kv_l = lax.ppermute(kv, "space", [(i, i + 1) for i in range(tiles - 1)])
    kv_r = lax.ppermute(kv, "space", [(i + 1, i) for i in range(tiles - 1)])

    f1 = flags_for(q1s[0][rows, 0:3], 1)
    p1s, q2s = [], []
    for c in range(CHUNKS):
        p1s.append(attend(f1, q1s[c], k, v, kv_l, kv_r, chunk_w, c * groups_c, 0))
        relay = q1s[c]
        if c > 0:
            relay, p1s[0], p1s[c] = lax.optimization_barrier((relay, p1s[0], p1s[c]))
        q2s.append(shift_tm(relay, -1))

    valid = (seg >= 1).astype(jnp.int32).reshape(1)
    f0 = flags_for(meta, 0)
    f2 = flags_for(q2s[0][rows, 0:3], 2)
    result = None
    q_self = q
    for c in range(CHUNKS):
        base = c * groups_c
        p_self = attend(f0, q_self, k, v, kv_l, kv_r, chunk_w, base, base)
        q2, p_self = lax.optimization_barrier((q2s[c], p_self))
        p2 = attend(f2, q2, k, v, kv_l, kv_r, chunk_w, base, 0)
        q_self, p2 = lax.optimization_barrier((q, p2))
        p2_in = shift_tm(p2, 1)
        pc = merge(valid, p1s[c], p2_in, 0)
        pc_in = shift_tm(pc, 1)
        result = merge(valid, p_self, pc_in, base, final=True, buf=result, out_width=width)
    return result.reshape(1, rows, width)


def solution(mesh):
    placed = (
        P("tm", "space", None),
        P("tm", "space", None),
        P("tm", "space", None),
        P("tm"),
        P("tm", "space", None),
    )
    return jax.shard_map(
        on_device, mesh=mesh, in_specs=placed, out_specs=P("tm", "space", None), check_vma=False
    )
```

```python
import jax
import jax.numpy as jnp
from jax import lax
from jax.experimental import pallas as pl
from jax.experimental.pallas import tpu as pltpu
from jax.sharding import PartitionSpec as P

HEAD_DIM = 128
HG = 5
CHUNKS = 2
NEG = -1e30
EXTRA = 16


def _store_stats(o_ref, st_ref, t, hg, rows):
    top, den = t[0:hg], t[hg : 2 * hg]
    top_hi = top.astype(jnp.bfloat16).astype(jnp.float32)
    rest = top - top_hi
    top_mid = rest.astype(jnp.bfloat16).astype(jnp.float32)
    den_hi = den.astype(jnp.bfloat16).astype(jnp.float32)
    st_ref[...] = jnp.zeros_like(st_ref)
    st_ref[0:hg, 0:rows] = top_hi
    st_ref[0:hg, rows : 2 * rows] = top_mid
    st_ref[2 * hg : 3 * hg, 0:rows] = rest - top_mid
    st_ref[hg : 2 * hg, 0:rows] = den_hi
    st_ref[hg : 2 * hg, rows : 2 * rows] = den - den_hi
    o_ref[rows : rows + EXTRA, :] = st_ref[...].astype(o_ref.dtype)


def _load_stats(ref, hg, rows):
    block = ref[rows : rows + EXTRA, :].astype(jnp.float32)
    top = block[0:hg, 0:rows] + block[0:hg, rows : 2 * rows] + block[2 * hg : 3 * hg, 0:rows]
    den = block[hg : 2 * hg, 0:rows] + block[hg : 2 * hg, rows : 2 * rows]
    return top, den


def _attn_kernel(flags_ref, q_ref, kl_ref, kc_ref, kr_ref, vl_ref, vc_ref, vr_ref, o_ref, col_ref, st_ref):
    hg = q_ref.shape[1] // HEAD_DIM
    rows = q_ref.shape[0]
    lanes = o_ref.shape[1]
    inv_root = 1.0 / HEAD_DIM**0.5
    seg_ok = flags_ref[1] == 1

    @pl.when(seg_ok)
    def _():
        bias_l = jnp.where(flags_ref[0] == 1, 0.0, NEG).astype(jnp.float32)
        bias_r = jnp.where(flags_ref[2] == 1, 0.0, NEG).astype(jnp.float32)
        col_ref[...] = jnp.zeros_like(col_ref)
        for h in range(hg):
            cols = slice(h * HEAD_DIM, (h + 1) * HEAD_DIM)
            q = q_ref[:, cols]

            def scores(k_ref):
                return (
                    lax.dot_general(
                        q, k_ref[:, cols], (((1,), (1,)), ((), ())), preferred_element_type=jnp.float32
                    )
                    * inv_root
                )

            s_l = scores(kl_ref) + bias_l
            s_c = scores(kc_ref)
            s_r = scores(kr_ref) + bias_r
            top = jnp.maximum(
                jnp.maximum(s_l.max(axis=1, keepdims=True), s_c.max(axis=1, keepdims=True)),
                s_r.max(axis=1, keepdims=True),
            )
            shift = top
            p_l = jnp.exp(s_l - shift)
            p_c = jnp.exp(s_c - shift)
            p_r = jnp.exp(s_r - shift)
            denom = (
                p_l.sum(axis=1, keepdims=True) + p_c.sum(axis=1, keepdims=True) + p_r.sum(axis=1, keepdims=True)
            )
            acc = jnp.dot(p_l.astype(jnp.bfloat16), vl_ref[:, cols], preferred_element_type=jnp.float32)
            acc += jnp.dot(p_c.astype(jnp.bfloat16), vc_ref[:, cols], preferred_element_type=jnp.float32)
            acc += jnp.dot(p_r.astype(jnp.bfloat16), vr_ref[:, cols], preferred_element_type=jnp.float32)
            o_ref[0:rows, cols] = (acc / denom).astype(o_ref.dtype)
            col_ref[:, h : h + 1] = shift
            col_ref[:, hg + h : hg + h + 1] = denom
        _store_stats(o_ref, st_ref, jnp.transpose(col_ref[...]), hg, rows)

    @pl.when(jnp.logical_not(seg_ok))
    def _():
        row = lax.broadcasted_iota(jnp.int32, o_ref.shape, 0)
        lane = lax.broadcasted_iota(jnp.int32, o_ref.shape, 1)
        empty = (row >= rows) & (row < rows + hg) & (lane < rows)
        o_ref[...] = jnp.where(empty, NEG, 0.0).astype(o_ref.dtype)


def attend(flags, q, k, v, kv_l, kv_r, width, base, q_base):
    rows = k.shape[0]
    heads = width // HEAD_DIM
    groups = heads // HG
    lanes = HG * HEAD_DIM
    q_spec = pl.BlockSpec((rows, lanes), lambda g, f: (0, g + q_base))
    kv_spec = pl.BlockSpec((rows, lanes), lambda g, f: (0, g + base))
    side_k = pl.BlockSpec((None, rows, lanes), lambda g, f: (0, 0, g + base))
    side_v = pl.BlockSpec((None, rows, lanes), lambda g, f: (1, 0, g + base))
    return pl.pallas_call(
        _attn_kernel,
        out_shape=jax.ShapeDtypeStruct((rows + EXTRA, width), jnp.bfloat16),
        grid_spec=pltpu.PrefetchScalarGridSpec(
            num_scalar_prefetch=1,
            grid=(groups,),
            in_specs=[q_spec, side_k, kv_spec, side_k, side_v, kv_spec, side_v],
            out_specs=pl.BlockSpec((rows + EXTRA, lanes), lambda g, f: (0, g)),
            scratch_shapes=[pltpu.VMEM((rows, 128), jnp.float32), pltpu.VMEM((EXTRA, lanes), jnp.float32)],
        ),
        cost_estimate=pl.CostEstimate(
            flops=4 * rows * 3 * rows * HEAD_DIM * heads,
            transcendentals=rows * 3 * rows * heads,
            bytes_accessed=2 * rows * width * 2 + 6 * rows * width * 2,
        ),
    )(flags, q, kv_l, k, kv_r, kv_l, v, kv_r)


def _merge_weights(valid_ref, a_ref, b_ref, wt_ref):
    rows = wt_ref.shape[1]
    hg = a_ref.shape[1] // HEAD_DIM
    a_top, a_den = _load_stats(a_ref, hg, rows)
    ok = valid_ref[0] == 1
    b_top, b_den = _load_stats(b_ref, hg, rows)
    b_top = jnp.where(ok, b_top, NEG)
    b_den = jnp.where(ok, b_den, 0.0)
    top = jnp.maximum(a_top, b_top)
    a_w = jnp.exp(a_top - top) * a_den
    b_w = jnp.exp(b_top - top) * b_den
    total = a_w + b_w
    safe = jnp.where(total > 0.0, total, 1.0)
    wt_ref[0:hg, :] = a_w / safe
    wt_ref[8 : 8 + hg, :] = b_w / safe
    return top, total, jnp.transpose(wt_ref[...])


def _merge_body(a_ref, b_ref, o_ref, w, hg, rows):
    for h in range(hg):
        cols = slice(h * HEAD_DIM, (h + 1) * HEAD_DIM)
        o = a_ref[0:rows, cols].astype(jnp.float32) * w[:, h : h + 1]
        o = o + b_ref[0:rows, cols].astype(jnp.float32) * w[:, 8 + h : 9 + h]
        o_ref[0:rows, cols] = o.astype(o_ref.dtype)


def _merge_kernel(valid_ref, a_ref, b_ref, o_ref, wt_ref, st_ref):
    rows = wt_ref.shape[1]
    hg = o_ref.shape[1] // HEAD_DIM
    top, total, w = _merge_weights(valid_ref, a_ref, b_ref, wt_ref)
    _merge_body(a_ref, b_ref, o_ref, w, hg, rows)
    wt_ref[0:hg, :] = top
    wt_ref[hg : 2 * hg, :] = total
    _store_stats(o_ref, st_ref, wt_ref[...], hg, rows)


def _final_kernel(valid_ref, a_ref, b_ref, *rest):
    o_ref, wt_ref = rest[-2], rest[-1]
    rows = wt_ref.shape[1]
    _, _, w = _merge_weights(valid_ref, a_ref, b_ref, wt_ref)
    _merge_body(a_ref, b_ref, o_ref, w, o_ref.shape[1] // HEAD_DIM, rows)


def merge(valid, a, b, base, final=False, buf=None, out_width=None):
    ext, width = b.shape
    rows = ext - EXTRA
    groups = width // HEAD_DIM // HG
    lanes = HG * HEAD_DIM
    a_base = 0 if out_width is not None else base
    a_spec = pl.BlockSpec((ext, lanes), lambda g, v: (0, g + a_base))
    b_spec = pl.BlockSpec((ext, lanes), lambda g, v: (0, g))
    in_specs = [a_spec, b_spec]
    operands = [valid, a, b]
    aliases = {}
    if final:
        kernel = _final_kernel
        out_shape = jax.ShapeDtypeStruct((rows, out_width or a.shape[1]), jnp.bfloat16)
        out_spec = pl.BlockSpec((rows, lanes), lambda g, v: (0, g + base))
        if buf is not None:
            in_specs.append(pl.BlockSpec(memory_space=pl.ANY))
            operands.append(buf)
            aliases = {3: 0}
    else:
        kernel = _merge_kernel
        out_shape = jax.ShapeDtypeStruct((ext, width), jnp.bfloat16)
        out_spec = b_spec
    return pl.pallas_call(
        kernel,
        out_shape=out_shape,
        grid_spec=pltpu.PrefetchScalarGridSpec(
            num_scalar_prefetch=1,
            grid=(groups,),
            in_specs=in_specs,
            out_specs=out_spec,
            scratch_shapes=[pltpu.VMEM((128, rows), jnp.float32)]
            + ([] if final else [pltpu.VMEM((EXTRA, lanes), jnp.float32)]),
        ),
        input_output_aliases=aliases,
        cost_estimate=pl.CostEstimate(
            flops=4 * rows * width, transcendentals=0, bytes_accessed=3 * rows * width * 2
        ),
    )(*operands)


def shift_tm(x, by):
    size = lax.axis_size("tm")
    pairs = [(i, i + by) for i in range(size) if 0 <= i + by < size]
    return lax.ppermute(x, "tm", pairs)


def on_device(query_states, key_states, value_states, history, neighbours):
    _, rows, width = query_states.shape
    seg = lax.axis_index("tm")
    tile = lax.axis_index("space")
    tiles = lax.axis_size("space")
    q = query_states[0]
    k = key_states[0]
    v = value_states[0]
    tile_l = tile > 0
    tile_r = tile < tiles - 1

    def flags_for(m, d):
        m = m.astype(jnp.int32)
        return jnp.stack(
            [
                ((m[1] == 1) & tile_l).astype(jnp.int32),
                (m[0] >= d).astype(jnp.int32),
                ((m[2] == 1) & tile_r).astype(jnp.int32),
            ]
        )

    meta = jnp.concatenate([history.reshape(1), neighbours.reshape(2)]).astype(jnp.bfloat16)
    chunk_w = width // CHUNKS
    groups_c = chunk_w // HEAD_DIM // HG
    meta_rows = jnp.zeros((EXTRA, chunk_w), jnp.bfloat16).at[0, 0:3].set(meta)
    sends = [jnp.concatenate([q[:, :chunk_w], meta_rows], axis=0)]
    sends += [q[:, c * chunk_w : (c + 1) * chunk_w] for c in range(1, CHUNKS)]
    q1s = [shift_tm(x, -1) for x in sends]

    kv = jnp.stack([k, v])
    kv_l = lax.ppermute(kv, "space", [(i, i + 1) for i in range(tiles - 1)])
    kv_r = lax.ppermute(kv, "space", [(i + 1, i) for i in range(tiles - 1)])

    f1 = flags_for(q1s[0][rows, 0:3], 1)
    p1s, q2s = [], []
    for c in range(CHUNKS):
        p1s.append(attend(f1, q1s[c], k, v, kv_l, kv_r, chunk_w, c * groups_c, 0))
        relay = q1s[c]
        if c > 0:
            relay, p1s[0], p1s[c] = lax.optimization_barrier((relay, p1s[0], p1s[c]))
        q2s.append(shift_tm(relay, -1))

    valid = (seg >= 1).astype(jnp.int32).reshape(1)
    f0 = flags_for(meta, 0)
    f2 = flags_for(q2s[0][rows, 0:3], 2)
    p2s = [attend(f2, q2s[c], k, v, kv_l, kv_r, chunk_w, c * groups_c, 0) for c in range(CHUNKS)]
    p2_ins = [shift_tm(p2, 1) for p2 in p2s]
    after = p2s[-1]
    result = None
    for c in range(CHUNKS):
        base = c * groups_c
        q_self, _ = lax.optimization_barrier((q, after))
        p_self = attend(f0, q_self, k, v, kv_l, kv_r, chunk_w, base, base)
        p2_in, p_self = lax.optimization_barrier((p2_ins[c], p_self))
        pc = merge(valid, p1s[c], p2_in, 0)
        after = pc
        pc_in = shift_tm(pc, 1)
        result = merge(valid, p_self, pc_in, base, final=True, buf=result, out_width=width)
    return result.reshape(1, rows, width)


def solution(mesh):
    placed = (
        P("tm", "space", None),
        P("tm", "space", None),
        P("tm", "space", None),
        P("tm"),
        P("tm", "space", None),
    )
    return jax.shard_map(
        on_device, mesh=mesh, in_specs=placed, out_specs=P("tm", "space", None), check_vma=False
    )
```

```python
import jax
import jax.numpy as jnp
from jax import lax
from jax.experimental import pallas as pl
from jax.experimental.pallas import tpu as pltpu
from jax.sharding import PartitionSpec as P

HEAD_DIM = 128
HG = 5
CHUNKS = 2
NEG = -1e30
EXTRA = 16


def _store_stats(o_ref, st_ref, t, hg, rows):
    top, den = t[0:hg], t[hg : 2 * hg]
    top_hi = top.astype(jnp.bfloat16).astype(jnp.float32)
    rest = top - top_hi
    top_mid = rest.astype(jnp.bfloat16).astype(jnp.float32)
    den_hi = den.astype(jnp.bfloat16).astype(jnp.float32)
    st_ref[...] = jnp.zeros_like(st_ref)
    st_ref[0:hg, 0:rows] = top_hi
    st_ref[0:hg, rows : 2 * rows] = top_mid
    st_ref[2 * hg : 3 * hg, 0:rows] = rest - top_mid
    st_ref[hg : 2 * hg, 0:rows] = den_hi
    st_ref[hg : 2 * hg, rows : 2 * rows] = den - den_hi
    o_ref[rows : rows + EXTRA, :] = st_ref[...].astype(o_ref.dtype)


def _load_stats(ref, hg, rows):
    block = ref[rows : rows + EXTRA, :].astype(jnp.float32)
    top = block[0:hg, 0:rows] + block[0:hg, rows : 2 * rows] + block[2 * hg : 3 * hg, 0:rows]
    den = block[hg : 2 * hg, 0:rows] + block[hg : 2 * hg, rows : 2 * rows]
    return top, den


def _attn_kernel(flags_ref, q_ref, kl_ref, kc_ref, kr_ref, vl_ref, vc_ref, vr_ref, o_ref, col_ref, st_ref):
    hg = q_ref.shape[1] // HEAD_DIM
    rows = q_ref.shape[0]
    lanes = o_ref.shape[1]
    inv_root = 1.0 / HEAD_DIM**0.5
    seg_ok = flags_ref[1] == 1

    @pl.when(seg_ok)
    def _():
        bias_l = jnp.where(flags_ref[0] == 1, 0.0, NEG).astype(jnp.float32)
        bias_r = jnp.where(flags_ref[2] == 1, 0.0, NEG).astype(jnp.float32)
        col_ref[...] = jnp.zeros_like(col_ref)
        for h in range(hg):
            cols = slice(h * HEAD_DIM, (h + 1) * HEAD_DIM)
            q = q_ref[:, cols]

            def scores(k_ref):
                return (
                    lax.dot_general(
                        q, k_ref[:, cols], (((1,), (1,)), ((), ())), preferred_element_type=jnp.float32
                    )
                    * inv_root
                )

            s_l = scores(kl_ref) + bias_l
            s_c = scores(kc_ref)
            s_r = scores(kr_ref) + bias_r
            top = jnp.maximum(
                jnp.maximum(s_l.max(axis=1, keepdims=True), s_c.max(axis=1, keepdims=True)),
                s_r.max(axis=1, keepdims=True),
            )
            shift = top
            p_l = jnp.exp(s_l - shift)
            p_c = jnp.exp(s_c - shift)
            p_r = jnp.exp(s_r - shift)
            denom = (
                p_l.sum(axis=1, keepdims=True) + p_c.sum(axis=1, keepdims=True) + p_r.sum(axis=1, keepdims=True)
            )
            acc = jnp.dot(p_l.astype(jnp.bfloat16), vl_ref[:, cols], preferred_element_type=jnp.float32)
            acc += jnp.dot(p_c.astype(jnp.bfloat16), vc_ref[:, cols], preferred_element_type=jnp.float32)
            acc += jnp.dot(p_r.astype(jnp.bfloat16), vr_ref[:, cols], preferred_element_type=jnp.float32)
            o_ref[0:rows, cols] = (acc / denom).astype(o_ref.dtype)
            col_ref[:, h : h + 1] = shift
            col_ref[:, hg + h : hg + h + 1] = denom
        _store_stats(o_ref, st_ref, jnp.transpose(col_ref[...]), hg, rows)

    @pl.when(jnp.logical_not(seg_ok))
    def _():
        row = lax.broadcasted_iota(jnp.int32, o_ref.shape, 0)
        lane = lax.broadcasted_iota(jnp.int32, o_ref.shape, 1)
        empty = (row >= rows) & (row < rows + hg) & (lane < rows)
        o_ref[...] = jnp.where(empty, NEG, 0.0).astype(o_ref.dtype)


def attend(flags, q, k, v, kv_l, kv_r, width, base, q_base):
    rows = k.shape[0]
    heads = width // HEAD_DIM
    groups = heads // HG
    lanes = HG * HEAD_DIM
    q_spec = pl.BlockSpec((rows, lanes), lambda g, f: (0, g + q_base))
    kv_spec = pl.BlockSpec((rows, lanes), lambda g, f: (0, g + base))
    side_k = pl.BlockSpec((None, rows, lanes), lambda g, f: (0, 0, g + base))
    side_v = pl.BlockSpec((None, rows, lanes), lambda g, f: (1, 0, g + base))
    return pl.pallas_call(
        _attn_kernel,
        out_shape=jax.ShapeDtypeStruct((rows + EXTRA, width), jnp.bfloat16),
        grid_spec=pltpu.PrefetchScalarGridSpec(
            num_scalar_prefetch=1,
            grid=(groups,),
            in_specs=[q_spec, side_k, kv_spec, side_k, side_v, kv_spec, side_v],
            out_specs=pl.BlockSpec((rows + EXTRA, lanes), lambda g, f: (0, g)),
            scratch_shapes=[pltpu.VMEM((rows, 128), jnp.float32), pltpu.VMEM((EXTRA, lanes), jnp.float32)],
        ),
        cost_estimate=pl.CostEstimate(
            flops=4 * rows * 3 * rows * HEAD_DIM * heads,
            transcendentals=rows * 3 * rows * heads,
            bytes_accessed=2 * rows * width * 2 + 6 * rows * width * 2,
        ),
    )(flags, q, kv_l, k, kv_r, kv_l, v, kv_r)


def _merge_weights(valid_ref, a_ref, b_ref, wt_ref):
    rows = wt_ref.shape[1]
    hg = a_ref.shape[1] // HEAD_DIM
    a_top, a_den = _load_stats(a_ref, hg, rows)
    ok = valid_ref[0] == 1
    b_top, b_den = _load_stats(b_ref, hg, rows)
    b_top = jnp.where(ok, b_top, NEG)
    b_den = jnp.where(ok, b_den, 0.0)
    top = jnp.maximum(a_top, b_top)
    a_w = jnp.exp(a_top - top) * a_den
    b_w = jnp.exp(b_top - top) * b_den
    total = a_w + b_w
    safe = jnp.where(total > 0.0, total, 1.0)
    wt_ref[0:hg, :] = a_w / safe
    wt_ref[8 : 8 + hg, :] = b_w / safe
    return top, total, jnp.transpose(wt_ref[...])


def _merge_body(a_ref, b_ref, o_ref, w, hg, rows):
    for h in range(hg):
        cols = slice(h * HEAD_DIM, (h + 1) * HEAD_DIM)
        o = a_ref[0:rows, cols].astype(jnp.float32) * w[:, h : h + 1]
        o = o + b_ref[0:rows, cols].astype(jnp.float32) * w[:, 8 + h : 9 + h]
        o_ref[0:rows, cols] = o.astype(o_ref.dtype)


def _merge_kernel(valid_ref, a_ref, b_ref, o_ref, wt_ref, st_ref):
    rows = wt_ref.shape[1]
    hg = o_ref.shape[1] // HEAD_DIM
    top, total, w = _merge_weights(valid_ref, a_ref, b_ref, wt_ref)
    _merge_body(a_ref, b_ref, o_ref, w, hg, rows)
    wt_ref[0:hg, :] = top
    wt_ref[hg : 2 * hg, :] = total
    _store_stats(o_ref, st_ref, wt_ref[...], hg, rows)


def _final_kernel(valid_ref, a_ref, b_ref, *rest):
    o_ref, wt_ref = rest[-2], rest[-1]
    rows = wt_ref.shape[1]
    _, _, w = _merge_weights(valid_ref, a_ref, b_ref, wt_ref)
    _merge_body(a_ref, b_ref, o_ref, w, o_ref.shape[1] // HEAD_DIM, rows)


def merge(valid, a, b, base, final=False, buf=None, out_width=None):
    ext, width = b.shape
    rows = ext - EXTRA
    groups = width // HEAD_DIM // HG
    lanes = HG * HEAD_DIM
    a_base = 0 if out_width is not None else base
    a_spec = pl.BlockSpec((ext, lanes), lambda g, v: (0, g + a_base))
    b_spec = pl.BlockSpec((ext, lanes), lambda g, v: (0, g))
    in_specs = [a_spec, b_spec]
    operands = [valid, a, b]
    aliases = {}
    if final:
        kernel = _final_kernel
        out_shape = jax.ShapeDtypeStruct((rows, out_width or a.shape[1]), jnp.bfloat16)
        out_spec = pl.BlockSpec((rows, lanes), lambda g, v: (0, g + base))
        if buf is not None:
            in_specs.append(pl.BlockSpec(memory_space=pl.ANY))
            operands.append(buf)
            aliases = {3: 0}
    else:
        kernel = _merge_kernel
        out_shape = jax.ShapeDtypeStruct((ext, width), jnp.bfloat16)
        out_spec = b_spec
    return pl.pallas_call(
        kernel,
        out_shape=out_shape,
        grid_spec=pltpu.PrefetchScalarGridSpec(
            num_scalar_prefetch=1,
            grid=(groups,),
            in_specs=in_specs,
            out_specs=out_spec,
            scratch_shapes=[pltpu.VMEM((128, rows), jnp.float32)]
            + ([] if final else [pltpu.VMEM((EXTRA, lanes), jnp.float32)]),
        ),
        input_output_aliases=aliases,
        cost_estimate=pl.CostEstimate(
            flops=4 * rows * width, transcendentals=0, bytes_accessed=3 * rows * width * 2
        ),
    )(*operands)


def shift_tm(x, by):
    size = lax.axis_size("tm")
    pairs = [(i, i + by) for i in range(size) if 0 <= i + by < size]
    return lax.ppermute(x, "tm", pairs)


def on_device(query_states, key_states, value_states, history, neighbours):
    _, rows, width = query_states.shape
    seg = lax.axis_index("tm")
    tile = lax.axis_index("space")
    tiles = lax.axis_size("space")
    q = query_states[0]
    k = key_states[0]
    v = value_states[0]
    tile_l = tile > 0
    tile_r = tile < tiles - 1

    def flags_for(m, d):
        m = m.astype(jnp.int32)
        return jnp.stack(
            [
                ((m[1] == 1) & tile_l).astype(jnp.int32),
                (m[0] >= d).astype(jnp.int32),
                ((m[2] == 1) & tile_r).astype(jnp.int32),
            ]
        )

    meta = jnp.concatenate([history.reshape(1), neighbours.reshape(2)]).astype(jnp.bfloat16)
    chunk_w = width // CHUNKS
    groups_c = chunk_w // HEAD_DIM // HG
    meta_rows = jnp.zeros((EXTRA, chunk_w), jnp.bfloat16).at[0, 0:3].set(meta)
    sends = [jnp.concatenate([q[:, :chunk_w], meta_rows], axis=0)]
    sends += [q[:, c * chunk_w : (c + 1) * chunk_w] for c in range(1, CHUNKS)]
    q1s = [shift_tm(x, -1) for x in sends]

    kv = jnp.stack([k, v])
    kv_l = lax.ppermute(kv, "space", [(i, i + 1) for i in range(tiles - 1)])
    kv_r = lax.ppermute(kv, "space", [(i + 1, i) for i in range(tiles - 1)])

    f1 = flags_for(q1s[0][rows, 0:3], 1)
    p1s, q2s = [], []
    for c in range(CHUNKS):
        p1s.append(attend(f1, q1s[c], k, v, kv_l, kv_r, chunk_w, c * groups_c, 0))
        relay = q1s[c]
        if c > 0:
            relay, p1s[0], p1s[c] = lax.optimization_barrier((relay, p1s[0], p1s[c]))
        q2s.append(shift_tm(relay, -1))

    valid = (seg >= 1).astype(jnp.int32).reshape(1)
    f0 = flags_for(meta, 0)
    f2 = flags_for(q2s[0][rows, 0:3], 2)
    p2s = [attend(f2, q2s[c], k, v, kv_l, kv_r, chunk_w, c * groups_c, 0) for c in range(CHUNKS)]
    p2_ins = [shift_tm(p2, 1) for p2 in p2s]
    result = None
    p_self = None
    for c in range(CHUNKS):
        base = c * groups_c
        p2_in = p2_ins[c]
        if p_self is not None:
            p2_in, p_self = lax.optimization_barrier((p2_in, p_self))
            result = merge(valid, p_self, pcs_in, base - groups_c, final=True, buf=result, out_width=width)
        pc = merge(valid, p1s[c], p2_in, 0)
        pcs_in = shift_tm(pc, 1)
        q_self, _ = lax.optimization_barrier((q, pc))
        p_self = attend(f0, q_self, k, v, kv_l, kv_r, chunk_w, base, base)
    result = merge(valid, p_self, pcs_in, (CHUNKS - 1) * groups_c, final=True, buf=result, out_width=width)
    return result.reshape(1, rows, width)


def solution(mesh):
    placed = (
        P("tm", "space", None),
        P("tm", "space", None),
        P("tm", "space", None),
        P("tm"),
        P("tm", "space", None),
    )
    return jax.shard_map(
        on_device, mesh=mesh, in_specs=placed, out_specs=P("tm", "space", None), check_vma=False
    )
```

```python
import jax
import jax.numpy as jnp
from jax import lax
from jax.experimental import pallas as pl
from jax.experimental.pallas import tpu as pltpu
from jax.sharding import PartitionSpec as P

HEAD_DIM = 128
HG = 5
CHUNKS = 2
NEG = -1e30
EXTRA = 16


def _store_stats(o_ref, st_ref, t, hg, rows):
    top, den = t[0:hg], t[hg : 2 * hg]
    top_hi = top.astype(jnp.bfloat16).astype(jnp.float32)
    rest = top - top_hi
    top_mid = rest.astype(jnp.bfloat16).astype(jnp.float32)
    den_hi = den.astype(jnp.bfloat16).astype(jnp.float32)
    st_ref[...] = jnp.zeros_like(st_ref)
    st_ref[0:hg, 0:rows] = top_hi
    st_ref[0:hg, rows : 2 * rows] = top_mid
    st_ref[2 * hg : 3 * hg, 0:rows] = rest - top_mid
    st_ref[hg : 2 * hg, 0:rows] = den_hi
    st_ref[hg : 2 * hg, rows : 2 * rows] = den - den_hi
    o_ref[rows : rows + EXTRA, :] = st_ref[...].astype(o_ref.dtype)


def _load_stats(ref, hg, rows):
    block = ref[rows : rows + EXTRA, :].astype(jnp.float32)
    top = block[0:hg, 0:rows] + block[0:hg, rows : 2 * rows] + block[2 * hg : 3 * hg, 0:rows]
    den = block[hg : 2 * hg, 0:rows] + block[hg : 2 * hg, rows : 2 * rows]
    return top, den


def _attn_kernel(flags_ref, q_ref, kl_ref, kc_ref, kr_ref, vl_ref, vc_ref, vr_ref, o_ref, col_ref, st_ref):
    hg = q_ref.shape[1] // HEAD_DIM
    rows = q_ref.shape[0]
    lanes = o_ref.shape[1]
    inv_root = 1.0 / HEAD_DIM**0.5
    seg_ok = flags_ref[1] == 1

    @pl.when(seg_ok)
    def _():
        bias_l = jnp.where(flags_ref[0] == 1, 0.0, NEG).astype(jnp.float32)
        bias_r = jnp.where(flags_ref[2] == 1, 0.0, NEG).astype(jnp.float32)
        col_ref[...] = jnp.zeros_like(col_ref)
        for h in range(hg):
            cols = slice(h * HEAD_DIM, (h + 1) * HEAD_DIM)
            q = q_ref[:, cols]

            def scores(k_ref):
                return (
                    lax.dot_general(
                        q, k_ref[:, cols], (((1,), (1,)), ((), ())), preferred_element_type=jnp.float32
                    )
                    * inv_root
                )

            s_l = scores(kl_ref) + bias_l
            s_c = scores(kc_ref)
            s_r = scores(kr_ref) + bias_r
            top = jnp.maximum(
                jnp.maximum(s_l.max(axis=1, keepdims=True), s_c.max(axis=1, keepdims=True)),
                s_r.max(axis=1, keepdims=True),
            )
            shift = top
            p_l = jnp.exp(s_l - shift)
            p_c = jnp.exp(s_c - shift)
            p_r = jnp.exp(s_r - shift)
            denom = (
                p_l.sum(axis=1, keepdims=True) + p_c.sum(axis=1, keepdims=True) + p_r.sum(axis=1, keepdims=True)
            )
            acc = jnp.dot(p_l.astype(jnp.bfloat16), vl_ref[:, cols], preferred_element_type=jnp.float32)
            acc += jnp.dot(p_c.astype(jnp.bfloat16), vc_ref[:, cols], preferred_element_type=jnp.float32)
            acc += jnp.dot(p_r.astype(jnp.bfloat16), vr_ref[:, cols], preferred_element_type=jnp.float32)
            o_ref[0:rows, cols] = (acc / denom).astype(o_ref.dtype)
            col_ref[:, h : h + 1] = shift
            col_ref[:, hg + h : hg + h + 1] = denom
        _store_stats(o_ref, st_ref, jnp.transpose(col_ref[...]), hg, rows)

    @pl.when(jnp.logical_not(seg_ok))
    def _():
        row = lax.broadcasted_iota(jnp.int32, o_ref.shape, 0)
        lane = lax.broadcasted_iota(jnp.int32, o_ref.shape, 1)
        empty = (row >= rows) & (row < rows + hg) & (lane < rows)
        o_ref[...] = jnp.where(empty, NEG, 0.0).astype(o_ref.dtype)


def attend(flags, q, k, v, kv_l, kv_r, width, base, q_base):
    rows = k.shape[0]
    heads = width // HEAD_DIM
    groups = heads // HG
    lanes = HG * HEAD_DIM
    q_spec = pl.BlockSpec((rows, lanes), lambda g, f: (0, g + q_base))
    kv_spec = pl.BlockSpec((rows, lanes), lambda g, f: (0, g + base))
    side_k = pl.BlockSpec((None, rows, lanes), lambda g, f: (0, 0, g + base))
    side_v = pl.BlockSpec((None, rows, lanes), lambda g, f: (1, 0, g + base))
    return pl.pallas_call(
        _attn_kernel,
        out_shape=jax.ShapeDtypeStruct((rows + EXTRA, width), jnp.bfloat16),
        grid_spec=pltpu.PrefetchScalarGridSpec(
            num_scalar_prefetch=1,
            grid=(groups,),
            in_specs=[q_spec, side_k, kv_spec, side_k, side_v, kv_spec, side_v],
            out_specs=pl.BlockSpec((rows + EXTRA, lanes), lambda g, f: (0, g)),
            scratch_shapes=[pltpu.VMEM((rows, 128), jnp.float32), pltpu.VMEM((EXTRA, lanes), jnp.float32)],
        ),
        cost_estimate=pl.CostEstimate(
            flops=4 * rows * 3 * rows * HEAD_DIM * heads,
            transcendentals=rows * 3 * rows * heads,
            bytes_accessed=2 * rows * width * 2 + 6 * rows * width * 2,
        ),
    )(flags, q, kv_l, k, kv_r, kv_l, v, kv_r)


def _merge_weights(valid_ref, a_ref, b_ref, wt_ref):
    rows = wt_ref.shape[1]
    hg = a_ref.shape[1] // HEAD_DIM
    a_top, a_den = _load_stats(a_ref, hg, rows)
    ok = valid_ref[0] == 1
    b_top, b_den = _load_stats(b_ref, hg, rows)
    b_top = jnp.where(ok, b_top, NEG)
    b_den = jnp.where(ok, b_den, 0.0)
    top = jnp.maximum(a_top, b_top)
    a_w = jnp.exp(a_top - top) * a_den
    b_w = jnp.exp(b_top - top) * b_den
    total = a_w + b_w
    safe = jnp.where(total > 0.0, total, 1.0)
    wt_ref[0:hg, :] = a_w / safe
    wt_ref[8 : 8 + hg, :] = b_w / safe
    return top, total, jnp.transpose(wt_ref[...])


def _merge_body(a_ref, b_ref, o_ref, w, hg, rows):
    for h in range(hg):
        cols = slice(h * HEAD_DIM, (h + 1) * HEAD_DIM)
        o = a_ref[0:rows, cols].astype(jnp.float32) * w[:, h : h + 1]
        o = o + b_ref[0:rows, cols].astype(jnp.float32) * w[:, 8 + h : 9 + h]
        o_ref[0:rows, cols] = o.astype(o_ref.dtype)


def _merge_kernel(valid_ref, a_ref, b_ref, o_ref, wt_ref, st_ref):
    rows = wt_ref.shape[1]
    hg = o_ref.shape[1] // HEAD_DIM
    top, total, w = _merge_weights(valid_ref, a_ref, b_ref, wt_ref)
    _merge_body(a_ref, b_ref, o_ref, w, hg, rows)
    wt_ref[0:hg, :] = top
    wt_ref[hg : 2 * hg, :] = total
    _store_stats(o_ref, st_ref, wt_ref[...], hg, rows)


def _final_kernel(valid_ref, a_ref, b_ref, *rest):
    o_ref, wt_ref = rest[-2], rest[-1]
    rows = wt_ref.shape[1]
    _, _, w = _merge_weights(valid_ref, a_ref, b_ref, wt_ref)
    _merge_body(a_ref, b_ref, o_ref, w, o_ref.shape[1] // HEAD_DIM, rows)


def merge(valid, a, b, base, final=False, buf=None, out_width=None):
    ext, width = b.shape
    rows = ext - EXTRA
    groups = width // HEAD_DIM // HG
    lanes = HG * HEAD_DIM
    a_base = 0 if out_width is not None else base
    a_spec = pl.BlockSpec((ext, lanes), lambda g, v: (0, g + a_base))
    b_spec = pl.BlockSpec((ext, lanes), lambda g, v: (0, g))
    in_specs = [a_spec, b_spec]
    operands = [valid, a, b]
    aliases = {}
    if final:
        kernel = _final_kernel
        out_shape = jax.ShapeDtypeStruct((rows, out_width or a.shape[1]), jnp.bfloat16)
        out_spec = pl.BlockSpec((rows, lanes), lambda g, v: (0, g + base))
        if buf is not None:
            in_specs.append(pl.BlockSpec(memory_space=pl.ANY))
            operands.append(buf)
            aliases = {3: 0}
    else:
        kernel = _merge_kernel
        out_shape = jax.ShapeDtypeStruct((ext, width), jnp.bfloat16)
        out_spec = b_spec
    return pl.pallas_call(
        kernel,
        out_shape=out_shape,
        grid_spec=pltpu.PrefetchScalarGridSpec(
            num_scalar_prefetch=1,
            grid=(groups,),
            in_specs=in_specs,
            out_specs=out_spec,
            scratch_shapes=[pltpu.VMEM((128, rows), jnp.float32)]
            + ([] if final else [pltpu.VMEM((EXTRA, lanes), jnp.float32)]),
        ),
        input_output_aliases=aliases,
        cost_estimate=pl.CostEstimate(
            flops=4 * rows * width, transcendentals=0, bytes_accessed=3 * rows * width * 2
        ),
    )(*operands)


def shift_tm(x, by):
    size = lax.axis_size("tm")
    pairs = [(i, i + by) for i in range(size) if 0 <= i + by < size]
    return lax.ppermute(x, "tm", pairs)


def on_device(query_states, key_states, value_states, history, neighbours):
    _, rows, width = query_states.shape
    seg = lax.axis_index("tm")
    tile = lax.axis_index("space")
    tiles = lax.axis_size("space")
    q = query_states[0]
    k = key_states[0]
    v = value_states[0]
    tile_l = tile > 0
    tile_r = tile < tiles - 1

    def flags_for(m, d):
        m = m.astype(jnp.int32)
        return jnp.stack(
            [
                ((m[1] == 1) & tile_l).astype(jnp.int32),
                (m[0] >= d).astype(jnp.int32),
                ((m[2] == 1) & tile_r).astype(jnp.int32),
            ]
        )

    meta = jnp.concatenate([history.reshape(1), neighbours.reshape(2)]).astype(jnp.bfloat16)
    chunk_w = width // CHUNKS
    groups_c = chunk_w // HEAD_DIM // HG
    meta_rows = jnp.zeros((EXTRA, chunk_w), jnp.bfloat16).at[0, 0:3].set(meta)
    sends = [jnp.concatenate([q[:, :chunk_w], meta_rows], axis=0)]
    sends += [q[:, c * chunk_w : (c + 1) * chunk_w] for c in range(1, CHUNKS)]
    q1s = [shift_tm(x, -1) for x in sends]

    kv = jnp.stack([k, v])
    kv_l = lax.ppermute(kv, "space", [(i, i + 1) for i in range(tiles - 1)])
    kv_r = lax.ppermute(kv, "space", [(i + 1, i) for i in range(tiles - 1)])

    f1 = flags_for(q1s[0][rows, 0:3], 1)
    p1s, q2s = [], []
    for c in range(CHUNKS):
        p1s.append(attend(f1, q1s[c], k, v, kv_l, kv_r, chunk_w, c * groups_c, 0))
        relay = q1s[c]
        if c > 0:
            relay, p1s[0], p1s[c] = lax.optimization_barrier((relay, p1s[0], p1s[c]))
        q2s.append(shift_tm(relay, -1))

    valid = (seg >= 1).astype(jnp.int32).reshape(1)
    f0 = flags_for(meta, 0)
    f2 = flags_for(q2s[0][rows, 0:3], 2)
    p2s = [attend(f2, q2s[c], k, v, kv_l, kv_r, chunk_w, c * groups_c, 0) for c in range(CHUNKS)]
    p2_ins = [shift_tm(p2, 1) for p2 in p2s]
    result = None
    for c in range(CHUNKS):
        base = c * groups_c
        pc = merge(valid, p1s[c], p2_ins[c], 0)
        pc_in = shift_tm(pc, 1)
        q_self, _ = lax.optimization_barrier((q, pc))
        p_self = attend(f0, q_self, k, v, kv_l, kv_r, chunk_w, base, base)
        result = merge(valid, p_self, pc_in, base, final=True, buf=result, out_width=width)
    return result.reshape(1, rows, width)


def solution(mesh):
    placed = (
        P("tm", "space", None),
        P("tm", "space", None),
        P("tm", "space", None),
        P("tm"),
        P("tm", "space", None),
    )
    return jax.shard_map(
        on_device, mesh=mesh, in_specs=placed, out_specs=P("tm", "space", None), check_vma=False
    )
```

```python
import jax
import jax.numpy as jnp
from jax import lax
from jax.experimental import pallas as pl
from jax.experimental.pallas import tpu as pltpu
from jax.sharding import PartitionSpec as P

HEAD_DIM = 128
HG = 5
CHUNKS = 2
NEG = -1e30
EXTRA = 16


def _store_stats(o_ref, st_ref, t, hg, rows):
    top, den = t[0:hg], t[hg : 2 * hg]
    top_hi = top.astype(jnp.bfloat16).astype(jnp.float32)
    rest = top - top_hi
    top_mid = rest.astype(jnp.bfloat16).astype(jnp.float32)
    den_hi = den.astype(jnp.bfloat16).astype(jnp.float32)
    st_ref[...] = jnp.zeros_like(st_ref)
    st_ref[0:hg, 0:rows] = top_hi
    st_ref[0:hg, rows : 2 * rows] = top_mid
    st_ref[2 * hg : 3 * hg, 0:rows] = rest - top_mid
    st_ref[hg : 2 * hg, 0:rows] = den_hi
    st_ref[hg : 2 * hg, rows : 2 * rows] = den - den_hi
    o_ref[rows : rows + EXTRA, :] = st_ref[...].astype(o_ref.dtype)


def _load_stats(ref, hg, rows):
    block = ref[rows : rows + EXTRA, :].astype(jnp.float32)
    top = block[0:hg, 0:rows] + block[0:hg, rows : 2 * rows] + block[2 * hg : 3 * hg, 0:rows]
    den = block[hg : 2 * hg, 0:rows] + block[hg : 2 * hg, rows : 2 * rows]
    return top, den


def _attn_kernel(flags_ref, q_ref, kl_ref, kc_ref, kr_ref, vl_ref, vc_ref, vr_ref, o_ref, col_ref, st_ref):
    hg = q_ref.shape[1] // HEAD_DIM
    rows = q_ref.shape[0]
    lanes = o_ref.shape[1]
    inv_root = 1.0 / HEAD_DIM**0.5
    seg_ok = flags_ref[1] == 1

    @pl.when(seg_ok)
    def _():
        bias_l = jnp.where(flags_ref[0] == 1, 0.0, NEG).astype(jnp.float32)
        bias_r = jnp.where(flags_ref[2] == 1, 0.0, NEG).astype(jnp.float32)
        col_ref[...] = jnp.zeros_like(col_ref)
        for h in range(hg):
            cols = slice(h * HEAD_DIM, (h + 1) * HEAD_DIM)
            q = q_ref[:, cols]

            def scores(k_ref):
                return (
                    lax.dot_general(
                        q, k_ref[:, cols], (((1,), (1,)), ((), ())), preferred_element_type=jnp.float32
                    )
                    * inv_root
                )

            s_l = scores(kl_ref) + bias_l
            s_c = scores(kc_ref)
            s_r = scores(kr_ref) + bias_r
            top = jnp.maximum(
                jnp.maximum(s_l.max(axis=1, keepdims=True), s_c.max(axis=1, keepdims=True)),
                s_r.max(axis=1, keepdims=True),
            )
            shift = top
            p_l = jnp.exp(s_l - shift)
            p_c = jnp.exp(s_c - shift)
            p_r = jnp.exp(s_r - shift)
            denom = (
                p_l.sum(axis=1, keepdims=True) + p_c.sum(axis=1, keepdims=True) + p_r.sum(axis=1, keepdims=True)
            )
            acc = jnp.dot(p_l.astype(jnp.bfloat16), vl_ref[:, cols], preferred_element_type=jnp.float32)
            acc += jnp.dot(p_c.astype(jnp.bfloat16), vc_ref[:, cols], preferred_element_type=jnp.float32)
            acc += jnp.dot(p_r.astype(jnp.bfloat16), vr_ref[:, cols], preferred_element_type=jnp.float32)
            o_ref[0:rows, cols] = (acc / denom).astype(o_ref.dtype)
            col_ref[:, h : h + 1] = shift
            col_ref[:, hg + h : hg + h + 1] = denom
        _store_stats(o_ref, st_ref, jnp.transpose(col_ref[...]), hg, rows)

    @pl.when(jnp.logical_not(seg_ok))
    def _():
        row = lax.broadcasted_iota(jnp.int32, o_ref.shape, 0)
        lane = lax.broadcasted_iota(jnp.int32, o_ref.shape, 1)
        empty = (row >= rows) & (row < rows + hg) & (lane < rows)
        o_ref[...] = jnp.where(empty, NEG, 0.0).astype(o_ref.dtype)


def attend(flags, q, k, v, kv_l, kv_r, width, base, q_base):
    rows = k.shape[0]
    heads = width // HEAD_DIM
    groups = heads // HG
    lanes = HG * HEAD_DIM
    q_spec = pl.BlockSpec((rows, lanes), lambda g, f: (0, g + q_base))
    kv_spec = pl.BlockSpec((rows, lanes), lambda g, f: (0, g + base))
    side_k = pl.BlockSpec((None, rows, lanes), lambda g, f: (0, 0, g + base))
    side_v = pl.BlockSpec((None, rows, lanes), lambda g, f: (1, 0, g + base))
    return pl.pallas_call(
        _attn_kernel,
        out_shape=jax.ShapeDtypeStruct((rows + EXTRA, width), jnp.bfloat16),
        grid_spec=pltpu.PrefetchScalarGridSpec(
            num_scalar_prefetch=1,
            grid=(groups,),
            in_specs=[q_spec, side_k, kv_spec, side_k, side_v, kv_spec, side_v],
            out_specs=pl.BlockSpec((rows + EXTRA, lanes), lambda g, f: (0, g)),
            scratch_shapes=[pltpu.VMEM((rows, 128), jnp.float32), pltpu.VMEM((EXTRA, lanes), jnp.float32)],
        ),
        cost_estimate=pl.CostEstimate(
            flops=4 * rows * 3 * rows * HEAD_DIM * heads,
            transcendentals=rows * 3 * rows * heads,
            bytes_accessed=2 * rows * width * 2 + 6 * rows * width * 2,
        ),
    )(flags, q, kv_l, k, kv_r, kv_l, v, kv_r)


def _merge_weights(valid_ref, a_ref, b_ref, wt_ref):
    rows = wt_ref.shape[1]
    hg = a_ref.shape[1] // HEAD_DIM
    a_top, a_den = _load_stats(a_ref, hg, rows)
    ok = valid_ref[0] == 1
    b_top, b_den = _load_stats(b_ref, hg, rows)
    b_top = jnp.where(ok, b_top, NEG)
    b_den = jnp.where(ok, b_den, 0.0)
    top = jnp.maximum(a_top, b_top)
    a_w = jnp.exp(a_top - top) * a_den
    b_w = jnp.exp(b_top - top) * b_den
    total = a_w + b_w
    safe = jnp.where(total > 0.0, total, 1.0)
    wt_ref[0:hg, :] = a_w / safe
    wt_ref[8 : 8 + hg, :] = b_w / safe
    return top, total, jnp.transpose(wt_ref[...])


def _merge_body(a_ref, b_ref, o_ref, w, hg, rows):
    for h in range(hg):
        cols = slice(h * HEAD_DIM, (h + 1) * HEAD_DIM)
        o = a_ref[0:rows, cols].astype(jnp.float32) * w[:, h : h + 1]
        o = o + b_ref[0:rows, cols].astype(jnp.float32) * w[:, 8 + h : 9 + h]
        o_ref[0:rows, cols] = o.astype(o_ref.dtype)


def _merge_kernel(valid_ref, a_ref, b_ref, o_ref, wt_ref, st_ref):
    rows = wt_ref.shape[1]
    hg = o_ref.shape[1] // HEAD_DIM
    top, total, w = _merge_weights(valid_ref, a_ref, b_ref, wt_ref)
    _merge_body(a_ref, b_ref, o_ref, w, hg, rows)
    wt_ref[0:hg, :] = top
    wt_ref[hg : 2 * hg, :] = total
    _store_stats(o_ref, st_ref, wt_ref[...], hg, rows)


def _final_kernel(valid_ref, a_ref, b_ref, *rest):
    o_ref, wt_ref = rest[-2], rest[-1]
    rows = wt_ref.shape[1]
    _, _, w = _merge_weights(valid_ref, a_ref, b_ref, wt_ref)
    _merge_body(a_ref, b_ref, o_ref, w, o_ref.shape[1] // HEAD_DIM, rows)


def merge(valid, a, b, base, final=False, buf=None, out_width=None):
    ext, width = b.shape
    rows = ext - EXTRA
    groups = width // HEAD_DIM // HG
    lanes = HG * HEAD_DIM
    a_base = 0 if out_width is not None else base
    a_spec = pl.BlockSpec((ext, lanes), lambda g, v: (0, g + a_base))
    b_spec = pl.BlockSpec((ext, lanes), lambda g, v: (0, g))
    in_specs = [a_spec, b_spec]
    operands = [valid, a, b]
    aliases = {}
    if final:
        kernel = _final_kernel
        out_shape = jax.ShapeDtypeStruct((rows, out_width or a.shape[1]), jnp.bfloat16)
        out_spec = pl.BlockSpec((rows, lanes), lambda g, v: (0, g + base))
        if buf is not None:
            in_specs.append(pl.BlockSpec(memory_space=pl.ANY))
            operands.append(buf)
            aliases = {3: 0}
    else:
        kernel = _merge_kernel
        out_shape = jax.ShapeDtypeStruct((ext, width), jnp.bfloat16)
        out_spec = b_spec
    return pl.pallas_call(
        kernel,
        out_shape=out_shape,
        grid_spec=pltpu.PrefetchScalarGridSpec(
            num_scalar_prefetch=1,
            grid=(groups,),
            in_specs=in_specs,
            out_specs=out_spec,
            scratch_shapes=[pltpu.VMEM((128, rows), jnp.float32)]
            + ([] if final else [pltpu.VMEM((EXTRA, lanes), jnp.float32)]),
        ),
        input_output_aliases=aliases,
        cost_estimate=pl.CostEstimate(
            flops=4 * rows * width, transcendentals=0, bytes_accessed=3 * rows * width * 2
        ),
    )(*operands)


def shift_tm(x, by):
    size = lax.axis_size("tm")
    pairs = [(i, i + by) for i in range(size) if 0 <= i + by < size]
    return lax.ppermute(x, "tm", pairs)


def on_device(query_states, key_states, value_states, history, neighbours):
    _, rows, width = query_states.shape
    seg = lax.axis_index("tm")
    tile = lax.axis_index("space")
    tiles = lax.axis_size("space")
    q = query_states[0]
    k = key_states[0]
    v = value_states[0]
    tile_l = tile > 0
    tile_r = tile < tiles - 1

    def flags_for(m, d):
        m = m.astype(jnp.int32)
        return jnp.stack(
            [
                ((m[1] == 1) & tile_l).astype(jnp.int32),
                (m[0] >= d).astype(jnp.int32),
                ((m[2] == 1) & tile_r).astype(jnp.int32),
            ]
        )

    meta = jnp.concatenate([history.reshape(1), neighbours.reshape(2)]).astype(jnp.bfloat16)
    chunk_w = width // CHUNKS
    groups_c = chunk_w // HEAD_DIM // HG
    meta_rows = jnp.zeros((EXTRA, chunk_w), jnp.bfloat16).at[0, 0:3].set(meta)
    sends = [jnp.concatenate([q[:, :chunk_w], meta_rows], axis=0)]
    sends += [q[:, c * chunk_w : (c + 1) * chunk_w] for c in range(1, CHUNKS)]
    q1s = [shift_tm(x, -1) for x in sends]

    kv = jnp.stack([k, v])
    kv_l = lax.ppermute(kv, "space", [(i, i + 1) for i in range(tiles - 1)])
    kv_r = lax.ppermute(kv, "space", [(i + 1, i) for i in range(tiles - 1)])

    f1 = flags_for(q1s[0][rows, 0:3], 1)
    p1s, q2s = [], []
    for c in range(CHUNKS):
        p1s.append(attend(f1, q1s[c], k, v, kv_l, kv_r, chunk_w, c * groups_c, 0))
        relay = q1s[c]
        if c > 0:
            relay, p1s[0] = lax.optimization_barrier((relay, p1s[0]))
        q2s.append(shift_tm(relay, -1))

    valid = (seg >= 1).astype(jnp.int32).reshape(1)
    f0 = flags_for(meta, 0)
    f2 = flags_for(q2s[0][rows, 0:3], 2)
    q2s[0], p1s[1] = lax.optimization_barrier((q2s[0], p1s[1]))
    p2s = [attend(f2, q2s[c], k, v, kv_l, kv_r, chunk_w, c * groups_c, 0) for c in range(CHUNKS)]
    p2_ins = [shift_tm(p2, 1) for p2 in p2s]
    result = None
    p_self = None
    for c in range(CHUNKS):
        base = c * groups_c
        p2_in = p2_ins[c]
        if p_self is not None:
            p2_in, p_self = lax.optimization_barrier((p2_in, p_self))
            result = merge(valid, p_self, pcs_in, base - groups_c, final=True, buf=result, out_width=width)
        pc = merge(valid, p1s[c], p2_in, 0)
        pcs_in = shift_tm(pc, 1)
        q_self, _ = lax.optimization_barrier((q, pc))
        p_self = attend(f0, q_self, k, v, kv_l, kv_r, chunk_w, base, base)
    result = merge(valid, p_self, pcs_in, (CHUNKS - 1) * groups_c, final=True, buf=result, out_width=width)
    return result.reshape(1, rows, width)


def solution(mesh):
    placed = (
        P("tm", "space", None),
        P("tm", "space", None),
        P("tm", "space", None),
        P("tm"),
        P("tm", "space", None),
    )
    return jax.shard_map(
        on_device, mesh=mesh, in_specs=placed, out_specs=P("tm", "space", None), check_vma=False
    )
```

```python
import jax
import jax.numpy as jnp
from jax import lax
from jax.experimental import pallas as pl
from jax.experimental.pallas import tpu as pltpu
from jax.sharding import PartitionSpec as P

HEAD_DIM = 128
HG = 5
CHUNKS = 2
NEG = -1e30
EXTRA = 16


def _store_stats(o_ref, st_ref, t, hg, rows):
    top, den = t[0:hg], t[hg : 2 * hg]
    top_hi = top.astype(jnp.bfloat16).astype(jnp.float32)
    rest = top - top_hi
    top_mid = rest.astype(jnp.bfloat16).astype(jnp.float32)
    den_hi = den.astype(jnp.bfloat16).astype(jnp.float32)
    st_ref[...] = jnp.zeros_like(st_ref)
    st_ref[0:hg, 0:rows] = top_hi
    st_ref[0:hg, rows : 2 * rows] = top_mid
    st_ref[2 * hg : 3 * hg, 0:rows] = rest - top_mid
    st_ref[hg : 2 * hg, 0:rows] = den_hi
    st_ref[hg : 2 * hg, rows : 2 * rows] = den - den_hi
    o_ref[rows : rows + EXTRA, :] = st_ref[...].astype(o_ref.dtype)


def _load_stats(ref, hg, rows):
    block = ref[rows : rows + EXTRA, :].astype(jnp.float32)
    top = block[0:hg, 0:rows] + block[0:hg, rows : 2 * rows] + block[2 * hg : 3 * hg, 0:rows]
    den = block[hg : 2 * hg, 0:rows] + block[hg : 2 * hg, rows : 2 * rows]
    return top, den


def _attn_kernel(flags_ref, q_ref, kl_ref, kc_ref, kr_ref, vl_ref, vc_ref, vr_ref, o_ref, col_ref, st_ref):
    hg = q_ref.shape[1] // HEAD_DIM
    rows = q_ref.shape[0]
    lanes = o_ref.shape[1]
    inv_root = 1.0 / HEAD_DIM**0.5
    seg_ok = flags_ref[1] == 1

    @pl.when(seg_ok)
    def _():
        bias_l = jnp.where(flags_ref[0] == 1, 0.0, NEG).astype(jnp.float32)
        bias_r = jnp.where(flags_ref[2] == 1, 0.0, NEG).astype(jnp.float32)
        col_ref[...] = jnp.zeros_like(col_ref)
        for h in range(hg):
            cols = slice(h * HEAD_DIM, (h + 1) * HEAD_DIM)
            q = q_ref[:, cols]

            def scores(k_ref):
                return (
                    lax.dot_general(
                        q, k_ref[:, cols], (((1,), (1,)), ((), ())), preferred_element_type=jnp.float32
                    )
                    * inv_root
                )

            s_l = scores(kl_ref) + bias_l
            s_c = scores(kc_ref)
            s_r = scores(kr_ref) + bias_r
            top = jnp.maximum(
                jnp.maximum(s_l.max(axis=1, keepdims=True), s_c.max(axis=1, keepdims=True)),
                s_r.max(axis=1, keepdims=True),
            )
            shift = top
            p_l = jnp.exp(s_l - shift)
            p_c = jnp.exp(s_c - shift)
            p_r = jnp.exp(s_r - shift)
            denom = (
                p_l.sum(axis=1, keepdims=True) + p_c.sum(axis=1, keepdims=True) + p_r.sum(axis=1, keepdims=True)
            )
            acc = jnp.dot(p_l.astype(jnp.bfloat16), vl_ref[:, cols], preferred_element_type=jnp.float32)
            acc += jnp.dot(p_c.astype(jnp.bfloat16), vc_ref[:, cols], preferred_element_type=jnp.float32)
            acc += jnp.dot(p_r.astype(jnp.bfloat16), vr_ref[:, cols], preferred_element_type=jnp.float32)
            o_ref[0:rows, cols] = (acc / denom).astype(o_ref.dtype)
            col_ref[:, h : h + 1] = shift
            col_ref[:, hg + h : hg + h + 1] = denom
        _store_stats(o_ref, st_ref, jnp.transpose(col_ref[...]), hg, rows)

    @pl.when(jnp.logical_not(seg_ok))
    def _():
        row = lax.broadcasted_iota(jnp.int32, o_ref.shape, 0)
        lane = lax.broadcasted_iota(jnp.int32, o_ref.shape, 1)
        empty = (row >= rows) & (row < rows + hg) & (lane < rows)
        o_ref[...] = jnp.where(empty, NEG, 0.0).astype(o_ref.dtype)


def attend(flags, q, k, v, kv_l, kv_r, width, base, q_base):
    rows = k.shape[0]
    heads = width // HEAD_DIM
    groups = heads // HG
    lanes = HG * HEAD_DIM
    q_spec = pl.BlockSpec((rows, lanes), lambda g, f: (0, g + q_base))
    kv_spec = pl.BlockSpec((rows, lanes), lambda g, f: (0, g + base))
    side_k = kv_spec
    side_v = kv_spec
    return pl.pallas_call(
        _attn_kernel,
        out_shape=jax.ShapeDtypeStruct((rows + EXTRA, width), jnp.bfloat16),
        grid_spec=pltpu.PrefetchScalarGridSpec(
            num_scalar_prefetch=1,
            grid=(groups,),
            in_specs=[q_spec, side_k, kv_spec, side_k, side_v, kv_spec, side_v],
            out_specs=pl.BlockSpec((rows + EXTRA, lanes), lambda g, f: (0, g)),
            scratch_shapes=[pltpu.VMEM((rows, 128), jnp.float32), pltpu.VMEM((EXTRA, lanes), jnp.float32)],
        ),
        cost_estimate=pl.CostEstimate(
            flops=4 * rows * 3 * rows * HEAD_DIM * heads,
            transcendentals=rows * 3 * rows * heads,
            bytes_accessed=2 * rows * width * 2 + 6 * rows * width * 2,
        ),
    )(flags, q, kv_l[0], k, kv_r[0], kv_l[1], v, kv_r[1])


def _merge_weights(valid_ref, a_ref, b_ref, wt_ref):
    rows = wt_ref.shape[1]
    hg = a_ref.shape[1] // HEAD_DIM
    a_top, a_den = _load_stats(a_ref, hg, rows)
    ok = valid_ref[0] == 1
    b_top, b_den = _load_stats(b_ref, hg, rows)
    b_top = jnp.where(ok, b_top, NEG)
    b_den = jnp.where(ok, b_den, 0.0)
    top = jnp.maximum(a_top, b_top)
    a_w = jnp.exp(a_top - top) * a_den
    b_w = jnp.exp(b_top - top) * b_den
    total = a_w + b_w
    safe = jnp.where(total > 0.0, total, 1.0)
    wt_ref[0:hg, :] = a_w / safe
    wt_ref[8 : 8 + hg, :] = b_w / safe
    return top, total, jnp.transpose(wt_ref[...])


def _merge_body(a_ref, b_ref, o_ref, w, hg, rows):
    for h in range(hg):
        cols = slice(h * HEAD_DIM, (h + 1) * HEAD_DIM)
        o = a_ref[0:rows, cols].astype(jnp.float32) * w[:, h : h + 1]
        o = o + b_ref[0:rows, cols].astype(jnp.float32) * w[:, 8 + h : 9 + h]
        o_ref[0:rows, cols] = o.astype(o_ref.dtype)


def _merge_kernel(valid_ref, a_ref, b_ref, o_ref, wt_ref, st_ref):
    rows = wt_ref.shape[1]
    hg = o_ref.shape[1] // HEAD_DIM
    top, total, w = _merge_weights(valid_ref, a_ref, b_ref, wt_ref)
    _merge_body(a_ref, b_ref, o_ref, w, hg, rows)
    wt_ref[0:hg, :] = top
    wt_ref[hg : 2 * hg, :] = total
    _store_stats(o_ref, st_ref, wt_ref[...], hg, rows)


def _final_kernel(valid_ref, a_ref, b_ref, *rest):
    o_ref, wt_ref = rest[-2], rest[-1]
    rows = wt_ref.shape[1]
    _, _, w = _merge_weights(valid_ref, a_ref, b_ref, wt_ref)
    _merge_body(a_ref, b_ref, o_ref, w, o_ref.shape[1] // HEAD_DIM, rows)


def merge(valid, a, b, base, final=False, buf=None, out_width=None):
    ext, width = b.shape
    rows = ext - EXTRA
    groups = width // HEAD_DIM // HG
    lanes = HG * HEAD_DIM
    a_base = 0 if out_width is not None else base
    a_spec = pl.BlockSpec((ext, lanes), lambda g, v: (0, g + a_base))
    b_spec = pl.BlockSpec((ext, lanes), lambda g, v: (0, g))
    in_specs = [a_spec, b_spec]
    operands = [valid, a, b]
    aliases = {}
    if final:
        kernel = _final_kernel
        out_shape = jax.ShapeDtypeStruct((rows, out_width or a.shape[1]), jnp.bfloat16)
        out_spec = pl.BlockSpec((rows, lanes), lambda g, v: (0, g + base))
        if buf is not None:
            in_specs.append(pl.BlockSpec(memory_space=pl.ANY))
            operands.append(buf)
            aliases = {3: 0}
    else:
        kernel = _merge_kernel
        out_shape = jax.ShapeDtypeStruct((ext, width), jnp.bfloat16)
        out_spec = b_spec
    return pl.pallas_call(
        kernel,
        out_shape=out_shape,
        grid_spec=pltpu.PrefetchScalarGridSpec(
            num_scalar_prefetch=1,
            grid=(groups,),
            in_specs=in_specs,
            out_specs=out_spec,
            scratch_shapes=[pltpu.VMEM((128, rows), jnp.float32)]
            + ([] if final else [pltpu.VMEM((EXTRA, lanes), jnp.float32)]),
        ),
        input_output_aliases=aliases,
        cost_estimate=pl.CostEstimate(
            flops=4 * rows * width, transcendentals=0, bytes_accessed=3 * rows * width * 2
        ),
    )(*operands)


def shift_tm(x, by):
    size = lax.axis_size("tm")
    pairs = [(i, i + by) for i in range(size) if 0 <= i + by < size]
    return lax.ppermute(x, "tm", pairs)


def on_device(query_states, key_states, value_states, history, neighbours):
    _, rows, width = query_states.shape
    seg = lax.axis_index("tm")
    tile = lax.axis_index("space")
    tiles = lax.axis_size("space")
    q = query_states[0]
    k = key_states[0]
    v = value_states[0]
    tile_l = tile > 0
    tile_r = tile < tiles - 1

    def flags_for(m, d):
        m = m.astype(jnp.int32)
        return jnp.stack(
            [
                ((m[1] == 1) & tile_l).astype(jnp.int32),
                (m[0] >= d).astype(jnp.int32),
                ((m[2] == 1) & tile_r).astype(jnp.int32),
            ]
        )

    meta = jnp.concatenate([history.reshape(1), neighbours.reshape(2)]).astype(jnp.bfloat16)
    chunk_w = width // CHUNKS
    groups_c = chunk_w // HEAD_DIM // HG
    meta_rows = jnp.zeros((EXTRA, width), jnp.bfloat16).at[0, 0:3].set(meta)
    q1_all = shift_tm(jnp.concatenate([q, meta_rows], axis=0), -1)

    kl, vl = lax.ppermute((k, v), "space", [(i, i + 1) for i in range(tiles - 1)])
    kr, vr = lax.ppermute((k, v), "space", [(i + 1, i) for i in range(tiles - 1)])
    kv_l, kv_r = (kl, vl), (kr, vr)

    f1 = flags_for(q1_all[rows, 0:3], 1)
    p1s, q2s = [], []
    for c in range(CHUNKS):
        p1s.append(attend(f1, q1_all, k, v, kv_l, kv_r, chunk_w, c * groups_c, c * groups_c))
        relay = q1_all[:, c * chunk_w : (c + 1) * chunk_w]
        if c > 0:
            relay, p1s[0], p1s[c] = lax.optimization_barrier((relay, p1s[0], p1s[c]))
        q2s.append(shift_tm(relay, -1))

    valid = (seg >= 1).astype(jnp.int32).reshape(1)
    f0 = flags_for(meta, 0)
    f2 = flags_for(q2s[0][rows, 0:3], 2)
    p2s = [attend(f2, q2s[c], k, v, kv_l, kv_r, chunk_w, c * groups_c, 0) for c in range(CHUNKS)]
    p2_ins = [shift_tm(p2, 1) for p2 in p2s]
    result = None
    p_self = None
    for c in range(CHUNKS):
        base = c * groups_c
        p2_in = p2_ins[c]
        if p_self is not None:
            p2_in, p_self = lax.optimization_barrier((p2_in, p_self))
            result = merge(valid, p_self, pcs_in, base - groups_c, final=True, buf=result, out_width=width)
        pc = merge(valid, p1s[c], p2_in, 0)
        pcs_in = shift_tm(pc, 1)
        q_self, _ = lax.optimization_barrier((q, pc))
        p_self = attend(f0, q_self, k, v, kv_l, kv_r, chunk_w, base, base)
    result = merge(valid, p_self, pcs_in, (CHUNKS - 1) * groups_c, final=True, buf=result, out_width=width)
    return result.reshape(1, rows, width)


def solution(mesh):
    placed = (
        P("tm", "space", None),
        P("tm", "space", None),
        P("tm", "space", None),
        P("tm"),
        P("tm", "space", None),
    )
    return jax.shard_map(
        on_device, mesh=mesh, in_specs=placed, out_specs=P("tm", "space", None), check_vma=False
    )
```

```python
import jax
import jax.numpy as jnp
from jax import lax
from jax.experimental import pallas as pl
from jax.experimental.pallas import tpu as pltpu
from jax.sharding import PartitionSpec as P

HEAD_DIM = 128
HG = 5
CHUNKS = 2
NEG = -1e30
EXTRA = 16


def _store_stats(o_ref, st_ref, t, hg, rows):
    top, den = t[0:hg], t[hg : 2 * hg]
    top_hi = top.astype(jnp.bfloat16).astype(jnp.float32)
    rest = top - top_hi
    top_mid = rest.astype(jnp.bfloat16).astype(jnp.float32)
    den_hi = den.astype(jnp.bfloat16).astype(jnp.float32)
    st_ref[...] = jnp.zeros_like(st_ref)
    st_ref[0:hg, 0:rows] = top_hi
    st_ref[0:hg, rows : 2 * rows] = top_mid
    st_ref[2 * hg : 3 * hg, 0:rows] = rest - top_mid
    st_ref[hg : 2 * hg, 0:rows] = den_hi
    st_ref[hg : 2 * hg, rows : 2 * rows] = den - den_hi
    o_ref[rows : rows + EXTRA, :] = st_ref[...].astype(o_ref.dtype)


def _load_stats(ref, hg, rows):
    block = ref[rows : rows + EXTRA, :].astype(jnp.float32)
    top = block[0:hg, 0:rows] + block[0:hg, rows : 2 * rows] + block[2 * hg : 3 * hg, 0:rows]
    den = block[hg : 2 * hg, 0:rows] + block[hg : 2 * hg, rows : 2 * rows]
    return top, den


def _attn_kernel(flags_ref, q_ref, kl_ref, kc_ref, kr_ref, vl_ref, vc_ref, vr_ref, o_ref, col_ref, st_ref):
    hg = q_ref.shape[1] // HEAD_DIM
    rows = q_ref.shape[0]
    lanes = o_ref.shape[1]
    inv_root = 1.0 / HEAD_DIM**0.5
    seg_ok = flags_ref[1] == 1

    @pl.when(seg_ok)
    def _():
        bias_l = jnp.where(flags_ref[0] == 1, 0.0, NEG).astype(jnp.float32)
        bias_r = jnp.where(flags_ref[2] == 1, 0.0, NEG).astype(jnp.float32)
        col_ref[...] = jnp.zeros_like(col_ref)
        for h in range(hg):
            cols = slice(h * HEAD_DIM, (h + 1) * HEAD_DIM)
            q = q_ref[:, cols]

            def scores(k_ref):
                return (
                    lax.dot_general(
                        q, k_ref[:, cols], (((1,), (1,)), ((), ())), preferred_element_type=jnp.float32
                    )
                    * inv_root
                )

            s_l = scores(kl_ref) + bias_l
            s_c = scores(kc_ref)
            s_r = scores(kr_ref) + bias_r
            top = jnp.maximum(
                jnp.maximum(s_l.max(axis=1, keepdims=True), s_c.max(axis=1, keepdims=True)),
                s_r.max(axis=1, keepdims=True),
            )
            shift = top
            p_l = jnp.exp(s_l - shift)
            p_c = jnp.exp(s_c - shift)
            p_r = jnp.exp(s_r - shift)
            denom = (
                p_l.sum(axis=1, keepdims=True) + p_c.sum(axis=1, keepdims=True) + p_r.sum(axis=1, keepdims=True)
            )
            acc = jnp.dot(p_l.astype(jnp.bfloat16), vl_ref[:, cols], preferred_element_type=jnp.float32)
            acc += jnp.dot(p_c.astype(jnp.bfloat16), vc_ref[:, cols], preferred_element_type=jnp.float32)
            acc += jnp.dot(p_r.astype(jnp.bfloat16), vr_ref[:, cols], preferred_element_type=jnp.float32)
            o_ref[0:rows, cols] = (acc / denom).astype(o_ref.dtype)
            col_ref[:, h : h + 1] = shift
            col_ref[:, hg + h : hg + h + 1] = denom
        _store_stats(o_ref, st_ref, jnp.transpose(col_ref[...]), hg, rows)

    @pl.when(jnp.logical_not(seg_ok))
    def _():
        row = lax.broadcasted_iota(jnp.int32, o_ref.shape, 0)
        lane = lax.broadcasted_iota(jnp.int32, o_ref.shape, 1)
        empty = (row >= rows) & (row < rows + hg) & (lane < rows)
        o_ref[...] = jnp.where(empty, NEG, 0.0).astype(o_ref.dtype)


def attend(flags, q, k, v, kv_l, kv_r, width, base, q_base, side_base=None):
    rows = k.shape[0]
    heads = width // HEAD_DIM
    groups = heads // HG
    lanes = HG * HEAD_DIM
    q_spec = pl.BlockSpec((rows, lanes), lambda g, f: (0, g + q_base))
    kv_spec = pl.BlockSpec((rows, lanes), lambda g, f: (0, g + base))
    sb = base if side_base is None else side_base
    side_k = pl.BlockSpec((None, rows, lanes), lambda g, f: (0, 0, g + sb))
    side_v = pl.BlockSpec((None, rows, lanes), lambda g, f: (1, 0, g + sb))
    return pl.pallas_call(
        _attn_kernel,
        out_shape=jax.ShapeDtypeStruct((rows + EXTRA, width), jnp.bfloat16),
        grid_spec=pltpu.PrefetchScalarGridSpec(
            num_scalar_prefetch=1,
            grid=(groups,),
            in_specs=[q_spec, side_k, kv_spec, side_k, side_v, kv_spec, side_v],
            out_specs=pl.BlockSpec((rows + EXTRA, lanes), lambda g, f: (0, g)),
            scratch_shapes=[pltpu.VMEM((rows, 128), jnp.float32), pltpu.VMEM((EXTRA, lanes), jnp.float32)],
        ),
        cost_estimate=pl.CostEstimate(
            flops=4 * rows * 3 * rows * HEAD_DIM * heads,
            transcendentals=rows * 3 * rows * heads,
            bytes_accessed=2 * rows * width * 2 + 6 * rows * width * 2,
        ),
    )(flags, q, kv_l, k, kv_r, kv_l, v, kv_r)


def _merge_weights(valid_ref, a_ref, b_ref, wt_ref):
    rows = wt_ref.shape[1]
    hg = a_ref.shape[1] // HEAD_DIM
    a_top, a_den = _load_stats(a_ref, hg, rows)
    ok = valid_ref[0] == 1
    b_top, b_den = _load_stats(b_ref, hg, rows)
    b_top = jnp.where(ok, b_top, NEG)
    b_den = jnp.where(ok, b_den, 0.0)
    top = jnp.maximum(a_top, b_top)
    a_w = jnp.exp(a_top - top) * a_den
    b_w = jnp.exp(b_top - top) * b_den
    total = a_w + b_w
    safe = jnp.where(total > 0.0, total, 1.0)
    wt_ref[0:hg, :] = a_w / safe
    wt_ref[8 : 8 + hg, :] = b_w / safe
    return top, total, jnp.transpose(wt_ref[...])


def _merge_body(a_ref, b_ref, o_ref, w, hg, rows):
    for h in range(hg):
        cols = slice(h * HEAD_DIM, (h + 1) * HEAD_DIM)
        o = a_ref[0:rows, cols].astype(jnp.float32) * w[:, h : h + 1]
        o = o + b_ref[0:rows, cols].astype(jnp.float32) * w[:, 8 + h : 9 + h]
        o_ref[0:rows, cols] = o.astype(o_ref.dtype)


def _merge_kernel(valid_ref, a_ref, b_ref, o_ref, wt_ref, st_ref):
    rows = wt_ref.shape[1]
    hg = o_ref.shape[1] // HEAD_DIM
    top, total, w = _merge_weights(valid_ref, a_ref, b_ref, wt_ref)
    _merge_body(a_ref, b_ref, o_ref, w, hg, rows)
    wt_ref[0:hg, :] = top
    wt_ref[hg : 2 * hg, :] = total
    _store_stats(o_ref, st_ref, wt_ref[...], hg, rows)


def _final_kernel(valid_ref, a_ref, b_ref, *rest):
    o_ref, wt_ref = rest[-2], rest[-1]
    rows = wt_ref.shape[1]
    _, _, w = _merge_weights(valid_ref, a_ref, b_ref, wt_ref)
    _merge_body(a_ref, b_ref, o_ref, w, o_ref.shape[1] // HEAD_DIM, rows)


def merge(valid, a, b, base, final=False, buf=None, out_width=None):
    ext, width = b.shape
    rows = ext - EXTRA
    groups = width // HEAD_DIM // HG
    lanes = HG * HEAD_DIM
    a_base = 0 if out_width is not None else base
    a_spec = pl.BlockSpec((ext, lanes), lambda g, v: (0, g + a_base))
    b_spec = pl.BlockSpec((ext, lanes), lambda g, v: (0, g))
    in_specs = [a_spec, b_spec]
    operands = [valid, a, b]
    aliases = {}
    if final:
        kernel = _final_kernel
        out_shape = jax.ShapeDtypeStruct((rows, out_width or a.shape[1]), jnp.bfloat16)
        out_spec = pl.BlockSpec((rows, lanes), lambda g, v: (0, g + base))
        if buf is not None:
            in_specs.append(pl.BlockSpec(memory_space=pl.ANY))
            operands.append(buf)
            aliases = {3: 0}
    else:
        kernel = _merge_kernel
        out_shape = jax.ShapeDtypeStruct((ext, width), jnp.bfloat16)
        out_spec = b_spec
    return pl.pallas_call(
        kernel,
        out_shape=out_shape,
        grid_spec=pltpu.PrefetchScalarGridSpec(
            num_scalar_prefetch=1,
            grid=(groups,),
            in_specs=in_specs,
            out_specs=out_spec,
            scratch_shapes=[pltpu.VMEM((128, rows), jnp.float32)]
            + ([] if final else [pltpu.VMEM((EXTRA, lanes), jnp.float32)]),
        ),
        input_output_aliases=aliases,
        cost_estimate=pl.CostEstimate(
            flops=4 * rows * width, transcendentals=0, bytes_accessed=3 * rows * width * 2
        ),
    )(*operands)


def shift_tm(x, by):
    size = lax.axis_size("tm")
    pairs = [(i, i + by) for i in range(size) if 0 <= i + by < size]
    return lax.ppermute(x, "tm", pairs)


def on_device(query_states, key_states, value_states, history, neighbours):
    _, rows, width = query_states.shape
    seg = lax.axis_index("tm")
    tile = lax.axis_index("space")
    tiles = lax.axis_size("space")
    q = query_states[0]
    k = key_states[0]
    v = value_states[0]
    tile_l = tile > 0
    tile_r = tile < tiles - 1

    def flags_for(m, d):
        m = m.astype(jnp.int32)
        return jnp.stack(
            [
                ((m[1] == 1) & tile_l).astype(jnp.int32),
                (m[0] >= d).astype(jnp.int32),
                ((m[2] == 1) & tile_r).astype(jnp.int32),
            ]
        )

    meta = jnp.concatenate([history.reshape(1), neighbours.reshape(2)]).astype(jnp.bfloat16)
    chunk_w = width // CHUNKS
    groups_c = chunk_w // HEAD_DIM // HG
    meta_rows = jnp.zeros((EXTRA, chunk_w), jnp.bfloat16).at[0, 0:3].set(meta)
    sends = [jnp.concatenate([q[:, :chunk_w], meta_rows], axis=0)]
    sends += [q[:, c * chunk_w : (c + 1) * chunk_w] for c in range(1, CHUNKS)]
    q1s = [shift_tm(x, -1) for x in sends]

    sides = []
    for c in range(CHUNKS):
        kv = jnp.stack([k[:, c * chunk_w : (c + 1) * chunk_w], v[:, c * chunk_w : (c + 1) * chunk_w]])
        kv_l = lax.ppermute(kv, "space", [(i, i + 1) for i in range(tiles - 1)])
        kv_r = lax.ppermute(kv, "space", [(i + 1, i) for i in range(tiles - 1)])
        sides.append((kv_l, kv_r))

    f1 = flags_for(q1s[0][rows, 0:3], 1)
    p1s, q2s = [], []
    for c in range(CHUNKS):
        p1s.append(attend(f1, q1s[c], k, v, *sides[c], chunk_w, c * groups_c, 0, 0))
        relay = q1s[c]
        if c > 0:
            relay, p1s[0], p1s[c] = lax.optimization_barrier((relay, p1s[0], p1s[c]))
        q2s.append(shift_tm(relay, -1))

    valid = (seg >= 1).astype(jnp.int32).reshape(1)
    f0 = flags_for(meta, 0)
    f2 = flags_for(q2s[0][rows, 0:3], 2)
    p2s = [attend(f2, q2s[c], k, v, *sides[c], chunk_w, c * groups_c, 0, 0) for c in range(CHUNKS)]
    p2_ins = [shift_tm(p2, 1) for p2 in p2s]
    result = None
    p_self = None
    for c in range(CHUNKS):
        base = c * groups_c
        p2_in = p2_ins[c]
        if p_self is not None:
            p2_in, p_self = lax.optimization_barrier((p2_in, p_self))
            result = merge(valid, p_self, pcs_in, base - groups_c, final=True, buf=result, out_width=width)
        pc = merge(valid, p1s[c], p2_in, 0)
        pcs_in = shift_tm(pc, 1)
        q_self, _ = lax.optimization_barrier((q, pc))
        p_self = attend(f0, q_self, k, v, *sides[c], chunk_w, base, base, 0)
    result = merge(valid, p_self, pcs_in, (CHUNKS - 1) * groups_c, final=True, buf=result, out_width=width)
    return result.reshape(1, rows, width)


def solution(mesh):
    placed = (
        P("tm", "space", None),
        P("tm", "space", None),
        P("tm", "space", None),
        P("tm"),
        P("tm", "space", None),
    )
    return jax.shard_map(
        on_device, mesh=mesh, in_specs=placed, out_specs=P("tm", "space", None), check_vma=False
    )
```

```python
import jax
import jax.numpy as jnp
from jax import lax
from jax.experimental import pallas as pl
from jax.experimental.pallas import tpu as pltpu
from jax.sharding import PartitionSpec as P

HEAD_DIM = 128
HG = 5
CHUNKS = 2
NEG = -1e30
EXTRA = 16


def _store_stats(o_ref, st_ref, t, hg, rows):
    top, den = t[0:hg], t[hg : 2 * hg]
    top_hi = top.astype(jnp.bfloat16).astype(jnp.float32)
    rest = top - top_hi
    top_mid = rest.astype(jnp.bfloat16).astype(jnp.float32)
    den_hi = den.astype(jnp.bfloat16).astype(jnp.float32)
    st_ref[...] = jnp.zeros_like(st_ref)
    st_ref[0:hg, 0:rows] = top_hi
    st_ref[0:hg, rows : 2 * rows] = top_mid
    st_ref[2 * hg : 3 * hg, 0:rows] = rest - top_mid
    st_ref[hg : 2 * hg, 0:rows] = den_hi
    st_ref[hg : 2 * hg, rows : 2 * rows] = den - den_hi
    o_ref[rows : rows + EXTRA, :] = st_ref[...].astype(o_ref.dtype)


def _load_stats(ref, hg, rows):
    block = ref[rows : rows + EXTRA, :].astype(jnp.float32)
    top = block[0:hg, 0:rows] + block[0:hg, rows : 2 * rows] + block[2 * hg : 3 * hg, 0:rows]
    den = block[hg : 2 * hg, 0:rows] + block[hg : 2 * hg, rows : 2 * rows]
    return top, den


def _attn_kernel(flags_ref, q_ref, kl_ref, kc_ref, kr_ref, vl_ref, vc_ref, vr_ref, o_ref, col_ref, st_ref):
    hg = q_ref.shape[1] // HEAD_DIM
    rows = q_ref.shape[0]
    lanes = o_ref.shape[1]
    inv_root = 1.0 / HEAD_DIM**0.5
    seg_ok = flags_ref[1] == 1

    @pl.when(seg_ok)
    def _():
        bias_l = jnp.where(flags_ref[0] == 1, 0.0, NEG).astype(jnp.float32)
        bias_r = jnp.where(flags_ref[2] == 1, 0.0, NEG).astype(jnp.float32)
        col_ref[...] = jnp.zeros_like(col_ref)
        for h in range(hg):
            cols = slice(h * HEAD_DIM, (h + 1) * HEAD_DIM)
            q = q_ref[:, cols]

            def scores(k_ref):
                return (
                    lax.dot_general(
                        q, k_ref[:, cols], (((1,), (1,)), ((), ())), preferred_element_type=jnp.float32
                    )
                    * inv_root
                )

            s_l = scores(kl_ref) + bias_l
            s_c = scores(kc_ref)
            s_r = scores(kr_ref) + bias_r
            top = jnp.maximum(
                jnp.maximum(s_l.max(axis=1, keepdims=True), s_c.max(axis=1, keepdims=True)),
                s_r.max(axis=1, keepdims=True),
            )
            shift = top
            p_l = jnp.exp(s_l - shift)
            p_c = jnp.exp(s_c - shift)
            p_r = jnp.exp(s_r - shift)
            denom = (
                p_l.sum(axis=1, keepdims=True) + p_c.sum(axis=1, keepdims=True) + p_r.sum(axis=1, keepdims=True)
            )
            acc = jnp.dot(p_l.astype(jnp.bfloat16), vl_ref[:, cols], preferred_element_type=jnp.float32)
            acc += jnp.dot(p_c.astype(jnp.bfloat16), vc_ref[:, cols], preferred_element_type=jnp.float32)
            acc += jnp.dot(p_r.astype(jnp.bfloat16), vr_ref[:, cols], preferred_element_type=jnp.float32)
            o_ref[0:rows, cols] = (acc / denom).astype(o_ref.dtype)
            col_ref[:, h : h + 1] = shift
            col_ref[:, hg + h : hg + h + 1] = denom
        _store_stats(o_ref, st_ref, jnp.transpose(col_ref[...]), hg, rows)

    @pl.when(jnp.logical_not(seg_ok))
    def _():
        row = lax.broadcasted_iota(jnp.int32, o_ref.shape, 0)
        lane = lax.broadcasted_iota(jnp.int32, o_ref.shape, 1)
        empty = (row >= rows) & (row < rows + hg) & (lane < rows)
        o_ref[...] = jnp.where(empty, NEG, 0.0).astype(o_ref.dtype)


def attend(flags, q, k, v, kv_l, kv_r, width, base, q_base):
    rows = k.shape[0]
    heads = width // HEAD_DIM
    groups = heads // HG
    lanes = HG * HEAD_DIM
    q_spec = pl.BlockSpec((rows, lanes), lambda g, f: (0, g + q_base))
    kv_spec = pl.BlockSpec((rows, lanes), lambda g, f: (0, g + base))
    side_k = pl.BlockSpec((None, rows, lanes), lambda g, f: (0, 0, g + base))
    side_v = pl.BlockSpec((None, rows, lanes), lambda g, f: (1, 0, g + base))
    return pl.pallas_call(
        _attn_kernel,
        out_shape=jax.ShapeDtypeStruct((rows + EXTRA, width), jnp.bfloat16),
        grid_spec=pltpu.PrefetchScalarGridSpec(
            num_scalar_prefetch=1,
            grid=(groups,),
            in_specs=[q_spec, side_k, kv_spec, side_k, side_v, kv_spec, side_v],
            out_specs=pl.BlockSpec((rows + EXTRA, lanes), lambda g, f: (0, g)),
            scratch_shapes=[pltpu.VMEM((rows, 128), jnp.float32), pltpu.VMEM((EXTRA, lanes), jnp.float32)],
        ),
        cost_estimate=pl.CostEstimate(
            flops=4 * rows * 3 * rows * HEAD_DIM * heads,
            transcendentals=rows * 3 * rows * heads,
            bytes_accessed=2 * rows * width * 2 + 6 * rows * width * 2,
        ),
    )(flags, q, kv_l, k, kv_r, kv_l, v, kv_r)


def _merge_weights(valid_ref, a_ref, b_ref, wt_ref):
    rows = wt_ref.shape[1]
    hg = a_ref.shape[1] // HEAD_DIM
    a_top, a_den = _load_stats(a_ref, hg, rows)
    ok = valid_ref[0] == 1
    b_top, b_den = _load_stats(b_ref, hg, rows)
    b_top = jnp.where(ok, b_top, NEG)
    b_den = jnp.where(ok, b_den, 0.0)
    top = jnp.maximum(a_top, b_top)
    a_w = jnp.exp(a_top - top) * a_den
    b_w = jnp.exp(b_top - top) * b_den
    total = a_w + b_w
    safe = jnp.where(total > 0.0, total, 1.0)
    wt_ref[0:hg, :] = a_w / safe
    wt_ref[8 : 8 + hg, :] = b_w / safe
    return top, total, jnp.transpose(wt_ref[...])


def _merge_body(a_ref, b_ref, o_ref, w, hg, rows):
    for h in range(hg):
        cols = slice(h * HEAD_DIM, (h + 1) * HEAD_DIM)
        o = a_ref[0:rows, cols].astype(jnp.float32) * w[:, h : h + 1]
        o = o + b_ref[0:rows, cols].astype(jnp.float32) * w[:, 8 + h : 9 + h]
        o_ref[0:rows, cols] = o.astype(o_ref.dtype)


def _merge_kernel(valid_ref, a_ref, b_ref, o_ref, wt_ref, st_ref):
    rows = wt_ref.shape[1]
    hg = o_ref.shape[1] // HEAD_DIM
    top, total, w = _merge_weights(valid_ref, a_ref, b_ref, wt_ref)
    _merge_body(a_ref, b_ref, o_ref, w, hg, rows)
    wt_ref[0:hg, :] = top
    wt_ref[hg : 2 * hg, :] = total
    _store_stats(o_ref, st_ref, wt_ref[...], hg, rows)


def _final_kernel(valid_ref, a_ref, b_ref, *rest):
    o_ref, wt_ref = rest[-2], rest[-1]
    rows = wt_ref.shape[1]
    _, _, w = _merge_weights(valid_ref, a_ref, b_ref, wt_ref)
    _merge_body(a_ref, b_ref, o_ref, w, o_ref.shape[1] // HEAD_DIM, rows)


def merge(valid, a, b, base, final=False, buf=None, out_width=None):
    ext, width = b.shape
    rows = ext - EXTRA
    groups = width // HEAD_DIM // HG
    lanes = HG * HEAD_DIM
    a_base = 0 if out_width is not None else base
    a_spec = pl.BlockSpec((ext, lanes), lambda g, v: (0, g + a_base))
    b_spec = pl.BlockSpec((ext, lanes), lambda g, v: (0, g))
    in_specs = [a_spec, b_spec]
    operands = [valid, a, b]
    aliases = {}
    if final:
        kernel = _final_kernel
        out_shape = jax.ShapeDtypeStruct((rows, out_width or a.shape[1]), jnp.bfloat16)
        out_spec = pl.BlockSpec((rows, lanes), lambda g, v: (0, g + base))
        if buf is not None:
            in_specs.append(pl.BlockSpec(memory_space=pl.ANY))
            operands.append(buf)
            aliases = {3: 0}
    else:
        kernel = _merge_kernel
        out_shape = jax.ShapeDtypeStruct((ext, width), jnp.bfloat16)
        out_spec = b_spec
    return pl.pallas_call(
        kernel,
        out_shape=out_shape,
        grid_spec=pltpu.PrefetchScalarGridSpec(
            num_scalar_prefetch=1,
            grid=(groups,),
            in_specs=in_specs,
            out_specs=out_spec,
            scratch_shapes=[pltpu.VMEM((128, rows), jnp.float32)]
            + ([] if final else [pltpu.VMEM((EXTRA, lanes), jnp.float32)]),
        ),
        input_output_aliases=aliases,
        cost_estimate=pl.CostEstimate(
            flops=4 * rows * width, transcendentals=0, bytes_accessed=3 * rows * width * 2
        ),
    )(*operands)


def _stack_kernel(k_ref, v_ref, o_ref):
    o_ref[0] = k_ref[...]
    o_ref[1] = v_ref[...]


def stack_kv(k, v):
    rows, width = k.shape
    lanes = width // 2
    spec = pl.BlockSpec((rows, lanes), lambda g: (0, g))
    return pl.pallas_call(
        _stack_kernel,
        out_shape=jax.ShapeDtypeStruct((2, rows, width), k.dtype),
        grid=(2,),
        in_specs=[spec, spec],
        out_specs=pl.BlockSpec((2, rows, lanes), lambda g: (0, 0, g)),
        cost_estimate=pl.CostEstimate(flops=0, transcendentals=0, bytes_accessed=4 * rows * width * 2),
    )(k, v)


def shift_tm(x, by):
    size = lax.axis_size("tm")
    pairs = [(i, i + by) for i in range(size) if 0 <= i + by < size]
    return lax.ppermute(x, "tm", pairs)


def on_device(query_states, key_states, value_states, history, neighbours):
    _, rows, width = query_states.shape
    seg = lax.axis_index("tm")
    tile = lax.axis_index("space")
    tiles = lax.axis_size("space")
    q = query_states[0]
    k = key_states[0]
    v = value_states[0]
    tile_l = tile > 0
    tile_r = tile < tiles - 1

    def flags_for(m, d):
        m = m.astype(jnp.int32)
        return jnp.stack(
            [
                ((m[1] == 1) & tile_l).astype(jnp.int32),
                (m[0] >= d).astype(jnp.int32),
                ((m[2] == 1) & tile_r).astype(jnp.int32),
            ]
        )

    meta = jnp.concatenate([history.reshape(1), neighbours.reshape(2)]).astype(jnp.bfloat16)
    chunk_w = width // CHUNKS
    groups_c = chunk_w // HEAD_DIM // HG
    meta_rows = jnp.zeros((EXTRA, chunk_w), jnp.bfloat16).at[0, 0:3].set(meta)
    sends = [jnp.concatenate([q[:, :chunk_w], meta_rows], axis=0)]
    sends += [q[:, c * chunk_w : (c + 1) * chunk_w] for c in range(1, CHUNKS)]
    q1s = [shift_tm(x, -1) for x in sends]

    kv = stack_kv(k, v)
    kv_l = lax.ppermute(kv, "space", [(i, i + 1) for i in range(tiles - 1)])
    kv_r = lax.ppermute(kv, "space", [(i + 1, i) for i in range(tiles - 1)])

    f1 = flags_for(q1s[0][rows, 0:3], 1)
    p1s, q2s = [], []
    for c in range(CHUNKS):
        p1s.append(attend(f1, q1s[c], k, v, kv_l, kv_r, chunk_w, c * groups_c, 0))
        relay = q1s[c]
        if c > 0:
            relay, p1s[0], p1s[c] = lax.optimization_barrier((relay, p1s[0], p1s[c]))
        q2s.append(shift_tm(relay, -1))

    valid = (seg >= 1).astype(jnp.int32).reshape(1)
    f0 = flags_for(meta, 0)
    f2 = flags_for(q2s[0][rows, 0:3], 2)
    p2s = [attend(f2, q2s[c], k, v, kv_l, kv_r, chunk_w, c * groups_c, 0) for c in range(CHUNKS)]
    p2_ins = [shift_tm(p2, 1) for p2 in p2s]
    result = None
    p_self = None
    for c in range(CHUNKS):
        base = c * groups_c
        p2_in = p2_ins[c]
        if p_self is not None:
            p2_in, p_self = lax.optimization_barrier((p2_in, p_self))
            result = merge(valid, p_self, pcs_in, base - groups_c, final=True, buf=result, out_width=width)
        pc = merge(valid, p1s[c], p2_in, 0)
        pcs_in = shift_tm(pc, 1)
        q_self, _ = lax.optimization_barrier((q, pc))
        p_self = attend(f0, q_self, k, v, kv_l, kv_r, chunk_w, base, base)
    result = merge(valid, p_self, pcs_in, (CHUNKS - 1) * groups_c, final=True, buf=result, out_width=width)
    return result.reshape(1, rows, width)


def solution(mesh):
    placed = (
        P("tm", "space", None),
        P("tm", "space", None),
        P("tm", "space", None),
        P("tm"),
        P("tm", "space", None),
    )
    return jax.shard_map(
        on_device, mesh=mesh, in_specs=placed, out_specs=P("tm", "space", None), check_vma=False
    )
```
